32 devices in a mesh: groups: 2 (over x), seq: 16 (over z, y, core).
Axes of the slice: x: 2, y: 2, z: 4, core: 2. Of those that a mesh axis runs over, the one named last changes fastest.
Arguments:
- hidden_in: bfloat16 [16384, 768], P(('groups', 'seq')), parts along dimension 0
- ln_gain: float32 [2, 768], replicated, may hold values from 0.5 to 1.5
- w_qkv: bfloat16 [2, 768, 2304], replicated
- w_out: bfloat16 [2, 768, 768], replicated, may hold values from -0.21875 to 0.21875
- final_gain: float32 [768], replicated, may hold values from 0.5 to 1.5
- w_heads: bfloat16 [768, 512], replicated
- actions: int32 [16384], P(('groups', 'seq')), parts along dimension 0, may hold values from 0 to 255
- propensity: int32 [16384], P(('groups', 'seq')), parts along dimension 0, may hold values from 1024 to 65535
- logged_reward: float32 [16384], P(('groups', 'seq')), parts along dimension 0, may hold values from -6 to 6
- switch_index: int32 [2], P('groups'), parts along dimension 0, may hold values from 2 to 9
Outputs:
- rewards: float32 [16384], P(('groups', 'seq')), parts along dimension 0
- dr_terms: float32 [16384], P(('groups', 'seq')), parts along dimension 0
The draws below stay inside these ranges and needn't reach their ends.
There are 2 independent parts, one for each index of `groups`. The reference program is written for one: setup_inputs(seed, part) draws one part's arguments, and reference() takes and returns one part's arrays. A program takes and returns all parts, laid end to end along the dimension named above; an argument that names none is the same for every part. Nothing has to cross between parts.
All inputs are finite; a program needn't handle non-finite values.
Results may differ from the reference program's by a relative error of at most 0.03.
Values may be sent and summed in bfloat16 or wider, within the bound.
No kernel may reach another device: no remote copies, remote signals or barrier semaphores. Data moves between devices by JAX's collectives and lax.ppermute only.
A program may use at most 128 MiB of HBM per device.

```python
import jax
import jax.numpy as jnp
from jax import lax

D = 768
HEADS = 12
HEAD = 64
HALF = 256
PROMPT = 256
ACTIONS = 256
LAYERS = 2
TOK_DEV = 512
SEQLEN = 8192


def draw_hidden_in(key, part):
    key_noise = jax.random.fold_in(key, 11)
    noise_part = jax.random.normal(key_noise, (SEQLEN, D), jnp.float32)
    result = noise_part
    return result.astype(jnp.bfloat16)


def draw_w_qkv(key, part):
    key_base = jax.random.fold_in(key, 21)
    base_draw = jax.random.normal(key_base, (LAYERS, D, 3 * D), jnp.float32) * D ** (-0.5)
    return base_draw.astype(jnp.bfloat16)


def draw_w_heads(key, part):
    key_policy = jax.random.fold_in(key, 31)
    key_reward = jax.random.fold_in(key, 32)
    policy_part = jax.random.normal(key_policy, (D, ACTIONS), jnp.float32) * (3.0 * D ** (-0.5))
    reward_part = jax.random.normal(key_reward, (D, ACTIONS), jnp.float32) * D ** (-0.5)
    return jnp.concatenate([policy_part, reward_part], axis=-1).astype(jnp.bfloat16)


def place_ends(array, stream_key, least, largest):
    extent = array.shape
    place = [jax.random.randint(jax.random.fold_in(stream_key, axis), (), 0, extent[axis]) for axis in range(len(extent))]
    array = array.at[tuple(place)].set(least)
    longest = extent.index(max(extent))
    place[longest] = (place[longest] + 1) % extent[longest]
    return array.at[tuple(place)].set(largest)


def block_scale(rng, dims, pieces, least, high):
    def one(axis_at, shards_of):
        steps = jax.random.uniform(jax.random.fold_in(jax.random.fold_in(rng, 6), axis_at), (shards_of,), jnp.float32, least / len(pieces), high / len(pieces))
        return jnp.repeat(jnp.exp(steps), dims[axis_at] // shards_of).reshape((-1,) + (1,) * (len(dims) - axis_at - 1))

    factor_of = one(*pieces[0])
    for cut in pieces[1:]:
        factor_of = factor_of * one(*cut)
    return factor_of


def scatter_about(key, shape, deviation, most, shards=(), kind=jnp.bfloat16):
    loudness = block_scale(key, shape, shards, -0.22, 0.18) if shards else 1.0
    values = jax.random.normal(key, shape, jnp.float32) * deviation * loudness
    return jnp.minimum(jnp.maximum(values, -most), most).astype(kind)


def setup_inputs(seed: int = 0, part: int = 0) -> dict:
    key_of = jax.random.split(jax.random.key(seed), 11)
    own_keys = jax.random.split(jax.random.fold_in(key_of[10], part), 11)
    return {
        "hidden_in": draw_hidden_in(jax.random.fold_in(jax.random.fold_in(key_of[10], part), 71), part),
        "ln_gain": jnp.clip(1.0 + 0.1 * jax.random.normal(key_of[1], (LAYERS, D), jnp.float32), 0.5, 1.5),
        "w_qkv": draw_w_qkv(jax.random.fold_in(key_of[10], 71), part),
        "w_out": scatter_about(key_of[3], (LAYERS, D, D), D ** -0.5, 0.21875),
        "final_gain": jnp.clip(1.0 + 0.1 * jax.random.normal(key_of[4], (D,), jnp.float32), 0.5, 1.5),
        "w_heads": draw_w_heads(jax.random.fold_in(key_of[10], 71), part),
        "actions": place_ends(jax.random.randint(own_keys[6], (SEQLEN,), 0, ACTIONS), jax.random.fold_in(own_keys[6], 1), 0, ACTIONS - 1).astype(jnp.int32),
        "propensity": place_ends(jax.random.randint(own_keys[7], (SEQLEN,), 1024, 65536), jax.random.fold_in(own_keys[7], 1), 1024, 65535).astype(jnp.int32),
        "logged_reward": scatter_about(own_keys[8], (SEQLEN,), 1.0, 6.0, ((0, 16),), jnp.float32),
        "switch_index": jax.random.randint(own_keys[9], (1,), 2, 10).astype(jnp.int32),
    }


def layer_norm(hidden_state, gain_row):
    values_f = hidden_state.astype(jnp.float32)
    row_mean = lax.optimization_barrier(jnp.mean(values_f, axis=-1, keepdims=True))
    centred = values_f - row_mean
    row_var = lax.optimization_barrier(jnp.mean(centred * centred, axis=-1, keepdims=True))
    return (centred * lax.rsqrt(row_var + 1e-05) * gain_row).astype(jnp.bfloat16)

def attend_block(query_block, key_block, value_block, prompt_keys, prompt_values, row_start, total_len):
    block_rows = query_block.shape[0]
    band_width = key_block.shape[0]
    query_f = query_block.astype(jnp.float32)
    band_scores = jnp.einsum('qhe,khe->hqk', query_f, key_block.astype(jnp.float32))
    prompt_scores = jnp.einsum('qhe,khe->hqk', query_f, prompt_keys.astype(jnp.float32))
    query_pos = row_start + jnp.arange(block_rows, dtype=jnp.int32)
    key_pos = row_start - HALF + jnp.arange(band_width, dtype=jnp.int32)
    prompt_pos = jnp.arange(PROMPT, dtype=jnp.int32)
    band_mask = (jnp.abs(key_pos[None, :] - query_pos[:, None]) <= HALF) & (key_pos[None, :] >= 0) & (key_pos[None, :] < total_len)
    prompt_mask = jnp.abs(prompt_pos[None, :] - query_pos[:, None]) > HALF
    scores = jnp.concatenate([jnp.where(prompt_mask[None], prompt_scores, -1e+30), jnp.where(band_mask[None], band_scores, -1e+30)], axis=-1)
    row_max = lax.optimization_barrier(jnp.max(scores, axis=-1, keepdims=True))
    exps = jnp.exp(scores - row_max)
    attn_probs = (exps / lax.optimization_barrier(jnp.sum(exps, axis=-1, keepdims=True))).astype(jnp.bfloat16)
    value_rows = jnp.concatenate([prompt_values, value_block], axis=0)
    attn_out = jnp.einsum('hqk,khe->qhe', attn_probs.astype(jnp.float32), value_rows.astype(jnp.float32))
    return attn_out.reshape(block_rows, HEADS * HEAD).astype(jnp.bfloat16)

def reference(hidden_in, ln_gain, w_qkv, w_out, final_gain, w_heads, actions, propensity, logged_reward, switch_index):
    total_len = hidden_in.shape[0]
    feat_width = hidden_in.shape[1]
    block_rows = min(256, TOK_DEV)
    block_count = total_len // block_rows
    hidden_state = hidden_in
    for layer_idx in range(LAYERS):
        normed = layer_norm(hidden_state, ln_gain[layer_idx])
        projected = jnp.dot(normed, w_qkv[layer_idx], preferred_element_type=jnp.float32)
        queries = (projected[:, :feat_width] * 0.125).astype(jnp.bfloat16).reshape(total_len, HEADS, HEAD)
        keys_all = projected[:, feat_width:2 * feat_width].astype(jnp.bfloat16).reshape(total_len, HEADS, HEAD)
        values_all = projected[:, 2 * feat_width:].astype(jnp.bfloat16).reshape(total_len, HEADS, HEAD)
        prompt_keys = keys_all[:PROMPT]
        prompt_values = values_all[:PROMPT]
        pad_keys = jnp.pad(keys_all, ((HALF, HALF), (0, 0), (0, 0)))
        pad_values = jnp.pad(values_all, ((HALF, HALF), (0, 0), (0, 0)))

        def one_block(block_idx):
            row_start = block_idx * block_rows
            return attend_block(lax.dynamic_slice_in_dim(queries, row_start, block_rows), lax.dynamic_slice_in_dim(pad_keys, row_start, block_rows + 2 * HALF), lax.dynamic_slice_in_dim(pad_values, row_start, block_rows + 2 * HALF), prompt_keys, prompt_values, row_start, total_len)
        attended = lax.map(one_block, jnp.arange(block_count, dtype=jnp.int32)).reshape(total_len, feat_width)
        projection = jnp.dot(attended, w_out[layer_idx], preferred_element_type=jnp.float32)
        hidden_state = (hidden_state.astype(jnp.float32) + projection).astype(jnp.bfloat16)
    final = layer_norm(hidden_state, final_gain)
    head_out = jnp.dot(final, w_heads, preferred_element_type=jnp.float32)
    logits = head_out[:, :ACTIONS]
    reward_table = head_out[:, ACTIONS:]
    logit_max = lax.optimization_barrier(jnp.max(logits, axis=-1, keepdims=True))
    exps = jnp.exp(logits - logit_max)
    policy = exps / lax.optimization_barrier(jnp.sum(exps, axis=-1, keepdims=True))
    chosen = actions[:, None] == jnp.arange(ACTIONS, dtype=jnp.int32)[None, :]
    rewards = lax.optimization_barrier(jnp.sum(jnp.where(chosen, reward_table, 0.0), axis=-1))
    chosen_prob = lax.optimization_barrier(jnp.sum(jnp.where(chosen, policy, 0.0), axis=-1))
    direct = lax.optimization_barrier(jnp.sum(policy * reward_table, axis=-1))
    logged_prob = propensity.astype(jnp.float32) / 65536.0
    cutoff = 0.5 * switch_index[0].astype(jnp.float32)
    dr_terms = direct + jnp.minimum(chosen_prob / logged_prob, cutoff) * (logged_reward - rewards)
    return (rewards, dr_terms)
```

```python
import jax
import jax.numpy as jnp
from jax import lax
from jax.sharding import PartitionSpec as P

HEADS = 12
HEAD = 64
HALF = 256
PROMPT = 256
ACTIONS = 256
LAYERS = 2


def with_halo(array, sides, width):
    for axis, dim in sides:
        count, length = (lax.axis_size(axis), array.shape[dim])
        up = [(i, (i + 1) % count) for i in range(count - 1)]
        down = [(j, i) for i, j in up]
        last = lax.slice_in_dim(array, length - width, length, axis=dim)
        leading = lax.slice_in_dim(array, 0, width, axis=dim)
        before = lax.ppermute(last, axis, up)
        after = lax.ppermute(leading, axis, down)
        array = jnp.concatenate([before, array, after], axis=dim)
    return array


def tree_rounds(count):
    def near(i):
        out = [i ^ 1]
        if count % 4 == 0:
            out += [i + 4, i ^ 2, i - 4]
        else:
            out += [i + 2, i - 2]
        return [j for j in out if 0 <= j < count]

    holders = {0}
    rounds = []
    while len(holders) < count:
        taken = set()
        pairs = []
        for i in sorted(holders):
            for j in near(i):
                if j not in holders and j not in taken:
                    taken.add(j)
                    pairs.append((i, j))
        if not pairs:
            for j in range(count):
                if j not in holders:
                    pairs.append((min(holders), j))
                    taken.add(j)
                    break
        ops = []
        for pair in pairs:
            for op in ops:
                if all(pair[0] != s for s, _ in op):
                    op.append(pair)
                    break
            else:
                ops.append([pair])
        rounds.append(ops)
        holders |= taken
    return rounds


def spread(block, axis):
    place = lax.axis_index(axis)
    block = jnp.where(place == 0, block, jnp.zeros_like(block))
    for ops in tree_rounds(lax.axis_size(axis)):
        received = block
        for op in ops:
            got = lax.ppermute(block, axis, op)
            targets = jnp.array([t for _, t in op], dtype=jnp.int32)
            received = jnp.where(jnp.any(place == targets), got, received)
        block = received
    return block


def layer_norm(hidden_state, gain_row):
    values_f = hidden_state.astype(jnp.float32)
    row_mean = jnp.mean(values_f, axis=-1, keepdims=True)
    centred = values_f - row_mean
    row_var = jnp.mean(centred * centred, axis=-1, keepdims=True)
    return (centred * lax.rsqrt(row_var + 1e-05) * gain_row).astype(jnp.bfloat16)


def attend_block(
    query_block, key_block, value_block, prompt_keys, prompt_values, row_start, total_len
):
    block_rows = query_block.shape[0]
    band_width = key_block.shape[0]
    band_scores = jnp.einsum(
        "qhe,khe->hqk", query_block, key_block, preferred_element_type=jnp.float32
    )
    prompt_scores = jnp.einsum(
        "qhe,khe->hqk", query_block, prompt_keys, preferred_element_type=jnp.float32
    )
    query_pos = row_start + jnp.arange(block_rows, dtype=jnp.int32)
    key_pos = row_start - HALF + jnp.arange(band_width, dtype=jnp.int32)
    prompt_pos = jnp.arange(PROMPT, dtype=jnp.int32)
    band_mask = (
        (jnp.abs(key_pos[None, :] - query_pos[:, None]) <= HALF)
        & (key_pos[None, :] >= 0)
        & (key_pos[None, :] < total_len)
    )
    prompt_mask = jnp.abs(prompt_pos[None, :] - query_pos[:, None]) > HALF
    scores = jnp.concatenate(
        [
            jnp.where(prompt_mask[None], prompt_scores, -1e30),
            jnp.where(band_mask[None], band_scores, -1e30),
        ],
        axis=-1,
    )
    row_max = jnp.max(scores, axis=-1, keepdims=True)
    exps = jnp.exp(scores - row_max)
    attn_probs = (exps / jnp.sum(exps, axis=-1, keepdims=True)).astype(jnp.bfloat16)
    value_rows = jnp.concatenate([prompt_values, value_block], axis=0)
    attn_out = jnp.einsum(
        "hqk,khe->qhe", attn_probs, value_rows, preferred_element_type=jnp.float32
    )
    return attn_out.reshape(block_rows, HEADS * HEAD).astype(jnp.bfloat16)


def per_device(
    hidden_in,
    ln_gain,
    w_qkv,
    w_out,
    final_gain,
    w_heads,
    actions,
    propensity,
    logged_reward,
    switch_index,
):
    tok_rows = hidden_in.shape[0]
    feat_width = hidden_in.shape[1]
    seq_devices = lax.axis_size("seq")
    seq_place = lax.axis_index("seq")
    total_len = tok_rows * seq_devices
    first_pos = seq_place * tok_rows
    block_rows = min(256, tok_rows)
    block_count = tok_rows // block_rows
    hidden_state = hidden_in
    for layer_idx in range(LAYERS):
        normed = layer_norm(hidden_state, ln_gain[layer_idx])
        weights = w_qkv[layer_idx]
        projected = jnp.dot(normed, weights, preferred_element_type=jnp.float32)
        queries = (projected[:, :feat_width] * 0.125).astype(jnp.bfloat16)
        key_value = projected[:, feat_width:].astype(jnp.bfloat16)
        extended = with_halo(key_value, (("seq", 0),), HALF)
        prompt_rows = spread(hidden_state[:PROMPT], "seq")
        prompt_kv = jnp.dot(
            layer_norm(prompt_rows, ln_gain[layer_idx]),
            weights[:, feat_width:],
            preferred_element_type=jnp.float32,
        ).astype(jnp.bfloat16)
        query_heads = queries.reshape(tok_rows, HEADS, HEAD)
        band_keys = extended[:, :feat_width].reshape(-1, HEADS, HEAD)
        band_values = extended[:, feat_width:].reshape(-1, HEADS, HEAD)
        prompt_keys = prompt_kv[:, :feat_width].reshape(PROMPT, HEADS, HEAD)
        prompt_values = prompt_kv[:, feat_width:].reshape(PROMPT, HEADS, HEAD)

        def one_block(block_idx):
            local_start = block_idx * block_rows
            return attend_block(
                lax.dynamic_slice_in_dim(query_heads, local_start, block_rows),
                lax.dynamic_slice_in_dim(band_keys, local_start, block_rows + 2 * HALF),
                lax.dynamic_slice_in_dim(band_values, local_start, block_rows + 2 * HALF),
                prompt_keys,
                prompt_values,
                first_pos + local_start,
                total_len,
            )

        attended = lax.map(one_block, jnp.arange(block_count, dtype=jnp.int32)).reshape(
            tok_rows, feat_width
        )
        projection = jnp.dot(attended, w_out[layer_idx], preferred_element_type=jnp.float32)
        hidden_state = (hidden_state.astype(jnp.float32) + projection).astype(jnp.bfloat16)
    final = layer_norm(hidden_state, final_gain)
    head_out = jnp.dot(final, w_heads, preferred_element_type=jnp.float32)
    logits = head_out[:, :ACTIONS]
    reward_table = head_out[:, ACTIONS:]
    logit_max = jnp.max(logits, axis=-1, keepdims=True)
    exps = jnp.exp(logits - logit_max)
    policy = exps / jnp.sum(exps, axis=-1, keepdims=True)
    chosen = actions[:, None] == jnp.arange(ACTIONS, dtype=jnp.int32)[None, :]
    rewards = jnp.sum(jnp.where(chosen, reward_table, 0.0), axis=-1)
    chosen_prob = jnp.sum(jnp.where(chosen, policy, 0.0), axis=-1)
    direct = jnp.sum(policy * reward_table, axis=-1)
    logged_prob = propensity.astype(jnp.float32) / 65536.0
    cutoff = 0.5 * switch_index[0].astype(jnp.float32)
    dr_terms = direct + jnp.minimum(chosen_prob / logged_prob, cutoff) * (logged_reward - rewards)
    return (rewards, dr_terms)


def solution(mesh):
    placed = (
        P(("groups", "seq"), None),
        P(),
        P(),
        P(),
        P(),
        P(),
        P(("groups", "seq")),
        P(("groups", "seq")),
        P(("groups", "seq")),
        P("groups"),
    )
    return jax.shard_map(
        per_device,
        mesh=mesh,
        in_specs=placed,
        out_specs=(P(("groups", "seq")), P(("groups", "seq"))),
        check_vma=False,
    )
```

```python
import jax
import jax.numpy as jnp
from jax import lax
from jax.experimental import pallas as pl
from jax.experimental.pallas import tpu as pltpu
from jax.sharding import PartitionSpec as P

HEADS = 12
HEAD = 64
HALF = 256
PROMPT = 256
ACTIONS = 256
LAYERS = 2


def with_halo(array, sides, width):
    for axis, dim in sides:
        count, length = (lax.axis_size(axis), array.shape[dim])
        up = [(i, (i + 1) % count) for i in range(count - 1)]
        down = [(j, i) for i, j in up]
        last = lax.slice_in_dim(array, length - width, length, axis=dim)
        leading = lax.slice_in_dim(array, 0, width, axis=dim)
        before = lax.ppermute(last, axis, up)
        after = lax.ppermute(leading, axis, down)
        array = jnp.concatenate([before, array, after], axis=dim)
    return array


def tree_rounds(count):
    def near(i):
        out = [i ^ 1]
        if count % 4 == 0:
            out += [i + 4, i ^ 2, i - 4]
        else:
            out += [i + 2, i - 2]
        return [j for j in out if 0 <= j < count]

    holders = {0}
    rounds = []
    while len(holders) < count:
        taken = set()
        pairs = []
        for i in sorted(holders):
            for j in near(i):
                if j not in holders and j not in taken:
                    taken.add(j)
                    pairs.append((i, j))
        if not pairs:
            for j in range(count):
                if j not in holders:
                    pairs.append((min(holders), j))
                    taken.add(j)
                    break
        ops = []
        for pair in pairs:
            for op in ops:
                if all(pair[0] != s for s, _ in op):
                    op.append(pair)
                    break
            else:
                ops.append([pair])
        rounds.append(ops)
        holders |= taken
    return rounds


def spread(block, axis):
    place = lax.axis_index(axis)
    block = jnp.where(place == 0, block, jnp.zeros_like(block))
    for ops in tree_rounds(lax.axis_size(axis)):
        received = block
        for op in ops:
            got = lax.ppermute(block, axis, op)
            targets = jnp.array([t for _, t in op], dtype=jnp.int32)
            received = jnp.where(jnp.any(place == targets), got, received)
        block = received
    return block


def layer_norm(hidden_state, gain_row):
    values_f = hidden_state.astype(jnp.float32)
    row_mean = jnp.mean(values_f, axis=-1, keepdims=True)
    centred = values_f - row_mean
    row_var = jnp.mean(centred * centred, axis=-1, keepdims=True)
    return (centred * lax.rsqrt(row_var + 1e-05) * gain_row).astype(jnp.bfloat16)


QUERY_TILE = 128


def attention_kernel(pos_ref, q_ref, band_ref, prompt_ref, out_ref):
    tile = q_ref.shape[0]
    width = tile + 2 * HALF
    feat = q_ref.shape[1]
    block = pl.program_id(0)
    first = pos_ref[0]
    total = pos_ref[1]
    query_pos = first + block * tile + lax.broadcasted_iota(jnp.int32, (tile, 1), 0)
    key_pos = first + block * tile - HALF + lax.broadcasted_iota(jnp.int32, (1, width), 1)
    gap = key_pos - query_pos
    band_ok = (gap >= -HALF) & (gap <= HALF) & (key_pos >= 0) & (key_pos < total)
    prompt_pos = lax.broadcasted_iota(jnp.int32, (1, PROMPT), 1)
    prompt_ok = jnp.abs(prompt_pos - query_pos) > HALF
    start = pl.multiple_of(block * tile, tile)
    contract = (((1,), (1,)), ((), ()))
    for head in range(HEADS):
        cols = slice(head * HEAD, (head + 1) * HEAD)
        vcols = slice(feat + head * HEAD, feat + (head + 1) * HEAD)
        query = q_ref[:, cols]
        band_scores = lax.dot_general(
            query, band_ref[pl.ds(start, width), cols], contract,
            preferred_element_type=jnp.float32,
        )
        prompt_scores = lax.dot_general(
            query, prompt_ref[:, cols], contract, preferred_element_type=jnp.float32
        )
        band_scores = jnp.where(band_ok, band_scores, -1e30)
        prompt_scores = jnp.where(prompt_ok, prompt_scores, -1e30)
        row_max = jnp.maximum(
            jnp.max(band_scores, axis=1, keepdims=True),
            jnp.max(prompt_scores, axis=1, keepdims=True),
        )
        band_exp = jnp.exp(band_scores - row_max)
        prompt_exp = jnp.exp(prompt_scores - row_max)
        denom = jnp.sum(band_exp, axis=1, keepdims=True) + jnp.sum(
            prompt_exp, axis=1, keepdims=True
        )
        band_probs = (band_exp / denom).astype(jnp.bfloat16)
        prompt_probs = (prompt_exp / denom).astype(jnp.bfloat16)
        attn = jnp.dot(
            band_probs, band_ref[pl.ds(start, width), vcols],
            preferred_element_type=jnp.float32,
        ) + jnp.dot(prompt_probs, prompt_ref[:, vcols], preferred_element_type=jnp.float32)
        out_ref[:, cols] = attn.astype(out_ref.dtype)


def attention(queries, band_kv, prompt_kv, first_pos, total_len):
    rows, feat = queries.shape
    tile = min(QUERY_TILE, rows)
    pos = jnp.stack([first_pos, total_len]).astype(jnp.int32)
    width = tile + 2 * HALF
    flops = 4 * rows * (width + PROMPT) * feat
    return pl.pallas_call(
        attention_kernel,
        out_shape=jax.ShapeDtypeStruct((rows, feat), jnp.bfloat16),
        grid_spec=pltpu.PrefetchScalarGridSpec(
            num_scalar_prefetch=1,
            grid=(rows // tile,),
            in_specs=[
                pl.BlockSpec((tile, feat), lambda b, p: (b, 0)),
                pl.BlockSpec(band_kv.shape, lambda b, p: (0, 0)),
                pl.BlockSpec(prompt_kv.shape, lambda b, p: (0, 0)),
            ],
            out_specs=pl.BlockSpec((tile, feat), lambda b, p: (b, 0)),
        ),
        cost_estimate=pl.CostEstimate(
            flops=flops,
            transcendentals=rows * (width + PROMPT) * HEADS,
            bytes_accessed=2 * (2 * queries.size + band_kv.size + prompt_kv.size),
        ),
    )(pos, queries, band_kv, prompt_kv)


def per_device(
    hidden_in,
    ln_gain,
    w_qkv,
    w_out,
    final_gain,
    w_heads,
    actions,
    propensity,
    logged_reward,
    switch_index,
):
    tok_rows = hidden_in.shape[0]
    feat_width = hidden_in.shape[1]
    seq_devices = lax.axis_size("seq")
    seq_place = lax.axis_index("seq")
    total_len = tok_rows * seq_devices
    first_pos = seq_place * tok_rows
    hidden_state = hidden_in
    for layer_idx in range(LAYERS):
        normed = layer_norm(hidden_state, ln_gain[layer_idx])
        weights = w_qkv[layer_idx]
        projected = jnp.dot(normed, weights, preferred_element_type=jnp.float32)
        queries = (projected[:, :feat_width] * 0.125).astype(jnp.bfloat16)
        key_value = projected[:, feat_width:].astype(jnp.bfloat16)
        extended = with_halo(key_value, (("seq", 0),), HALF)
        prompt_rows = spread(hidden_state[:PROMPT], "seq")
        prompt_kv = jnp.dot(
            layer_norm(prompt_rows, ln_gain[layer_idx]),
            weights[:, feat_width:],
            preferred_element_type=jnp.float32,
        ).astype(jnp.bfloat16)
        attended = attention(queries, extended, prompt_kv, first_pos, total_len)
        projection = jnp.dot(attended, w_out[layer_idx], preferred_element_type=jnp.float32)
        hidden_state = (hidden_state.astype(jnp.float32) + projection).astype(jnp.bfloat16)
    final = layer_norm(hidden_state, final_gain)
    head_out = jnp.dot(final, w_heads, preferred_element_type=jnp.float32)
    logits = head_out[:, :ACTIONS]
    reward_table = head_out[:, ACTIONS:]
    logit_max = jnp.max(logits, axis=-1, keepdims=True)
    exps = jnp.exp(logits - logit_max)
    policy = exps / jnp.sum(exps, axis=-1, keepdims=True)
    chosen = actions[:, None] == jnp.arange(ACTIONS, dtype=jnp.int32)[None, :]
    rewards = jnp.sum(jnp.where(chosen, reward_table, 0.0), axis=-1)
    chosen_prob = jnp.sum(jnp.where(chosen, policy, 0.0), axis=-1)
    direct = jnp.sum(policy * reward_table, axis=-1)
    logged_prob = propensity.astype(jnp.float32) / 65536.0
    cutoff = 0.5 * switch_index[0].astype(jnp.float32)
    dr_terms = direct + jnp.minimum(chosen_prob / logged_prob, cutoff) * (logged_reward - rewards)
    return (rewards, dr_terms)


def solution(mesh):
    placed = (
        P(("groups", "seq"), None),
        P(),
        P(),
        P(),
        P(),
        P(),
        P(("groups", "seq")),
        P(("groups", "seq")),
        P(("groups", "seq")),
        P("groups"),
    )
    return jax.shard_map(
        per_device,
        mesh=mesh,
        in_specs=placed,
        out_specs=(P(("groups", "seq")), P(("groups", "seq"))),
        check_vma=False,
    )
```

```python
import jax
import jax.numpy as jnp
from jax import lax
from jax.experimental import pallas as pl
from jax.experimental.pallas import tpu as pltpu
from jax.sharding import PartitionSpec as P

HEADS = 12
HEAD = 64
HALF = 256
PROMPT = 256
ACTIONS = 256
LAYERS = 2


def with_halo(array, sides, width):
    for axis, dim in sides:
        count, length = (lax.axis_size(axis), array.shape[dim])
        up = [(i, (i + 1) % count) for i in range(count - 1)]
        down = [(j, i) for i, j in up]
        last = lax.slice_in_dim(array, length - width, length, axis=dim)
        leading = lax.slice_in_dim(array, 0, width, axis=dim)
        before = lax.ppermute(last, axis, up)
        after = lax.ppermute(leading, axis, down)
        array = jnp.concatenate([before, array, after], axis=dim)
    return array


def tree_rounds(count):
    def near(i):
        out = [i ^ 1]
        if count % 4 == 0:
            out += [i + 4, i ^ 2, i - 4]
        else:
            out += [i + 2, i - 2]
        return [j for j in out if 0 <= j < count]

    holders = {0}
    rounds = []
    while len(holders) < count:
        taken = set()
        pairs = []
        for i in sorted(holders):
            for j in near(i):
                if j not in holders and j not in taken:
                    taken.add(j)
                    pairs.append((i, j))
        if not pairs:
            for j in range(count):
                if j not in holders:
                    pairs.append((min(holders), j))
                    taken.add(j)
                    break
        ops = []
        for pair in pairs:
            for op in ops:
                if all(pair[0] != s for s, _ in op):
                    op.append(pair)
                    break
            else:
                ops.append([pair])
        rounds.append(ops)
        holders |= taken
    return rounds


def spread(block, axis):
    place = lax.axis_index(axis)
    block = jnp.where(place == 0, block, jnp.zeros_like(block))
    for ops in tree_rounds(lax.axis_size(axis)):
        received = block
        for op in ops:
            got = lax.ppermute(block, axis, op)
            targets = jnp.array([t for _, t in op], dtype=jnp.int32)
            received = jnp.where(jnp.any(place == targets), got, received)
        block = received
    return block


def layer_norm(hidden_state, gain_row):
    values_f = hidden_state.astype(jnp.float32)
    row_mean = jnp.mean(values_f, axis=-1, keepdims=True)
    centred = values_f - row_mean
    row_var = jnp.mean(centred * centred, axis=-1, keepdims=True)
    return (centred * lax.rsqrt(row_var + 1e-05) * gain_row).astype(jnp.bfloat16)


QUERY_TILE = 128


def attention_kernel(pos_ref, q_ref, band_ref, prompt_ref, out_ref):
    tile = q_ref.shape[0]
    width = tile + 2 * HALF
    feat = q_ref.shape[1]
    block = pl.program_id(0)
    first = pos_ref[0]
    total = pos_ref[1]
    query_pos = first + block * tile + lax.broadcasted_iota(jnp.int32, (tile, 1), 0)
    key_pos = first + block * tile - HALF + lax.broadcasted_iota(jnp.int32, (1, width), 1)
    gap = key_pos - query_pos
    band_ok = (gap >= -HALF) & (gap <= HALF) & (key_pos >= 0) & (key_pos < total)
    prompt_pos = lax.broadcasted_iota(jnp.int32, (1, PROMPT), 1)
    prompt_ok = jnp.abs(prompt_pos - query_pos) > HALF
    start = pl.multiple_of(block * tile, tile)
    contract = (((1,), (1,)), ((), ()))
    pair = 2 * HEAD
    low_lanes = lax.broadcasted_iota(jnp.int32, (1, pair), 1) < HEAD
    for head_pair in range(HEADS // 2):
        cols = slice(head_pair * pair, (head_pair + 1) * pair)
        vcols = slice(feat + head_pair * pair, feat + (head_pair + 1) * pair)
        query_two = q_ref[:, cols]
        band_keys = band_ref[pl.ds(start, width), cols]
        band_values = band_ref[pl.ds(start, width), vcols]
        prompt_keys = prompt_ref[:, cols]
        prompt_values = prompt_ref[:, vcols]
        halves = []
        for low in (True, False):
            keep = low_lanes if low else jnp.logical_not(low_lanes)
            query = jnp.where(keep, query_two, jnp.zeros_like(query_two))
            band_scores = lax.dot_general(
                query, band_keys, contract, preferred_element_type=jnp.float32
            )
            prompt_scores = lax.dot_general(
                query, prompt_keys, contract, preferred_element_type=jnp.float32
            )
            band_scores = jnp.where(band_ok, band_scores, -1e30)
            prompt_scores = jnp.where(prompt_ok, prompt_scores, -1e30)
            row_max = jnp.maximum(
                jnp.max(band_scores, axis=1, keepdims=True),
                jnp.max(prompt_scores, axis=1, keepdims=True),
            )
            band_exp = jnp.exp(band_scores - row_max)
            prompt_exp = jnp.exp(prompt_scores - row_max)
            denom = jnp.sum(band_exp, axis=1, keepdims=True) + jnp.sum(
                prompt_exp, axis=1, keepdims=True
            )
            scale = 1.0 / denom
            band_probs = (band_exp * scale).astype(jnp.bfloat16)
            prompt_probs = (prompt_exp * scale).astype(jnp.bfloat16)
            halves.append(
                jnp.dot(band_probs, band_values, preferred_element_type=jnp.float32)
                + jnp.dot(prompt_probs, prompt_values, preferred_element_type=jnp.float32)
            )
        attn = jnp.where(low_lanes, halves[0], halves[1])
        out_ref[:, cols] = attn.astype(out_ref.dtype)


def attention(queries, band_kv, prompt_kv, first_pos, total_len):
    rows, feat = queries.shape
    tile = min(QUERY_TILE, rows)
    pos = jnp.stack([first_pos, total_len]).astype(jnp.int32)
    width = tile + 2 * HALF
    flops = 4 * rows * (width + PROMPT) * feat
    return pl.pallas_call(
        attention_kernel,
        out_shape=jax.ShapeDtypeStruct((rows, feat), jnp.bfloat16),
        grid_spec=pltpu.PrefetchScalarGridSpec(
            num_scalar_prefetch=1,
            grid=(rows // tile,),
            in_specs=[
                pl.BlockSpec((tile, feat), lambda b, p: (b, 0)),
                pl.BlockSpec(band_kv.shape, lambda b, p: (0, 0)),
                pl.BlockSpec(prompt_kv.shape, lambda b, p: (0, 0)),
            ],
            out_specs=pl.BlockSpec((tile, feat), lambda b, p: (b, 0)),
        ),
        cost_estimate=pl.CostEstimate(
            flops=flops,
            transcendentals=rows * (width + PROMPT) * HEADS,
            bytes_accessed=2 * (2 * queries.size + band_kv.size + prompt_kv.size),
        ),
    )(pos, queries, band_kv, prompt_kv)


def per_device(
    hidden_in,
    ln_gain,
    w_qkv,
    w_out,
    final_gain,
    w_heads,
    actions,
    propensity,
    logged_reward,
    switch_index,
):
    tok_rows = hidden_in.shape[0]
    feat_width = hidden_in.shape[1]
    seq_devices = lax.axis_size("seq")
    seq_place = lax.axis_index("seq")
    total_len = tok_rows * seq_devices
    first_pos = seq_place * tok_rows
    hidden_state = hidden_in
    for layer_idx in range(LAYERS):
        normed = layer_norm(hidden_state, ln_gain[layer_idx])
        weights = w_qkv[layer_idx]
        projected = jnp.dot(normed, weights, preferred_element_type=jnp.float32)
        queries = (projected[:, :feat_width] * 0.125).astype(jnp.bfloat16)
        key_value = projected[:, feat_width:].astype(jnp.bfloat16)
        extended = with_halo(key_value, (("seq", 0),), HALF)
        prompt_rows = spread(hidden_state[:PROMPT], "seq")
        prompt_kv = jnp.dot(
            layer_norm(prompt_rows, ln_gain[layer_idx]),
            weights[:, feat_width:],
            preferred_element_type=jnp.float32,
        ).astype(jnp.bfloat16)
        attended = attention(queries, extended, prompt_kv, first_pos, total_len)
        projection = jnp.dot(attended, w_out[layer_idx], preferred_element_type=jnp.float32)
        hidden_state = (hidden_state.astype(jnp.float32) + projection).astype(jnp.bfloat16)
    final = layer_norm(hidden_state, final_gain)
    head_out = jnp.dot(final, w_heads, preferred_element_type=jnp.float32)
    logits = head_out[:, :ACTIONS]
    reward_table = head_out[:, ACTIONS:]
    logit_max = jnp.max(logits, axis=-1, keepdims=True)
    exps = jnp.exp(logits - logit_max)
    policy = exps / jnp.sum(exps, axis=-1, keepdims=True)
    chosen = actions[:, None] == jnp.arange(ACTIONS, dtype=jnp.int32)[None, :]
    rewards = jnp.sum(jnp.where(chosen, reward_table, 0.0), axis=-1)
    chosen_prob = jnp.sum(jnp.where(chosen, policy, 0.0), axis=-1)
    direct = jnp.sum(policy * reward_table, axis=-1)
    logged_prob = propensity.astype(jnp.float32) / 65536.0
    cutoff = 0.5 * switch_index[0].astype(jnp.float32)
    dr_terms = direct + jnp.minimum(chosen_prob / logged_prob, cutoff) * (logged_reward - rewards)
    return (rewards, dr_terms)


def solution(mesh):
    placed = (
        P(("groups", "seq"), None),
        P(),
        P(),
        P(),
        P(),
        P(),
        P(("groups", "seq")),
        P(("groups", "seq")),
        P(("groups", "seq")),
        P("groups"),
    )
    return jax.shard_map(
        per_device,
        mesh=mesh,
        in_specs=placed,
        out_specs=(P(("groups", "seq")), P(("groups", "seq"))),
        check_vma=False,
    )
```

```python
import functools

import jax
import jax.numpy as jnp
from jax import lax
from jax.experimental import pallas as pl
from jax.experimental.pallas import tpu as pltpu
from jax.sharding import PartitionSpec as P

HEADS = 12
HEAD = 64
HALF = 256
PROMPT = 256
ACTIONS = 256
LAYERS = 2


def with_halo(array, sides, width):
    for axis, dim in sides:
        count, length = (lax.axis_size(axis), array.shape[dim])
        up = [(i, (i + 1) % count) for i in range(count - 1)]
        down = [(j, i) for i, j in up]
        last = lax.slice_in_dim(array, length - width, length, axis=dim)
        leading = lax.slice_in_dim(array, 0, width, axis=dim)
        before = lax.ppermute(last, axis, up)
        after = lax.ppermute(leading, axis, down)
        array = jnp.concatenate([before, array, after], axis=dim)
    return array


def tree_rounds(count):
    def near(i):
        out = [i ^ 1]
        if count % 4 == 0:
            out += [i + 4, i ^ 2, i - 4]
        else:
            out += [i + 2, i - 2]
        return [j for j in out if 0 <= j < count]

    holders = {0}
    rounds = []
    while len(holders) < count:
        taken = set()
        pairs = []
        for i in sorted(holders):
            for j in near(i):
                if j not in holders and j not in taken:
                    taken.add(j)
                    pairs.append((i, j))
        if not pairs:
            for j in range(count):
                if j not in holders:
                    pairs.append((min(holders), j))
                    taken.add(j)
                    break
        ops = []
        for pair in pairs:
            for op in ops:
                if all(pair[0] != s for s, _ in op):
                    op.append(pair)
                    break
            else:
                ops.append([pair])
        rounds.append(ops)
        holders |= taken
    return rounds


def spread(block, axis):
    place = lax.axis_index(axis)
    block = jnp.where(place == 0, block, jnp.zeros_like(block))
    for ops in tree_rounds(lax.axis_size(axis)):
        received = block
        for op in ops:
            got = lax.ppermute(block, axis, op)
            targets = jnp.array([t for _, t in op], dtype=jnp.int32)
            received = jnp.where(jnp.any(place == targets), got, received)
        block = received
    return block


def layer_norm(hidden_state, gain_row):
    values_f = hidden_state.astype(jnp.float32)
    row_mean = jnp.mean(values_f, axis=-1, keepdims=True)
    centred = values_f - row_mean
    row_var = jnp.mean(centred * centred, axis=-1, keepdims=True)
    return (centred * lax.rsqrt(row_var + 1e-05) * gain_row).astype(jnp.bfloat16)


QUERY_TILE = 128


def attention_kernel(row0, pos_ref, q_ref, band_ref, prompt_ref, out_ref):
    tile = q_ref.shape[0]
    width = tile + 2 * HALF
    feat = q_ref.shape[1]
    block = pl.program_id(0)
    first = pos_ref[0]
    total = pos_ref[1]
    query_pos = first + row0 + block * tile + lax.broadcasted_iota(jnp.int32, (tile, 1), 0)
    key_pos = first + row0 + block * tile - HALF + lax.broadcasted_iota(jnp.int32, (1, width), 1)
    gap = key_pos - query_pos
    band_ok = (gap >= -HALF) & (gap <= HALF) & (key_pos >= 0) & (key_pos < total)
    prompt_pos = lax.broadcasted_iota(jnp.int32, (1, PROMPT), 1)
    prompt_ok = jnp.abs(prompt_pos - query_pos) > HALF
    start = pl.multiple_of(row0 + block * tile, tile)
    contract = (((1,), (1,)), ((), ()))
    pair = 2 * HEAD
    low_lanes = lax.broadcasted_iota(jnp.int32, (1, pair), 1) < HEAD
    for head_pair in range(HEADS // 2):
        cols = slice(head_pair * pair, (head_pair + 1) * pair)
        vcols = slice(feat + head_pair * pair, feat + (head_pair + 1) * pair)
        query_two = q_ref[:, cols]
        band_keys = band_ref[pl.ds(start, width), cols]
        band_values = band_ref[pl.ds(start, width), vcols]
        prompt_keys = prompt_ref[:, cols]
        prompt_values = prompt_ref[:, vcols]
        halves = []
        for low in (True, False):
            keep = low_lanes if low else jnp.logical_not(low_lanes)
            query = jnp.where(keep, query_two, jnp.zeros_like(query_two))
            band_scores = lax.dot_general(
                query, band_keys, contract, preferred_element_type=jnp.float32
            )
            prompt_scores = lax.dot_general(
                query, prompt_keys, contract, preferred_element_type=jnp.float32
            )
            band_scores = jnp.where(band_ok, band_scores, -1e30)
            prompt_scores = jnp.where(prompt_ok, prompt_scores, -1e30)
            row_max = jnp.maximum(
                jnp.max(band_scores, axis=1, keepdims=True),
                jnp.max(prompt_scores, axis=1, keepdims=True),
            )
            band_exp = jnp.exp(band_scores - row_max)
            prompt_exp = jnp.exp(prompt_scores - row_max)
            denom = jnp.sum(band_exp, axis=1, keepdims=True) + jnp.sum(
                prompt_exp, axis=1, keepdims=True
            )
            scale = 1.0 / denom
            band_probs = (band_exp * scale).astype(jnp.bfloat16)
            prompt_probs = (prompt_exp * scale).astype(jnp.bfloat16)
            halves.append(
                jnp.dot(band_probs, band_values, preferred_element_type=jnp.float32)
                + jnp.dot(prompt_probs, prompt_values, preferred_element_type=jnp.float32)
            )
        attn = jnp.where(low_lanes, halves[0], halves[1])
        out_ref[:, cols] = attn.astype(out_ref.dtype)


def attention(queries, band_kv, prompt_kv, first_pos, total_len, row0, count):
    feat = queries.shape[1]
    tile = min(QUERY_TILE, count)
    pos = jnp.stack([first_pos, total_len]).astype(jnp.int32)
    width = tile + 2 * HALF
    flops = 4 * count * (width + PROMPT) * feat
    skip = row0 // tile
    return pl.pallas_call(
        functools.partial(attention_kernel, row0),
        out_shape=jax.ShapeDtypeStruct((count, feat), jnp.bfloat16),
        grid_spec=pltpu.PrefetchScalarGridSpec(
            num_scalar_prefetch=1,
            grid=(count // tile,),
            in_specs=[
                pl.BlockSpec((tile, feat), lambda b, p: (b + skip, 0)),
                pl.BlockSpec(band_kv.shape, lambda b, p: (0, 0)),
                pl.BlockSpec(prompt_kv.shape, lambda b, p: (0, 0)),
            ],
            out_specs=pl.BlockSpec((tile, feat), lambda b, p: (b, 0)),
        ),
        cost_estimate=pl.CostEstimate(
            flops=flops,
            transcendentals=count * (width + PROMPT) * HEADS,
            bytes_accessed=2 * (2 * count * feat + band_kv.size + prompt_kv.size),
        ),
    )(pos, queries, band_kv, prompt_kv)


def per_device(
    hidden_in,
    ln_gain,
    w_qkv,
    w_out,
    final_gain,
    w_heads,
    actions,
    propensity,
    logged_reward,
    switch_index,
):
    tok_rows = hidden_in.shape[0]
    feat_width = hidden_in.shape[1]
    seq_devices = lax.axis_size("seq")
    seq_place = lax.axis_index("seq")
    total_len = tok_rows * seq_devices
    first_pos = seq_place * tok_rows
    half_rows = tok_rows // 2
    hidden_state = hidden_in
    prompt_source = hidden_in[:PROMPT]
    for layer_idx in range(LAYERS):
        gain = ln_gain[layer_idx]
        weights = w_qkv[layer_idx]
        extended = with_halo(hidden_state, (("seq", 0),), HALF)
        prompt_rows = spread(prompt_source, "seq")
        extended_normed = layer_norm(extended, gain)
        band_kv = jnp.dot(
            extended_normed, weights[:, feat_width:], preferred_element_type=jnp.float32
        ).astype(jnp.bfloat16)
        normed = extended_normed[HALF : HALF + tok_rows]
        queries = (
            jnp.dot(normed, weights[:, :feat_width], preferred_element_type=jnp.float32) * 0.125
        ).astype(jnp.bfloat16)
        prompt_kv = jnp.dot(
            layer_norm(prompt_rows, gain),
            weights[:, feat_width:],
            preferred_element_type=jnp.float32,
        ).astype(jnp.bfloat16)
        parts = []
        for row0 in (0, half_rows):
            attended = attention(
                queries, band_kv, prompt_kv, first_pos, total_len, row0, half_rows
            )
            projection = jnp.dot(
                attended, w_out[layer_idx], preferred_element_type=jnp.float32
            )
            rows_in = hidden_state[row0 : row0 + half_rows].astype(jnp.float32)
            parts.append((rows_in + projection).astype(jnp.bfloat16))
        hidden_state = jnp.concatenate(parts, axis=0)
        if half_rows >= PROMPT:
            prompt_source = parts[0][:PROMPT]
        else:
            prompt_source = hidden_state[:PROMPT]
    final = layer_norm(hidden_state, final_gain)
    head_out = jnp.dot(final, w_heads, preferred_element_type=jnp.float32)
    logits = head_out[:, :ACTIONS]
    reward_table = head_out[:, ACTIONS:]
    logit_max = jnp.max(logits, axis=-1, keepdims=True)
    exps = jnp.exp(logits - logit_max)
    policy = exps / jnp.sum(exps, axis=-1, keepdims=True)
    chosen = actions[:, None] == jnp.arange(ACTIONS, dtype=jnp.int32)[None, :]
    rewards = jnp.sum(jnp.where(chosen, reward_table, 0.0), axis=-1)
    chosen_prob = jnp.sum(jnp.where(chosen, policy, 0.0), axis=-1)
    direct = jnp.sum(policy * reward_table, axis=-1)
    logged_prob = propensity.astype(jnp.float32) / 65536.0
    cutoff = 0.5 * switch_index[0].astype(jnp.float32)
    dr_terms = direct + jnp.minimum(chosen_prob / logged_prob, cutoff) * (logged_reward - rewards)
    return (rewards, dr_terms)


def solution(mesh):
    placed = (
        P(("groups", "seq"), None),
        P(),
        P(),
        P(),
        P(),
        P(),
        P(("groups", "seq")),
        P(("groups", "seq")),
        P(("groups", "seq")),
        P("groups"),
    )
    return jax.shard_map(
        per_device,
        mesh=mesh,
        in_specs=placed,
        out_specs=(P(("groups", "seq")), P(("groups", "seq"))),
        check_vma=False,
    )
```

```python
import functools

import jax
import jax.numpy as jnp
from jax import lax
from jax.experimental import pallas as pl
from jax.experimental.pallas import tpu as pltpu
from jax.sharding import PartitionSpec as P

HEADS = 12
HEAD = 64
HALF = 256
PROMPT = 256
ACTIONS = 256
LAYERS = 2


def with_halo(array, sides, width):
    for axis, dim in sides:
        count, length = (lax.axis_size(axis), array.shape[dim])
        up = [(i, (i + 1) % count) for i in range(count - 1)]
        down = [(j, i) for i, j in up]
        last = lax.slice_in_dim(array, length - width, length, axis=dim)
        leading = lax.slice_in_dim(array, 0, width, axis=dim)
        before = lax.ppermute(last, axis, up)
        after = lax.ppermute(leading, axis, down)
        array = jnp.concatenate([before, array, after], axis=dim)
    return array


def tree_rounds(count):
    def near(i):
        out = [i ^ 1]
        if count % 4 == 0:
            out += [i + 4, i ^ 2, i - 4]
        else:
            out += [i + 2, i - 2]
        return [j for j in out if 0 <= j < count]

    holders = {0}
    rounds = []
    while len(holders) < count:
        taken = set()
        pairs = []
        for i in sorted(holders):
            for j in near(i):
                if j not in holders and j not in taken:
                    taken.add(j)
                    pairs.append((i, j))
        if not pairs:
            for j in range(count):
                if j not in holders:
                    pairs.append((min(holders), j))
                    taken.add(j)
                    break
        ops = []
        for pair in pairs:
            for op in ops:
                if all(pair[0] != s for s, _ in op):
                    op.append(pair)
                    break
            else:
                ops.append([pair])
        rounds.append(ops)
        holders |= taken
    return rounds


def spread(block, axis):
    place = lax.axis_index(axis)
    block = jnp.where(place == 0, block, jnp.zeros_like(block))
    for ops in tree_rounds(lax.axis_size(axis)):
        received = block
        for op in ops:
            got = lax.ppermute(block, axis, op)
            targets = jnp.array([t for _, t in op], dtype=jnp.int32)
            received = jnp.where(jnp.any(place == targets), got, received)
        block = received
    return block


def layer_norm(hidden_state, gain_row):
    values_f = hidden_state.astype(jnp.float32)
    row_mean = jnp.mean(values_f, axis=-1, keepdims=True)
    centred = values_f - row_mean
    row_var = jnp.mean(centred * centred, axis=-1, keepdims=True)
    return (centred * lax.rsqrt(row_var + 1e-05) * gain_row).astype(jnp.bfloat16)


QUERY_TILE = 128
GROUP = 4


def attention_kernel(row0, pos_ref, q_ref, *refs):
    band_refs = refs[:-2]
    prompt_ref, out_ref = refs[-2:]
    tile = q_ref.shape[0]
    width = tile * len(band_refs)
    feat = q_ref.shape[1]
    lanes = GROUP * HEAD
    block = pl.program_id(0)
    first = pos_ref[0]
    total = pos_ref[1]
    row_in_tile = lax.broadcasted_iota(jnp.int32, (GROUP * tile, 1), 0) % tile
    query_pos = first + row0 + block * tile + row_in_tile
    key_pos = first + row0 + block * tile - HALF + lax.broadcasted_iota(jnp.int32, (1, width), 1)
    gap = key_pos - query_pos
    band_ok = (gap >= -HALF) & (gap <= HALF) & (key_pos >= 0) & (key_pos < total)
    prompt_pos = lax.broadcasted_iota(jnp.int32, (1, PROMPT), 1)
    prompt_ok = jnp.abs(prompt_pos - query_pos) > HALF
    contract = (((1,), (1,)), ((), ()))
    lane_head = lax.broadcasted_iota(jnp.int32, (1, lanes), 1) // HEAD
    for group in range(feat // lanes):
        cols = slice(group * lanes, (group + 1) * lanes)
        vcols = slice(feat + group * lanes, feat + (group + 1) * lanes)
        band_keys = jnp.concatenate([ref[:, cols] for ref in band_refs], axis=0)
        band_values = jnp.concatenate([ref[:, vcols] for ref in band_refs], axis=0)
        query = q_ref[:, cols]
        stacked = jnp.concatenate(
            [jnp.where(lane_head == j, query, jnp.zeros_like(query)) for j in range(GROUP)],
            axis=0,
        )
        band_scores = lax.dot_general(
            stacked, band_keys, contract, preferred_element_type=jnp.float32
        )
        prompt_scores = lax.dot_general(
            stacked, prompt_ref[:, cols], contract, preferred_element_type=jnp.float32
        )
        band_scores = jnp.where(band_ok, band_scores, -1e30)
        prompt_scores = jnp.where(prompt_ok, prompt_scores, -1e30)
        row_max = jnp.maximum(
            jnp.max(band_scores, axis=1, keepdims=True),
            jnp.max(prompt_scores, axis=1, keepdims=True),
        )
        band_exp = jnp.exp(band_scores - row_max)
        prompt_exp = jnp.exp(prompt_scores - row_max)
        denom = jnp.sum(band_exp, axis=1, keepdims=True) + jnp.sum(
            prompt_exp, axis=1, keepdims=True
        )
        scale = 1.0 / denom
        band_probs = (band_exp * scale).astype(jnp.bfloat16)
        prompt_probs = (prompt_exp * scale).astype(jnp.bfloat16)
        mixed = jnp.dot(band_probs, band_values, preferred_element_type=jnp.float32) + jnp.dot(
            prompt_probs, prompt_ref[:, vcols], preferred_element_type=jnp.float32
        )
        attn = mixed[:tile]
        for j in range(1, GROUP):
            attn = jnp.where(lane_head == j, mixed[j * tile : (j + 1) * tile], attn)
        out_ref[:, cols] = attn.astype(out_ref.dtype)


def attention(queries, band_kv, prompt_kv, first_pos, total_len, row0, count):
    feat = queries.shape[1]
    tile = min(QUERY_TILE, count)
    pos = jnp.stack([first_pos, total_len]).astype(jnp.int32)
    pieces = 1 + 2 * HALF // tile
    width = tile * pieces
    flops = 4 * count * (width + PROMPT) * feat * GROUP
    skip = row0 // tile
    band_specs = [
        pl.BlockSpec((tile, band_kv.shape[1]), lambda b, p, k=k: (b + skip + k, 0))
        for k in range(pieces)
    ]
    return pl.pallas_call(
        functools.partial(attention_kernel, row0),
        out_shape=jax.ShapeDtypeStruct((count, feat), jnp.bfloat16),
        grid_spec=pltpu.PrefetchScalarGridSpec(
            num_scalar_prefetch=1,
            grid=(count // tile,),
            in_specs=[pl.BlockSpec((tile, feat), lambda b, p: (b + skip, 0))]
            + band_specs
            + [pl.BlockSpec(prompt_kv.shape, lambda b, p: (0, 0))],
            out_specs=pl.BlockSpec((tile, feat), lambda b, p: (b, 0)),
        ),
        cost_estimate=pl.CostEstimate(
            flops=flops,
            transcendentals=count * (width + PROMPT) * HEADS,
            bytes_accessed=2 * (2 * count * feat + pieces * count * band_kv.shape[1] + prompt_kv.size),
        ),
    )(pos, queries, *([band_kv] * pieces), prompt_kv)


def per_device(
    hidden_in,
    ln_gain,
    w_qkv,
    w_out,
    final_gain,
    w_heads,
    actions,
    propensity,
    logged_reward,
    switch_index,
):
    tok_rows = hidden_in.shape[0]
    feat_width = hidden_in.shape[1]
    seq_devices = lax.axis_size("seq")
    seq_place = lax.axis_index("seq")
    total_len = tok_rows * seq_devices
    first_pos = seq_place * tok_rows
    half_rows = tok_rows // 2
    hidden_state = hidden_in
    prompt_source = hidden_in[:PROMPT]
    for layer_idx in range(LAYERS):
        gain = ln_gain[layer_idx]
        weights = w_qkv[layer_idx]
        extended = with_halo(hidden_state, (("seq", 0),), HALF)
        prompt_rows = spread(prompt_source, "seq")
        extended_normed = layer_norm(extended, gain)
        band_kv = jnp.dot(
            extended_normed, weights[:, feat_width:], preferred_element_type=jnp.float32
        ).astype(jnp.bfloat16)
        normed = extended_normed[HALF : HALF + tok_rows]
        queries = (
            jnp.dot(normed, weights[:, :feat_width], preferred_element_type=jnp.float32) * 0.125
        ).astype(jnp.bfloat16)
        prompt_kv = jnp.dot(
            layer_norm(prompt_rows, gain),
            weights[:, feat_width:],
            preferred_element_type=jnp.float32,
        ).astype(jnp.bfloat16)
        parts = []
        for row0 in (0, half_rows):
            attended = attention(
                queries, band_kv, prompt_kv, first_pos, total_len, row0, half_rows
            )
            projection = jnp.dot(
                attended, w_out[layer_idx], preferred_element_type=jnp.float32
            )
            rows_in = hidden_state[row0 : row0 + half_rows].astype(jnp.float32)
            parts.append((rows_in + projection).astype(jnp.bfloat16))
        hidden_state = jnp.concatenate(parts, axis=0)
        if half_rows >= PROMPT:
            prompt_source = parts[0][:PROMPT]
        else:
            prompt_source = hidden_state[:PROMPT]
    final = layer_norm(hidden_state, final_gain)
    head_out = jnp.dot(final, w_heads, preferred_element_type=jnp.float32)
    logits = head_out[:, :ACTIONS]
    reward_table = head_out[:, ACTIONS:]
    logit_max = jnp.max(logits, axis=-1, keepdims=True)
    exps = jnp.exp(logits - logit_max)
    policy = exps / jnp.sum(exps, axis=-1, keepdims=True)
    chosen = actions[:, None] == jnp.arange(ACTIONS, dtype=jnp.int32)[None, :]
    rewards = jnp.sum(jnp.where(chosen, reward_table, 0.0), axis=-1)
    chosen_prob = jnp.sum(jnp.where(chosen, policy, 0.0), axis=-1)
    direct = jnp.sum(policy * reward_table, axis=-1)
    logged_prob = propensity.astype(jnp.float32) / 65536.0
    cutoff = 0.5 * switch_index[0].astype(jnp.float32)
    dr_terms = direct + jnp.minimum(chosen_prob / logged_prob, cutoff) * (logged_reward - rewards)
    return (rewards, dr_terms)


def solution(mesh):
    placed = (
        P(("groups", "seq"), None),
        P(),
        P(),
        P(),
        P(),
        P(),
        P(("groups", "seq")),
        P(("groups", "seq")),
        P(("groups", "seq")),
        P("groups"),
    )
    return jax.shard_map(
        per_device,
        mesh=mesh,
        in_specs=placed,
        out_specs=(P(("groups", "seq")), P(("groups", "seq"))),
        check_vma=False,
    )
```

```python
import functools

import jax
import jax.numpy as jnp
from jax import lax
from jax.experimental import pallas as pl
from jax.experimental.pallas import tpu as pltpu
from jax.sharding import PartitionSpec as P

HEADS = 12
HEAD = 64
HALF = 256
PROMPT = 256
ACTIONS = 256
LAYERS = 2


def with_halo(array, sides, width):
    for axis, dim in sides:
        count, length = (lax.axis_size(axis), array.shape[dim])
        up = [(i, (i + 1) % count) for i in range(count - 1)]
        down = [(j, i) for i, j in up]
        last = lax.slice_in_dim(array, length - width, length, axis=dim)
        leading = lax.slice_in_dim(array, 0, width, axis=dim)
        before = lax.ppermute(last, axis, up)
        after = lax.ppermute(leading, axis, down)
        array = jnp.concatenate([before, array, after], axis=dim)
    return array


def tree_rounds(count):
    def near(i):
        out = [i ^ 1]
        if count % 4 == 0:
            out += [i + 4, i ^ 2, i - 4]
        else:
            out += [i + 2, i - 2]
        return [j for j in out if 0 <= j < count]

    holders = {0}
    rounds = []
    while len(holders) < count:
        taken = set()
        pairs = []
        for i in sorted(holders):
            for j in near(i):
                if j not in holders and j not in taken:
                    taken.add(j)
                    pairs.append((i, j))
        if not pairs:
            for j in range(count):
                if j not in holders:
                    pairs.append((min(holders), j))
                    taken.add(j)
                    break
        ops = []
        for pair in pairs:
            for op in ops:
                if all(pair[0] != s for s, _ in op):
                    op.append(pair)
                    break
            else:
                ops.append([pair])
        rounds.append(ops)
        holders |= taken
    return rounds


def spread(block, axis):
    place = lax.axis_index(axis)
    block = jnp.where(place == 0, block, jnp.zeros_like(block))
    for ops in tree_rounds(lax.axis_size(axis)):
        received = block
        for op in ops:
            got = lax.ppermute(block, axis, op)
            targets = jnp.array([t for _, t in op], dtype=jnp.int32)
            received = jnp.where(jnp.any(place == targets), got, received)
        block = received
    return block


def layer_norm(hidden_state, gain_row):
    values_f = hidden_state.astype(jnp.float32)
    row_mean = jnp.mean(values_f, axis=-1, keepdims=True)
    centred = values_f - row_mean
    row_var = jnp.mean(centred * centred, axis=-1, keepdims=True)
    return (centred * lax.rsqrt(row_var + 1e-05) * gain_row).astype(jnp.bfloat16)


QUERY_TILE = 128
GROUP = 4


def stack_heads(query, lane_head):
    return jnp.concatenate(
        [jnp.where(lane_head == j, query, jnp.zeros_like(query)) for j in range(GROUP)],
        axis=0,
    )


def to_lanes(stacked, lane_head, tile):
    out = stacked[:tile]
    for j in range(1, GROUP):
        out = jnp.where(lane_head == j, stacked[j * tile : (j + 1) * tile], out)
    return out


def band_kernel(row0, pos_ref, q_ref, *refs):
    band_refs = refs[:-2]
    out_ref, lse_ref = refs[-2:]
    tile = q_ref.shape[0]
    width = tile * len(band_refs)
    feat = q_ref.shape[1]
    lanes = GROUP * HEAD
    block = pl.program_id(0)
    first = pos_ref[0]
    total = pos_ref[1]
    row_in_tile = lax.broadcasted_iota(jnp.int32, (GROUP * tile, 1), 0) % tile
    query_pos = first + row0 + block * tile + row_in_tile
    key_pos = first + row0 + block * tile - HALF + lax.broadcasted_iota(jnp.int32, (1, width), 1)
    gap = key_pos - query_pos
    band_ok = (gap >= -HALF) & (gap <= HALF) & (key_pos >= 0) & (key_pos < total)
    contract = (((1,), (1,)), ((), ()))
    lane_head = lax.broadcasted_iota(jnp.int32, (1, lanes), 1) // HEAD
    for group in range(feat // lanes):
        cols = slice(group * lanes, (group + 1) * lanes)
        vcols = slice(feat + group * lanes, feat + (group + 1) * lanes)
        band_keys = jnp.concatenate([ref[:, cols] for ref in band_refs], axis=0)
        band_values = jnp.concatenate([ref[:, vcols] for ref in band_refs], axis=0)
        stacked = stack_heads(q_ref[:, cols], lane_head)
        scores = lax.dot_general(stacked, band_keys, contract, preferred_element_type=jnp.float32)
        scores = jnp.where(band_ok, scores, -1e30)
        row_max = jnp.max(scores, axis=1, keepdims=True)
        exps = jnp.exp(scores - row_max)
        denom = jnp.sum(exps, axis=1, keepdims=True)
        mixed = jnp.dot(exps.astype(jnp.bfloat16), band_values, preferred_element_type=jnp.float32)
        mixed = mixed * (1.0 / denom)
        out_ref[:, cols] = to_lanes(mixed, lane_head, tile)
        lse_ref[:, cols] = to_lanes(
            jnp.broadcast_to(row_max + jnp.log(denom), mixed.shape), lane_head, tile
        )


def prompt_kernel(row0, pos_ref, q_ref, prompt_ref, band_out_ref, lse_ref, out_ref):
    tile = q_ref.shape[0]
    feat = q_ref.shape[1]
    lanes = GROUP * HEAD
    block = pl.program_id(0)
    first = pos_ref[0]
    row_in_tile = lax.broadcasted_iota(jnp.int32, (GROUP * tile, 1), 0) % tile
    query_pos = first + row0 + block * tile + row_in_tile
    prompt_pos = lax.broadcasted_iota(jnp.int32, (1, PROMPT), 1)
    prompt_ok = jnp.abs(prompt_pos - query_pos) > HALF
    contract = (((1,), (1,)), ((), ()))
    lane_head = lax.broadcasted_iota(jnp.int32, (1, lanes), 1) // HEAD
    for group in range(feat // lanes):
        cols = slice(group * lanes, (group + 1) * lanes)
        vcols = slice(feat + group * lanes, feat + (group + 1) * lanes)
        stacked = stack_heads(q_ref[:, cols], lane_head)
        scores = lax.dot_general(
            stacked, prompt_ref[:, cols], contract, preferred_element_type=jnp.float32
        )
        scores = jnp.where(prompt_ok, scores, -1e30)
        row_max = jnp.max(scores, axis=1, keepdims=True)
        exps = jnp.exp(scores - row_max)
        denom = jnp.sum(exps, axis=1, keepdims=True)
        mixed = jnp.dot(
            exps.astype(jnp.bfloat16), prompt_ref[:, vcols], preferred_element_type=jnp.float32
        )
        prompt_acc = to_lanes(mixed, lane_head, tile)
        prompt_max = to_lanes(jnp.broadcast_to(row_max, mixed.shape), lane_head, tile)
        prompt_sum = to_lanes(jnp.broadcast_to(denom, mixed.shape), lane_head, tile)
        band_lse = lse_ref[:, cols]
        top = jnp.maximum(band_lse, prompt_max)
        band_weight = jnp.exp(band_lse - top)
        prompt_weight = jnp.exp(prompt_max - top)
        merged = (band_out_ref[:, cols] * band_weight + prompt_acc * prompt_weight) / (
            band_weight + prompt_sum * prompt_weight
        )
        out_ref[:, cols] = merged.astype(out_ref.dtype)


def attention(queries, band_kv, prompt_kv, first_pos, total_len, row0, count):
    feat = queries.shape[1]
    tile = min(QUERY_TILE, count)
    pos = jnp.stack([first_pos, total_len]).astype(jnp.int32)
    pieces = 1 + 2 * HALF // tile
    width = tile * pieces
    skip = row0 // tile
    band_specs = [
        pl.BlockSpec((tile, band_kv.shape[1]), lambda b, p, k=k: (b + skip + k, 0))
        for k in range(pieces)
    ]
    row_spec = pl.BlockSpec((tile, feat), lambda b, p: (b, 0))
    q_spec = pl.BlockSpec((tile, feat), lambda b, p: (b + skip, 0))
    band_out, band_lse = pl.pallas_call(
        functools.partial(band_kernel, row0),
        out_shape=(
            jax.ShapeDtypeStruct((count, feat), jnp.float32),
            jax.ShapeDtypeStruct((count, feat), jnp.float32),
        ),
        grid_spec=pltpu.PrefetchScalarGridSpec(
            num_scalar_prefetch=1,
            grid=(count // tile,),
            in_specs=[q_spec] + band_specs,
            out_specs=(row_spec, row_spec),
        ),
        cost_estimate=pl.CostEstimate(
            flops=4 * count * width * feat * GROUP,
            transcendentals=count * width * HEADS,
            bytes_accessed=2 * count * feat + 2 * pieces * count * band_kv.shape[1] + 8 * count * feat,
        ),
    )(pos, queries, *([band_kv] * pieces))
    return pl.pallas_call(
        functools.partial(prompt_kernel, row0),
        out_shape=jax.ShapeDtypeStruct((count, feat), jnp.bfloat16),
        grid_spec=pltpu.PrefetchScalarGridSpec(
            num_scalar_prefetch=1,
            grid=(count // tile,),
            in_specs=[q_spec, pl.BlockSpec(prompt_kv.shape, lambda b, p: (0, 0)), row_spec, row_spec],
            out_specs=row_spec,
        ),
        cost_estimate=pl.CostEstimate(
            flops=4 * count * PROMPT * feat * GROUP,
            transcendentals=count * PROMPT * HEADS,
            bytes_accessed=4 * count * feat + 2 * prompt_kv.size + 8 * count * feat,
        ),
    )(pos, queries, prompt_kv, band_out, band_lse)


def per_device(
    hidden_in,
    ln_gain,
    w_qkv,
    w_out,
    final_gain,
    w_heads,
    actions,
    propensity,
    logged_reward,
    switch_index,
):
    tok_rows = hidden_in.shape[0]
    feat_width = hidden_in.shape[1]
    seq_devices = lax.axis_size("seq")
    seq_place = lax.axis_index("seq")
    total_len = tok_rows * seq_devices
    first_pos = seq_place * tok_rows
    half_rows = tok_rows // 2
    hidden_state = hidden_in
    prompt_source = hidden_in[:PROMPT]
    for layer_idx in range(LAYERS):
        gain = ln_gain[layer_idx]
        weights = w_qkv[layer_idx]
        extended = with_halo(hidden_state, (("seq", 0),), HALF)
        prompt_rows = spread(prompt_source, "seq")
        extended_normed = layer_norm(extended, gain)
        band_kv = jnp.dot(
            extended_normed, weights[:, feat_width:], preferred_element_type=jnp.float32
        ).astype(jnp.bfloat16)
        normed = extended_normed[HALF : HALF + tok_rows]
        queries = (
            jnp.dot(normed, weights[:, :feat_width], preferred_element_type=jnp.float32) * 0.125
        ).astype(jnp.bfloat16)
        prompt_kv = jnp.dot(
            layer_norm(prompt_rows, gain),
            weights[:, feat_width:],
            preferred_element_type=jnp.float32,
        ).astype(jnp.bfloat16)
        parts = []
        for row0 in (0, half_rows):
            attended = attention(
                queries, band_kv, prompt_kv, first_pos, total_len, row0, half_rows
            )
            projection = jnp.dot(
                attended, w_out[layer_idx], preferred_element_type=jnp.float32
            )
            rows_in = hidden_state[row0 : row0 + half_rows].astype(jnp.float32)
            parts.append((rows_in + projection).astype(jnp.bfloat16))
        hidden_state = jnp.concatenate(parts, axis=0)
        if half_rows >= PROMPT:
            prompt_source = parts[0][:PROMPT]
        else:
            prompt_source = hidden_state[:PROMPT]
    final = layer_norm(hidden_state, final_gain)
    head_out = jnp.dot(final, w_heads, preferred_element_type=jnp.float32)
    logits = head_out[:, :ACTIONS]
    reward_table = head_out[:, ACTIONS:]
    logit_max = jnp.max(logits, axis=-1, keepdims=True)
    exps = jnp.exp(logits - logit_max)
    policy = exps / jnp.sum(exps, axis=-1, keepdims=True)
    chosen = actions[:, None] == jnp.arange(ACTIONS, dtype=jnp.int32)[None, :]
    rewards = jnp.sum(jnp.where(chosen, reward_table, 0.0), axis=-1)
    chosen_prob = jnp.sum(jnp.where(chosen, policy, 0.0), axis=-1)
    direct = jnp.sum(policy * reward_table, axis=-1)
    logged_prob = propensity.astype(jnp.float32) / 65536.0
    cutoff = 0.5 * switch_index[0].astype(jnp.float32)
    dr_terms = direct + jnp.minimum(chosen_prob / logged_prob, cutoff) * (logged_reward - rewards)
    return (rewards, dr_terms)


def solution(mesh):
    placed = (
        P(("groups", "seq"), None),
        P(),
        P(),
        P(),
        P(),
        P(),
        P(("groups", "seq")),
        P(("groups", "seq")),
        P(("groups", "seq")),
        P("groups"),
    )
    return jax.shard_map(
        per_device,
        mesh=mesh,
        in_specs=placed,
        out_specs=(P(("groups", "seq")), P(("groups", "seq"))),
        check_vma=False,
    )
```

```python
import functools

import jax
import jax.numpy as jnp
from jax import lax
from jax.experimental import pallas as pl
from jax.experimental.pallas import tpu as pltpu
from jax.sharding import PartitionSpec as P

HEADS = 12
HEAD = 64
HALF = 256
PROMPT = 256
ACTIONS = 256
LAYERS = 2


def with_halo(array, sides, width):
    for axis, dim in sides:
        count, length = (lax.axis_size(axis), array.shape[dim])
        up = [(i, (i + 1) % count) for i in range(count - 1)]
        down = [(j, i) for i, j in up]
        last = lax.slice_in_dim(array, length - width, length, axis=dim)
        leading = lax.slice_in_dim(array, 0, width, axis=dim)
        before = lax.ppermute(last, axis, up)
        after = lax.ppermute(leading, axis, down)
        array = jnp.concatenate([before, array, after], axis=dim)
    return array


def tree_rounds(count):
    if count & (count - 1) == 0:
        bits = []
        step = count // 2
        while step:
            bits.append(step)
            step //= 2
        return [[[(i, i + bit) for i in range(0, count, 2 * bit)]] for bit in bits]
    rounds = []
    held = 1
    while held < count:
        rounds.append([[(i, i + held) for i in range(min(held, count - held))]])
        held *= 2
    return rounds


def spread(block, axis):
    place = lax.axis_index(axis)
    block = jnp.where(place == 0, block, jnp.zeros_like(block))
    for ops in tree_rounds(lax.axis_size(axis)):
        received = block
        for op in ops:
            got = lax.ppermute(block, axis, op)
            targets = jnp.array([t for _, t in op], dtype=jnp.int32)
            received = jnp.where(jnp.any(place == targets), got, received)
        block = received
    return block


def layer_norm(hidden_state, gain_row):
    values_f = hidden_state.astype(jnp.float32)
    row_mean = jnp.mean(values_f, axis=-1, keepdims=True)
    centred = values_f - row_mean
    row_var = jnp.mean(centred * centred, axis=-1, keepdims=True)
    return (centred * lax.rsqrt(row_var + 1e-05) * gain_row).astype(jnp.bfloat16)


QUERY_TILE = 128
GROUP = 4


def attention_kernel(row0, pos_ref, q_ref, *refs):
    band_refs = refs[:-2]
    prompt_ref, out_ref = refs[-2:]
    tile = q_ref.shape[0]
    width = tile * len(band_refs)
    feat = q_ref.shape[1]
    lanes = GROUP * HEAD
    block = pl.program_id(0)
    first = pos_ref[0]
    total = pos_ref[1]
    row_in_tile = lax.broadcasted_iota(jnp.int32, (GROUP * tile, 1), 0) % tile
    query_pos = first + row0 + block * tile + row_in_tile
    key_pos = first + row0 + block * tile - HALF + lax.broadcasted_iota(jnp.int32, (1, width), 1)
    gap = key_pos - query_pos
    band_ok = (gap >= -HALF) & (gap <= HALF) & (key_pos >= 0) & (key_pos < total)
    prompt_pos = lax.broadcasted_iota(jnp.int32, (1, PROMPT), 1)
    prompt_ok = jnp.abs(prompt_pos - query_pos) > HALF
    contract = (((1,), (1,)), ((), ()))
    lane_head = lax.broadcasted_iota(jnp.int32, (1, lanes), 1) // HEAD
    for group in range(feat // lanes):
        cols = slice(group * lanes, (group + 1) * lanes)
        vcols = slice(feat + group * lanes, feat + (group + 1) * lanes)
        band_keys = jnp.concatenate([ref[:, cols] for ref in band_refs], axis=0)
        band_values = jnp.concatenate([ref[:, vcols] for ref in band_refs], axis=0)
        query = q_ref[:, cols]
        stacked = jnp.concatenate(
            [jnp.where(lane_head == j, query, jnp.zeros_like(query)) for j in range(GROUP)],
            axis=0,
        )
        band_scores = lax.dot_general(
            stacked, band_keys, contract, preferred_element_type=jnp.float32
        )
        prompt_scores = lax.dot_general(
            stacked, prompt_ref[:, cols], contract, preferred_element_type=jnp.float32
        )
        band_scores = jnp.where(band_ok, band_scores, -1e30)
        prompt_scores = jnp.where(prompt_ok, prompt_scores, -1e30)
        row_max = jnp.maximum(
            jnp.max(band_scores, axis=1, keepdims=True),
            jnp.max(prompt_scores, axis=1, keepdims=True),
        )
        band_exp = jnp.exp(band_scores - row_max)
        prompt_exp = jnp.exp(prompt_scores - row_max)
        denom = jnp.sum(band_exp, axis=1, keepdims=True) + jnp.sum(
            prompt_exp, axis=1, keepdims=True
        )
        scale = 1.0 / denom
        band_probs = (band_exp * scale).astype(jnp.bfloat16)
        prompt_probs = (prompt_exp * scale).astype(jnp.bfloat16)
        mixed = jnp.dot(band_probs, band_values, preferred_element_type=jnp.float32) + jnp.dot(
            prompt_probs, prompt_ref[:, vcols], preferred_element_type=jnp.float32
        )
        attn = mixed[:tile]
        for j in range(1, GROUP):
            attn = jnp.where(lane_head == j, mixed[j * tile : (j + 1) * tile], attn)
        out_ref[:, cols] = attn.astype(out_ref.dtype)


def attention(queries, band_kv, prompt_kv, first_pos, total_len, row0, count):
    feat = queries.shape[1]
    tile = min(QUERY_TILE, count)
    pos = jnp.stack([first_pos, total_len]).astype(jnp.int32)
    pieces = 1 + 2 * HALF // tile
    width = tile * pieces
    flops = 4 * count * (width + PROMPT) * feat * GROUP
    skip = row0 // tile
    band_specs = [
        pl.BlockSpec((tile, band_kv.shape[1]), lambda b, p, k=k: (b + skip + k, 0))
        for k in range(pieces)
    ]
    return pl.pallas_call(
        functools.partial(attention_kernel, row0),
        out_shape=jax.ShapeDtypeStruct((count, feat), jnp.bfloat16),
        grid_spec=pltpu.PrefetchScalarGridSpec(
            num_scalar_prefetch=1,
            grid=(count // tile,),
            in_specs=[pl.BlockSpec((tile, feat), lambda b, p: (b + skip, 0))]
            + band_specs
            + [pl.BlockSpec(prompt_kv.shape, lambda b, p: (0, 0))],
            out_specs=pl.BlockSpec((tile, feat), lambda b, p: (b, 0)),
        ),
        cost_estimate=pl.CostEstimate(
            flops=flops,
            transcendentals=count * (width + PROMPT) * HEADS,
            bytes_accessed=2 * (2 * count * feat + pieces * count * band_kv.shape[1] + prompt_kv.size),
        ),
    )(pos, queries, *([band_kv] * pieces), prompt_kv)


def per_device(
    hidden_in,
    ln_gain,
    w_qkv,
    w_out,
    final_gain,
    w_heads,
    actions,
    propensity,
    logged_reward,
    switch_index,
):
    tok_rows = hidden_in.shape[0]
    feat_width = hidden_in.shape[1]
    seq_devices = lax.axis_size("seq")
    seq_place = lax.axis_index("seq")
    total_len = tok_rows * seq_devices
    first_pos = seq_place * tok_rows
    half_rows = tok_rows // 2
    hidden_state = hidden_in
    prompt_source = hidden_in[:PROMPT]
    for layer_idx in range(LAYERS):
        gain = ln_gain[layer_idx]
        weights = w_qkv[layer_idx]
        extended = with_halo(hidden_state, (("seq", 0),), HALF)
        prompt_rows = spread(prompt_source, "seq")
        extended_normed = layer_norm(extended, gain)
        band_kv = jnp.dot(
            extended_normed, weights[:, feat_width:], preferred_element_type=jnp.float32
        ).astype(jnp.bfloat16)
        normed = extended_normed[HALF : HALF + tok_rows]
        queries = (
            jnp.dot(normed, weights[:, :feat_width], preferred_element_type=jnp.float32) * 0.125
        ).astype(jnp.bfloat16)
        prompt_kv = jnp.dot(
            layer_norm(prompt_rows, gain),
            weights[:, feat_width:],
            preferred_element_type=jnp.float32,
        ).astype(jnp.bfloat16)
        parts = []
        for row0 in (0, half_rows):
            attended = attention(
                queries, band_kv, prompt_kv, first_pos, total_len, row0, half_rows
            )
            projection = jnp.dot(
                attended, w_out[layer_idx], preferred_element_type=jnp.float32
            )
            rows_in = hidden_state[row0 : row0 + half_rows].astype(jnp.float32)
            parts.append((rows_in + projection).astype(jnp.bfloat16))
        hidden_state = jnp.concatenate(parts, axis=0)
        if half_rows >= PROMPT:
            prompt_source = parts[0][:PROMPT]
        else:
            prompt_source = hidden_state[:PROMPT]
    final = layer_norm(hidden_state, final_gain)
    head_out = jnp.dot(final, w_heads, preferred_element_type=jnp.float32)
    logits = head_out[:, :ACTIONS]
    reward_table = head_out[:, ACTIONS:]
    logit_max = jnp.max(logits, axis=-1, keepdims=True)
    exps = jnp.exp(logits - logit_max)
    policy = exps / jnp.sum(exps, axis=-1, keepdims=True)
    chosen = actions[:, None] == jnp.arange(ACTIONS, dtype=jnp.int32)[None, :]
    rewards = jnp.sum(jnp.where(chosen, reward_table, 0.0), axis=-1)
    chosen_prob = jnp.sum(jnp.where(chosen, policy, 0.0), axis=-1)
    direct = jnp.sum(policy * reward_table, axis=-1)
    logged_prob = propensity.astype(jnp.float32) / 65536.0
    cutoff = 0.5 * switch_index[0].astype(jnp.float32)
    dr_terms = direct + jnp.minimum(chosen_prob / logged_prob, cutoff) * (logged_reward - rewards)
    return (rewards, dr_terms)


def solution(mesh):
    placed = (
        P(("groups", "seq"), None),
        P(),
        P(),
        P(),
        P(),
        P(),
        P(("groups", "seq")),
        P(("groups", "seq")),
        P(("groups", "seq")),
        P("groups"),
    )
    return jax.shard_map(
        per_device,
        mesh=mesh,
        in_specs=placed,
        out_specs=(P(("groups", "seq")), P(("groups", "seq"))),
        check_vma=False,
    )
```

```python
import functools

import jax
import jax.numpy as jnp
from jax import lax
from jax.experimental import pallas as pl
from jax.experimental.pallas import tpu as pltpu
from jax.sharding import PartitionSpec as P

HEADS = 12
HEAD = 64
HALF = 256
PROMPT = 256
ACTIONS = 256
LAYERS = 2


def with_halo(array, sides, width):
    for axis, dim in sides:
        count, length = (lax.axis_size(axis), array.shape[dim])
        up = [(i, (i + 1) % count) for i in range(count - 1)]
        down = [(j, i) for i, j in up]
        last = lax.slice_in_dim(array, length - width, length, axis=dim)
        leading = lax.slice_in_dim(array, 0, width, axis=dim)
        before = lax.ppermute(last, axis, up)
        after = lax.ppermute(leading, axis, down)
        array = jnp.concatenate([before, array, after], axis=dim)
    return array


def tree_rounds(count):
    if count & (count - 1) == 0:
        bits = []
        step = count // 2
        while step:
            bits.append(step)
            step //= 2
        return [[[(i, i + bit) for i in range(0, count, 2 * bit)]] for bit in bits]
    rounds = []
    held = 1
    while held < count:
        rounds.append([[(i, i + held) for i in range(min(held, count - held))]])
        held *= 2
    return rounds


def spread(block, axis):
    place = lax.axis_index(axis)
    block = jnp.where(place == 0, block, jnp.zeros_like(block))
    for ops in tree_rounds(lax.axis_size(axis)):
        received = block
        for op in ops:
            got = lax.ppermute(block, axis, op)
            targets = jnp.array([t for _, t in op], dtype=jnp.int32)
            received = jnp.where(jnp.any(place == targets), got, received)
        block = received
    return block


def layer_norm(hidden_state, gain_row):
    values_f = hidden_state.astype(jnp.float32)
    row_mean = jnp.mean(values_f, axis=-1, keepdims=True)
    centred = values_f - row_mean
    row_var = jnp.mean(centred * centred, axis=-1, keepdims=True)
    return (centred * lax.rsqrt(row_var + 1e-05) * gain_row).astype(jnp.bfloat16)


QUERY_TILE = 256
GROUP = 4


def attention_kernel(row0, pos_ref, q_ref, *refs):
    band_refs = refs[:-2]
    prompt_ref, out_ref = refs[-2:]
    tile = q_ref.shape[0]
    width = tile * len(band_refs)
    feat = q_ref.shape[1]
    lanes = GROUP * HEAD
    block = pl.program_id(0)
    first = pos_ref[0]
    total = pos_ref[1]
    row_in_tile = lax.broadcasted_iota(jnp.int32, (GROUP * tile, 1), 0) % tile
    query_pos = first + row0 + block * tile + row_in_tile
    key_pos = first + row0 + block * tile - HALF + lax.broadcasted_iota(jnp.int32, (1, width), 1)
    gap = key_pos - query_pos
    band_ok = (gap >= -HALF) & (gap <= HALF) & (key_pos >= 0) & (key_pos < total)
    prompt_pos = lax.broadcasted_iota(jnp.int32, (1, PROMPT), 1)
    prompt_ok = jnp.abs(prompt_pos - query_pos) > HALF
    contract = (((1,), (1,)), ((), ()))
    lane_head = lax.broadcasted_iota(jnp.int32, (1, lanes), 1) // HEAD
    for group in range(feat // lanes):
        cols = slice(group * lanes, (group + 1) * lanes)
        vcols = slice(feat + group * lanes, feat + (group + 1) * lanes)
        band_keys = jnp.concatenate([ref[:, cols] for ref in band_refs], axis=0)
        band_values = jnp.concatenate([ref[:, vcols] for ref in band_refs], axis=0)
        query = q_ref[:, cols]
        stacked = jnp.concatenate(
            [jnp.where(lane_head == j, query, jnp.zeros_like(query)) for j in range(GROUP)],
            axis=0,
        )
        band_scores = lax.dot_general(
            stacked, band_keys, contract, preferred_element_type=jnp.float32
        )
        prompt_scores = lax.dot_general(
            stacked, prompt_ref[:, cols], contract, preferred_element_type=jnp.float32
        )
        band_scores = jnp.where(band_ok, band_scores, -1e30)
        prompt_scores = jnp.where(prompt_ok, prompt_scores, -1e30)
        row_max = jnp.maximum(
            jnp.max(band_scores, axis=1, keepdims=True),
            jnp.max(prompt_scores, axis=1, keepdims=True),
        )
        band_exp = jnp.exp(band_scores - row_max)
        prompt_exp = jnp.exp(prompt_scores - row_max)
        denom = jnp.sum(band_exp, axis=1, keepdims=True) + jnp.sum(
            prompt_exp, axis=1, keepdims=True
        )
        scale = 1.0 / denom
        band_probs = (band_exp * scale).astype(jnp.bfloat16)
        prompt_probs = (prompt_exp * scale).astype(jnp.bfloat16)
        mixed = jnp.dot(band_probs, band_values, preferred_element_type=jnp.float32) + jnp.dot(
            prompt_probs, prompt_ref[:, vcols], preferred_element_type=jnp.float32
        )
        attn = mixed[:tile]
        for j in range(1, GROUP):
            attn = jnp.where(lane_head == j, mixed[j * tile : (j + 1) * tile], attn)
        out_ref[:, cols] = attn.astype(out_ref.dtype)


def attention(queries, band_kv, prompt_kv, first_pos, total_len, row0, count):
    feat = queries.shape[1]
    tile = min(QUERY_TILE, count)
    pos = jnp.stack([first_pos, total_len]).astype(jnp.int32)
    pieces = 1 + 2 * HALF // tile
    width = tile * pieces
    flops = 4 * count * (width + PROMPT) * feat * GROUP
    skip = row0 // tile
    band_specs = [
        pl.BlockSpec((tile, band_kv.shape[1]), lambda b, p, k=k: (b + skip + k, 0))
        for k in range(pieces)
    ]
    return pl.pallas_call(
        functools.partial(attention_kernel, row0),
        out_shape=jax.ShapeDtypeStruct((count, feat), jnp.bfloat16),
        grid_spec=pltpu.PrefetchScalarGridSpec(
            num_scalar_prefetch=1,
            grid=(count // tile,),
            in_specs=[pl.BlockSpec((tile, feat), lambda b, p: (b + skip, 0))]
            + band_specs
            + [pl.BlockSpec(prompt_kv.shape, lambda b, p: (0, 0))],
            out_specs=pl.BlockSpec((tile, feat), lambda b, p: (b, 0)),
        ),
        cost_estimate=pl.CostEstimate(
            flops=flops,
            transcendentals=count * (width + PROMPT) * HEADS,
            bytes_accessed=2 * (2 * count * feat + pieces * count * band_kv.shape[1] + prompt_kv.size),
        ),
    )(pos, queries, *([band_kv] * pieces), prompt_kv)


def per_device(
    hidden_in,
    ln_gain,
    w_qkv,
    w_out,
    final_gain,
    w_heads,
    actions,
    propensity,
    logged_reward,
    switch_index,
):
    tok_rows = hidden_in.shape[0]
    feat_width = hidden_in.shape[1]
    seq_devices = lax.axis_size("seq")
    seq_place = lax.axis_index("seq")
    total_len = tok_rows * seq_devices
    first_pos = seq_place * tok_rows
    hidden_state = hidden_in
    prompt_source = hidden_in[:PROMPT]
    for layer_idx in range(LAYERS):
        gain = ln_gain[layer_idx]
        weights = w_qkv[layer_idx]
        extended = with_halo(hidden_state, (("seq", 0),), HALF)
        prompt_rows = spread(prompt_source, "seq")
        extended_normed = layer_norm(extended, gain)
        band_kv = jnp.dot(
            extended_normed, weights[:, feat_width:], preferred_element_type=jnp.float32
        ).astype(jnp.bfloat16)
        normed = extended_normed[HALF : HALF + tok_rows]
        queries = (
            jnp.dot(normed, weights[:, :feat_width], preferred_element_type=jnp.float32) * 0.125
        ).astype(jnp.bfloat16)
        prompt_kv = jnp.dot(
            layer_norm(prompt_rows, gain),
            weights[:, feat_width:],
            preferred_element_type=jnp.float32,
        ).astype(jnp.bfloat16)
        attended = attention(queries, band_kv, prompt_kv, first_pos, total_len, 0, tok_rows)
        projection = jnp.dot(attended, w_out[layer_idx], preferred_element_type=jnp.float32)
        hidden_state = (hidden_state.astype(jnp.float32) + projection).astype(jnp.bfloat16)
        prompt_source = hidden_state[:PROMPT]
    final = layer_norm(hidden_state, final_gain)
    head_out = jnp.dot(final, w_heads, preferred_element_type=jnp.float32)
    logits = head_out[:, :ACTIONS]
    reward_table = head_out[:, ACTIONS:]
    logit_max = jnp.max(logits, axis=-1, keepdims=True)
    exps = jnp.exp(logits - logit_max)
    policy = exps / jnp.sum(exps, axis=-1, keepdims=True)
    chosen = actions[:, None] == jnp.arange(ACTIONS, dtype=jnp.int32)[None, :]
    rewards = jnp.sum(jnp.where(chosen, reward_table, 0.0), axis=-1)
    chosen_prob = jnp.sum(jnp.where(chosen, policy, 0.0), axis=-1)
    direct = jnp.sum(policy * reward_table, axis=-1)
    logged_prob = propensity.astype(jnp.float32) / 65536.0
    cutoff = 0.5 * switch_index[0].astype(jnp.float32)
    dr_terms = direct + jnp.minimum(chosen_prob / logged_prob, cutoff) * (logged_reward - rewards)
    return (rewards, dr_terms)


def solution(mesh):
    placed = (
        P(("groups", "seq"), None),
        P(),
        P(),
        P(),
        P(),
        P(),
        P(("groups", "seq")),
        P(("groups", "seq")),
        P(("groups", "seq")),
        P("groups"),
    )
    return jax.shard_map(
        per_device,
        mesh=mesh,
        in_specs=placed,
        out_specs=(P(("groups", "seq")), P(("groups", "seq"))),
        check_vma=False,
    )
```

```python
import functools

import jax
import jax.numpy as jnp
from jax import lax
from jax.experimental import pallas as pl
from jax.experimental.pallas import tpu as pltpu
from jax.sharding import PartitionSpec as P

HEADS = 12
HEAD = 64
HALF = 256
PROMPT = 256
ACTIONS = 256
LAYERS = 2


def with_halo(array, sides, width):
    for axis, dim in sides:
        count, length = (lax.axis_size(axis), array.shape[dim])
        up = [(i, (i + 1) % count) for i in range(count - 1)]
        down = [(j, i) for i, j in up]
        last = lax.slice_in_dim(array, length - width, length, axis=dim)
        leading = lax.slice_in_dim(array, 0, width, axis=dim)
        before = lax.ppermute(last, axis, up)
        after = lax.ppermute(leading, axis, down)
        array = jnp.concatenate([before, array, after], axis=dim)
    return array


def tree_rounds(count):
    if count & (count - 1) == 0:
        bits = []
        step = count // 2
        while step:
            bits.append(step)
            step //= 2
        return [[[(i, i + bit) for i in range(0, count, 2 * bit)]] for bit in bits]
    rounds = []
    held = 1
    while held < count:
        rounds.append([[(i, i + held) for i in range(min(held, count - held))]])
        held *= 2
    return rounds


def spread(block, axis):
    place = lax.axis_index(axis)
    block = jnp.where(place == 0, block, jnp.zeros_like(block))
    for ops in tree_rounds(lax.axis_size(axis)):
        received = block
        for op in ops:
            got = lax.ppermute(block, axis, op)
            targets = jnp.array([t for _, t in op], dtype=jnp.int32)
            received = jnp.where(jnp.any(place == targets), got, received)
        block = received
    return block


def layer_norm(hidden_state, gain_row):
    values_f = hidden_state.astype(jnp.float32)
    row_mean = jnp.mean(values_f, axis=-1, keepdims=True)
    centred = values_f - row_mean
    row_var = jnp.mean(centred * centred, axis=-1, keepdims=True)
    return (centred * lax.rsqrt(row_var + 1e-05) * gain_row).astype(jnp.bfloat16)


QUERY_TILE = 256
GROUP = 4


def attention_kernel(row0, pos_ref, q_ref, *refs):
    band_refs = refs[:-2]
    prompt_ref, out_ref = refs[-2:]
    tile = q_ref.shape[0]
    width = tile * len(band_refs)
    feat = q_ref.shape[1]
    lanes = GROUP * HEAD
    block = pl.program_id(0)
    first = pos_ref[0]
    total = pos_ref[1]
    row_in_tile = lax.broadcasted_iota(jnp.int32, (GROUP * tile, 1), 0) % tile
    query_pos = first + row0 + block * tile + row_in_tile
    key_pos = first + row0 + block * tile - HALF + lax.broadcasted_iota(jnp.int32, (1, width), 1)
    gap = key_pos - query_pos
    band_ok = (gap >= -HALF) & (gap <= HALF) & (key_pos >= 0) & (key_pos < total)
    prompt_pos = lax.broadcasted_iota(jnp.int32, (1, PROMPT), 1)
    prompt_ok = jnp.abs(prompt_pos - query_pos) > HALF
    contract = (((1,), (1,)), ((), ()))
    lane_head = lax.broadcasted_iota(jnp.int32, (1, lanes), 1) // HEAD
    for group in range(feat // lanes):
        cols = slice(group * lanes, (group + 1) * lanes)
        vcols = slice(feat + group * lanes, feat + (group + 1) * lanes)
        band_keys = jnp.concatenate([ref[:, cols] for ref in band_refs], axis=0)
        band_values = jnp.concatenate([ref[:, vcols] for ref in band_refs], axis=0)
        query = q_ref[:, cols]
        stacked = jnp.concatenate(
            [jnp.where(lane_head == j, query, jnp.zeros_like(query)) for j in range(GROUP)],
            axis=0,
        )
        band_scores = lax.dot_general(
            stacked, band_keys, contract, preferred_element_type=jnp.float32
        )
        prompt_scores = lax.dot_general(
            stacked, prompt_ref[:, cols], contract, preferred_element_type=jnp.float32
        )
        band_scores = jnp.where(band_ok, band_scores, -1e30)
        prompt_scores = jnp.where(prompt_ok, prompt_scores, -1e30)
        row_max = jnp.maximum(
            jnp.max(band_scores, axis=1, keepdims=True),
            jnp.max(prompt_scores, axis=1, keepdims=True),
        )
        band_exp = jnp.exp(band_scores - row_max)
        prompt_exp = jnp.exp(prompt_scores - row_max)
        denom = jnp.sum(band_exp, axis=1, keepdims=True) + jnp.sum(
            prompt_exp, axis=1, keepdims=True
        )
        scale = 1.0 / denom
        band_probs = (band_exp * scale).astype(jnp.bfloat16)
        prompt_probs = (prompt_exp * scale).astype(jnp.bfloat16)
        mixed = jnp.dot(band_probs, band_values, preferred_element_type=jnp.float32) + jnp.dot(
            prompt_probs, prompt_ref[:, vcols], preferred_element_type=jnp.float32
        )
        attn = mixed[:tile]
        for j in range(1, GROUP):
            attn = jnp.where(lane_head == j, mixed[j * tile : (j + 1) * tile], attn)
        out_ref[:, cols] = attn.astype(out_ref.dtype)


def attention(queries, band_kv, prompt_kv, first_pos, total_len, row0, count):
    feat = queries.shape[1]
    tile = min(QUERY_TILE, count)
    pos = jnp.stack([first_pos, total_len]).astype(jnp.int32)
    pieces = 1 + 2 * HALF // tile
    width = tile * pieces
    flops = 4 * count * (width + PROMPT) * feat * GROUP
    skip = row0 // tile
    band_specs = [
        pl.BlockSpec((tile, band_kv.shape[1]), lambda b, p, k=k: (b + skip + k, 0))
        for k in range(pieces)
    ]
    return pl.pallas_call(
        functools.partial(attention_kernel, row0),
        out_shape=jax.ShapeDtypeStruct((count, feat), jnp.bfloat16),
        grid_spec=pltpu.PrefetchScalarGridSpec(
            num_scalar_prefetch=1,
            grid=(count // tile,),
            in_specs=[pl.BlockSpec((tile, feat), lambda b, p: (b + skip, 0))]
            + band_specs
            + [pl.BlockSpec(prompt_kv.shape, lambda b, p: (0, 0))],
            out_specs=pl.BlockSpec((tile, feat), lambda b, p: (b, 0)),
        ),
        cost_estimate=pl.CostEstimate(
            flops=flops,
            transcendentals=count * (width + PROMPT) * HEADS,
            bytes_accessed=2 * (2 * count * feat + pieces * count * band_kv.shape[1] + prompt_kv.size),
        ),
    )(pos, queries, *([band_kv] * pieces), prompt_kv)


PROJ_COLS = 256


def projection_kernel(scale, x_ref, w_ref, out_ref):
    product = jnp.dot(x_ref[...], w_ref[...], preferred_element_type=jnp.float32)
    if scale != 1.0:
        product = product * scale
    out_ref[...] = product.astype(out_ref.dtype)


def project(rows, weights, layer, col0, cols, scale):
    count, depth = rows.shape
    first_block = col0 // PROJ_COLS
    return pl.pallas_call(
        functools.partial(projection_kernel, scale),
        out_shape=jax.ShapeDtypeStruct((count, cols), jnp.bfloat16),
        grid=(cols // PROJ_COLS,),
        in_specs=[
            pl.BlockSpec((count, depth), lambda j: (0, 0)),
            pl.BlockSpec((None, depth, PROJ_COLS), lambda j: (layer, 0, j + first_block)),
        ],
        out_specs=pl.BlockSpec((count, PROJ_COLS), lambda j: (0, j)),
        cost_estimate=pl.CostEstimate(
            flops=2 * count * depth * cols,
            transcendentals=0,
            bytes_accessed=2 * (count * depth + depth * cols + count * cols),
        ),
    )(rows, weights)


def per_device(
    hidden_in,
    ln_gain,
    w_qkv,
    w_out,
    final_gain,
    w_heads,
    actions,
    propensity,
    logged_reward,
    switch_index,
):
    tok_rows = hidden_in.shape[0]
    feat_width = hidden_in.shape[1]
    seq_devices = lax.axis_size("seq")
    seq_place = lax.axis_index("seq")
    total_len = tok_rows * seq_devices
    first_pos = seq_place * tok_rows
    hidden_state = hidden_in
    prompt_source = hidden_in[:PROMPT]
    for layer_idx in range(LAYERS):
        gain = ln_gain[layer_idx]
        extended = with_halo(hidden_state, (("seq", 0),), HALF)
        prompt_rows = spread(prompt_source, "seq")
        extended_normed = layer_norm(extended, gain)
        band_kv = project(extended_normed, w_qkv, layer_idx, feat_width, 2 * feat_width, 1.0)
        normed = extended_normed[HALF : HALF + tok_rows]
        queries = project(normed, w_qkv, layer_idx, 0, feat_width, 0.125)
        prompt_kv = project(
            layer_norm(prompt_rows, gain), w_qkv, layer_idx, feat_width, 2 * feat_width, 1.0
        )
        attended = attention(queries, band_kv, prompt_kv, first_pos, total_len, 0, tok_rows)
        projection = jnp.dot(attended, w_out[layer_idx], preferred_element_type=jnp.float32)
        hidden_state = (hidden_state.astype(jnp.float32) + projection).astype(jnp.bfloat16)
        prompt_source = hidden_state[:PROMPT]
    final = layer_norm(hidden_state, final_gain)
    head_out = jnp.dot(final, w_heads, preferred_element_type=jnp.float32)
    logits = head_out[:, :ACTIONS]
    reward_table = head_out[:, ACTIONS:]
    logit_max = jnp.max(logits, axis=-1, keepdims=True)
    exps = jnp.exp(logits - logit_max)
    policy = exps / jnp.sum(exps, axis=-1, keepdims=True)
    chosen = actions[:, None] == jnp.arange(ACTIONS, dtype=jnp.int32)[None, :]
    rewards = jnp.sum(jnp.where(chosen, reward_table, 0.0), axis=-1)
    chosen_prob = jnp.sum(jnp.where(chosen, policy, 0.0), axis=-1)
    direct = jnp.sum(policy * reward_table, axis=-1)
    logged_prob = propensity.astype(jnp.float32) / 65536.0
    cutoff = 0.5 * switch_index[0].astype(jnp.float32)
    dr_terms = direct + jnp.minimum(chosen_prob / logged_prob, cutoff) * (logged_reward - rewards)
    return (rewards, dr_terms)


def solution(mesh):
    placed = (
        P(("groups", "seq"), None),
        P(),
        P(),
        P(),
        P(),
        P(),
        P(("groups", "seq")),
        P(("groups", "seq")),
        P(("groups", "seq")),
        P("groups"),
    )
    return jax.shard_map(
        per_device,
        mesh=mesh,
        in_specs=placed,
        out_specs=(P(("groups", "seq")), P(("groups", "seq"))),
        check_vma=False,
    )
```

```python
import functools

import jax
import jax.numpy as jnp
from jax import lax
from jax.experimental import pallas as pl
from jax.experimental.pallas import tpu as pltpu
from jax.sharding import PartitionSpec as P

HEADS = 12
HEAD = 64
HALF = 256
PROMPT = 256
ACTIONS = 256
LAYERS = 2


def with_halo(array, sides, width):
    for axis, dim in sides:
        count, length = (lax.axis_size(axis), array.shape[dim])
        up = [(i, (i + 1) % count) for i in range(count - 1)]
        down = [(j, i) for i, j in up]
        last = lax.slice_in_dim(array, length - width, length, axis=dim)
        leading = lax.slice_in_dim(array, 0, width, axis=dim)
        before = lax.ppermute(last, axis, up)
        after = lax.ppermute(leading, axis, down)
        array = jnp.concatenate([before, array, after], axis=dim)
    return array


def tree_rounds(count):
    if count & (count - 1) == 0:
        bits = []
        step = count // 2
        while step:
            bits.append(step)
            step //= 2
        return [[[(i, i + bit) for i in range(0, count, 2 * bit)]] for bit in bits]
    rounds = []
    held = 1
    while held < count:
        rounds.append([[(i, i + held) for i in range(min(held, count - held))]])
        held *= 2
    return rounds


def spread(block, axis):
    place = lax.axis_index(axis)
    block = jnp.where(place == 0, block, jnp.zeros_like(block))
    for ops in tree_rounds(lax.axis_size(axis)):
        received = block
        for op in ops:
            got = lax.ppermute(block, axis, op)
            targets = jnp.array([t for _, t in op], dtype=jnp.int32)
            received = jnp.where(jnp.any(place == targets), got, received)
        block = received
    return block


def layer_norm(hidden_state, gain_row):
    values_f = hidden_state.astype(jnp.float32)
    row_mean = jnp.mean(values_f, axis=-1, keepdims=True)
    centred = values_f - row_mean
    row_var = jnp.mean(centred * centred, axis=-1, keepdims=True)
    return (centred * lax.rsqrt(row_var + 1e-05) * gain_row).astype(jnp.bfloat16)


QUERY_TILE = 256
GROUP = 4


def attention_kernel(row0, pos_ref, q_ref, *refs):
    band_refs = refs[:-2]
    prompt_ref, out_ref = refs[-2:]
    tile = q_ref.shape[0]
    width = tile * len(band_refs)
    feat = q_ref.shape[1]
    lanes = GROUP * HEAD
    block = pl.program_id(0)
    first = pos_ref[0]
    total = pos_ref[1]
    query_pos = first + row0 + block * tile + lax.broadcasted_iota(jnp.int32, (tile, 1), 0)
    key_pos = first + row0 + block * tile - HALF + lax.broadcasted_iota(jnp.int32, (1, width), 1)
    gap = key_pos - query_pos
    band_ok = (gap >= -HALF) & (gap <= HALF) & (key_pos >= 0) & (key_pos < total)
    prompt_pos = lax.broadcasted_iota(jnp.int32, (1, PROMPT), 1)
    prompt_ok = jnp.abs(prompt_pos - query_pos) > HALF
    contract = (((1,), (1,)), ((), ()))
    lane_head = lax.broadcasted_iota(jnp.int32, (1, lanes), 1) // HEAD
    for group in range(feat // lanes):
        cols = slice(group * lanes, (group + 1) * lanes)
        vcols = slice(feat + group * lanes, feat + (group + 1) * lanes)
        band_keys = jnp.concatenate([ref[:, cols] for ref in band_refs], axis=0)
        band_values = jnp.concatenate([ref[:, vcols] for ref in band_refs], axis=0)
        query = q_ref[:, cols]
        stacked = jnp.concatenate(
            [jnp.where(lane_head == j, query, jnp.zeros_like(query)) for j in range(GROUP)],
            axis=0,
        )
        band_scores = lax.dot_general(
            stacked, band_keys, contract, preferred_element_type=jnp.float32
        ).reshape(GROUP, tile, width)
        prompt_scores = lax.dot_general(
            stacked, prompt_ref[:, cols], contract, preferred_element_type=jnp.float32
        ).reshape(GROUP, tile, PROMPT)
        band_scores = jnp.where(band_ok[None], band_scores, -1e30)
        prompt_scores = jnp.where(prompt_ok[None], prompt_scores, -1e30)
        row_max = jnp.maximum(
            jnp.max(band_scores, axis=2, keepdims=True),
            jnp.max(prompt_scores, axis=2, keepdims=True),
        )
        band_exp = jnp.exp(band_scores - row_max)
        prompt_exp = jnp.exp(prompt_scores - row_max)
        denom = jnp.sum(band_exp, axis=2, keepdims=True) + jnp.sum(
            prompt_exp, axis=2, keepdims=True
        )
        band_probs = band_exp.astype(jnp.bfloat16).reshape(GROUP * tile, width)
        prompt_probs = prompt_exp.astype(jnp.bfloat16).reshape(GROUP * tile, PROMPT)
        mixed = jnp.dot(band_probs, band_values, preferred_element_type=jnp.float32) + jnp.dot(
            prompt_probs, prompt_ref[:, vcols], preferred_element_type=jnp.float32
        )
        mixed = mixed * (1.0 / denom.reshape(GROUP * tile, 1))
        attn = mixed[:tile]
        for j in range(1, GROUP):
            attn = jnp.where(lane_head == j, mixed[j * tile : (j + 1) * tile], attn)
        out_ref[:, cols] = attn.astype(out_ref.dtype)


def attention(queries, band_kv, prompt_kv, first_pos, total_len, row0, count):
    feat = queries.shape[1]
    tile = min(QUERY_TILE, count)
    pos = jnp.stack([first_pos, total_len]).astype(jnp.int32)
    pieces = 1 + 2 * HALF // tile
    width = tile * pieces
    flops = 4 * count * (width + PROMPT) * feat * GROUP
    skip = row0 // tile
    band_specs = [
        pl.BlockSpec((tile, band_kv.shape[1]), lambda b, p, k=k: (b + skip + k, 0))
        for k in range(pieces)
    ]
    return pl.pallas_call(
        functools.partial(attention_kernel, row0),
        out_shape=jax.ShapeDtypeStruct((count, feat), jnp.bfloat16),
        grid_spec=pltpu.PrefetchScalarGridSpec(
            num_scalar_prefetch=1,
            grid=(count // tile,),
            in_specs=[pl.BlockSpec((tile, feat), lambda b, p: (b + skip, 0))]
            + band_specs
            + [pl.BlockSpec(prompt_kv.shape, lambda b, p: (0, 0))],
            out_specs=pl.BlockSpec((tile, feat), lambda b, p: (b, 0)),
        ),
        cost_estimate=pl.CostEstimate(
            flops=flops,
            transcendentals=count * (width + PROMPT) * HEADS,
            bytes_accessed=2 * (2 * count * feat + pieces * count * band_kv.shape[1] + prompt_kv.size),
        ),
    )(pos, queries, *([band_kv] * pieces), prompt_kv)


def per_device(
    hidden_in,
    ln_gain,
    w_qkv,
    w_out,
    final_gain,
    w_heads,
    actions,
    propensity,
    logged_reward,
    switch_index,
):
    tok_rows = hidden_in.shape[0]
    feat_width = hidden_in.shape[1]
    seq_devices = lax.axis_size("seq")
    seq_place = lax.axis_index("seq")
    total_len = tok_rows * seq_devices
    first_pos = seq_place * tok_rows
    hidden_state = hidden_in
    prompt_source = hidden_in[:PROMPT]
    for layer_idx in range(LAYERS):
        gain = ln_gain[layer_idx]
        weights = w_qkv[layer_idx]
        extended = with_halo(hidden_state, (("seq", 0),), HALF)
        prompt_rows = spread(prompt_source, "seq")
        extended_normed = layer_norm(extended, gain)
        band_kv = jnp.dot(
            extended_normed, weights[:, feat_width:], preferred_element_type=jnp.float32
        ).astype(jnp.bfloat16)
        normed = extended_normed[HALF : HALF + tok_rows]
        queries = (
            jnp.dot(normed, weights[:, :feat_width], preferred_element_type=jnp.float32) * 0.125
        ).astype(jnp.bfloat16)
        prompt_kv = jnp.dot(
            layer_norm(prompt_rows, gain),
            weights[:, feat_width:],
            preferred_element_type=jnp.float32,
        ).astype(jnp.bfloat16)
        attended = attention(queries, band_kv, prompt_kv, first_pos, total_len, 0, tok_rows)
        projection = jnp.dot(attended, w_out[layer_idx], preferred_element_type=jnp.float32)
        hidden_state = (hidden_state.astype(jnp.float32) + projection).astype(jnp.bfloat16)
        prompt_source = hidden_state[:PROMPT]
    final = layer_norm(hidden_state, final_gain)
    head_out = jnp.dot(final, w_heads, preferred_element_type=jnp.float32)
    logits = head_out[:, :ACTIONS]
    reward_table = head_out[:, ACTIONS:]
    logit_max = jnp.max(logits, axis=-1, keepdims=True)
    exps = jnp.exp(logits - logit_max)
    policy = exps / jnp.sum(exps, axis=-1, keepdims=True)
    chosen = actions[:, None] == jnp.arange(ACTIONS, dtype=jnp.int32)[None, :]
    rewards = jnp.sum(jnp.where(chosen, reward_table, 0.0), axis=-1)
    chosen_prob = jnp.sum(jnp.where(chosen, policy, 0.0), axis=-1)
    direct = jnp.sum(policy * reward_table, axis=-1)
    logged_prob = propensity.astype(jnp.float32) / 65536.0
    cutoff = 0.5 * switch_index[0].astype(jnp.float32)
    dr_terms = direct + jnp.minimum(chosen_prob / logged_prob, cutoff) * (logged_reward - rewards)
    return (rewards, dr_terms)


def solution(mesh):
    placed = (
        P(("groups", "seq"), None),
        P(),
        P(),
        P(),
        P(),
        P(),
        P(("groups", "seq")),
        P(("groups", "seq")),
        P(("groups", "seq")),
        P("groups"),
    )
    return jax.shard_map(
        per_device,
        mesh=mesh,
        in_specs=placed,
        out_specs=(P(("groups", "seq")), P(("groups", "seq"))),
        check_vma=False,
    )
```

```python
import functools

import jax
import jax.numpy as jnp
from jax import lax
from jax.experimental import pallas as pl
from jax.experimental.pallas import tpu as pltpu
from jax.sharding import PartitionSpec as P

HEADS = 12
HEAD = 64
HALF = 256
PROMPT = 256
ACTIONS = 256
LAYERS = 2


def with_halo(array, sides, width):
    for axis, dim in sides:
        count, length = (lax.axis_size(axis), array.shape[dim])
        up = [(i, (i + 1) % count) for i in range(count - 1)]
        down = [(j, i) for i, j in up]
        last = lax.slice_in_dim(array, length - width, length, axis=dim)
        leading = lax.slice_in_dim(array, 0, width, axis=dim)
        before = lax.ppermute(last, axis, up)
        after = lax.ppermute(leading, axis, down)
        array = jnp.concatenate([before, array, after], axis=dim)
    return array


def tree_rounds(count):
    if count & (count - 1) == 0:
        bits = []
        step = count // 2
        while step:
            bits.append(step)
            step //= 2
        return [[[(i, i + bit) for i in range(0, count, 2 * bit)]] for bit in bits]
    rounds = []
    held = 1
    while held < count:
        rounds.append([[(i, i + held) for i in range(min(held, count - held))]])
        held *= 2
    return rounds


def spread(block, axis):
    place = lax.axis_index(axis)
    block = jnp.where(place == 0, block, jnp.zeros_like(block))
    for ops in tree_rounds(lax.axis_size(axis)):
        received = block
        for op in ops:
            got = lax.ppermute(block, axis, op)
            targets = jnp.array([t for _, t in op], dtype=jnp.int32)
            received = jnp.where(jnp.any(place == targets), got, received)
        block = received
    return block


def layer_norm(hidden_state, gain_row):
    values_f = hidden_state.astype(jnp.float32)
    row_mean = jnp.mean(values_f, axis=-1, keepdims=True)
    centred = values_f - row_mean
    row_var = jnp.mean(centred * centred, axis=-1, keepdims=True)
    return (centred * lax.rsqrt(row_var + 1e-05) * gain_row).astype(jnp.bfloat16)


QUERY_TILE = 256
GROUP = 4


def attention_kernel(row0, pos_ref, q_ref, *refs):
    band_refs = refs[:-2]
    prompt_ref, out_ref = refs[-2:]
    tile = q_ref.shape[0]
    width = tile * len(band_refs)
    feat = q_ref.shape[1]
    lanes = GROUP * HEAD
    block = pl.program_id(0)
    first = pos_ref[0]
    total = pos_ref[1]
    query_pos = first + row0 + block * tile + lax.broadcasted_iota(jnp.int32, (tile, 1), 0)
    key_pos = first + row0 + block * tile - HALF + lax.broadcasted_iota(jnp.int32, (1, width), 1)
    gap = key_pos - query_pos
    band_ok = (gap >= -HALF) & (gap <= HALF) & (key_pos >= 0) & (key_pos < total)
    prompt_pos = lax.broadcasted_iota(jnp.int32, (1, PROMPT), 1)
    prompt_ok = jnp.abs(prompt_pos - query_pos) > HALF
    contract = (((1,), (1,)), ((), ()))
    lane_head = lax.broadcasted_iota(jnp.int32, (1, lanes), 1) // HEAD
    for group in range(feat // lanes):
        cols = slice(group * lanes, (group + 1) * lanes)
        vcols = slice(feat + group * lanes, feat + (group + 1) * lanes)
        band_keys = jnp.concatenate([ref[:, cols] for ref in band_refs], axis=0)
        band_values = jnp.concatenate([ref[:, vcols] for ref in band_refs], axis=0)
        query = q_ref[:, cols]
        stacked = jnp.concatenate(
            [jnp.where(lane_head == j, query, jnp.zeros_like(query)) for j in range(GROUP)],
            axis=0,
        )
        band_scores = lax.dot_general(
            stacked, band_keys, contract, preferred_element_type=jnp.float32
        ).reshape(GROUP, tile, width)
        prompt_scores = lax.dot_general(
            stacked, prompt_ref[:, cols], contract, preferred_element_type=jnp.float32
        ).reshape(GROUP, tile, PROMPT)
        band_scores = jnp.where(band_ok[None], band_scores, -1e30)
        prompt_scores = jnp.where(prompt_ok[None], prompt_scores, -1e30)
        row_max = jnp.maximum(
            jnp.max(band_scores, axis=2, keepdims=True),
            jnp.max(prompt_scores, axis=2, keepdims=True),
        )
        band_exp = jnp.exp(band_scores - row_max)
        prompt_exp = jnp.exp(prompt_scores - row_max)
        denom = jnp.sum(band_exp, axis=2, keepdims=True) + jnp.sum(
            prompt_exp, axis=2, keepdims=True
        )
        band_probs = band_exp.astype(jnp.bfloat16).reshape(GROUP * tile, width)
        prompt_probs = prompt_exp.astype(jnp.bfloat16).reshape(GROUP * tile, PROMPT)
        mixed = jnp.dot(band_probs, band_values, preferred_element_type=jnp.float32) + jnp.dot(
            prompt_probs, prompt_ref[:, vcols], preferred_element_type=jnp.float32
        )
        mixed = mixed * (1.0 / denom.reshape(GROUP * tile, 1))
        attn = mixed[:tile]
        for j in range(1, GROUP):
            attn = jnp.where(lane_head == j, mixed[j * tile : (j + 1) * tile], attn)
        out_ref[:, cols] = attn.astype(out_ref.dtype)


def attention(queries, band_kv, prompt_kv, first_pos, total_len, row0, count):
    feat = queries.shape[1]
    tile = min(QUERY_TILE, count)
    pos = jnp.stack([first_pos, total_len]).astype(jnp.int32)
    pieces = 1 + 2 * HALF // tile
    width = tile * pieces
    flops = 4 * count * (width + PROMPT) * feat * GROUP
    skip = row0 // tile
    band_specs = [
        pl.BlockSpec((tile, band_kv.shape[1]), lambda b, p, k=k: (b + skip + k, 0))
        for k in range(pieces)
    ]
    return pl.pallas_call(
        functools.partial(attention_kernel, row0),
        out_shape=jax.ShapeDtypeStruct((count, feat), jnp.bfloat16),
        grid_spec=pltpu.PrefetchScalarGridSpec(
            num_scalar_prefetch=1,
            grid=(count // tile,),
            in_specs=[pl.BlockSpec((tile, feat), lambda b, p: (b + skip, 0))]
            + band_specs
            + [pl.BlockSpec(prompt_kv.shape, lambda b, p: (0, 0))],
            out_specs=pl.BlockSpec((tile, feat), lambda b, p: (b, 0)),
        ),
        cost_estimate=pl.CostEstimate(
            flops=flops,
            transcendentals=count * (width + PROMPT) * HEADS,
            bytes_accessed=2 * (2 * count * feat + pieces * count * band_kv.shape[1] + prompt_kv.size),
        ),
    )(pos, queries, *([band_kv] * pieces), prompt_kv)


def per_device(
    hidden_in,
    ln_gain,
    w_qkv,
    w_out,
    final_gain,
    w_heads,
    actions,
    propensity,
    logged_reward,
    switch_index,
):
    tok_rows = hidden_in.shape[0]
    feat_width = hidden_in.shape[1]
    seq_devices = lax.axis_size("seq")
    seq_place = lax.axis_index("seq")
    total_len = tok_rows * seq_devices
    first_pos = seq_place * tok_rows
    hidden_state = hidden_in
    prompt_source = hidden_in[:PROMPT]
    for layer_idx in range(LAYERS):
        gain = ln_gain[layer_idx]
        weights = w_qkv[layer_idx]
        extended = with_halo(hidden_state, (("seq", 0),), HALF)
        prompt_rows = spread(prompt_source, "seq")
        extended_normed = layer_norm(extended, gain)
        band_kv = jnp.dot(
            extended_normed, weights[:, feat_width:], preferred_element_type=jnp.float32
        ).astype(jnp.bfloat16)
        normed = extended_normed[HALF : HALF + tok_rows]
        queries = (
            jnp.dot(normed, weights[:, :feat_width], preferred_element_type=jnp.float32) * 0.125
        ).astype(jnp.bfloat16)
        prompt_kv = jnp.dot(
            layer_norm(prompt_rows, gain),
            weights[:, feat_width:],
            preferred_element_type=jnp.float32,
        ).astype(jnp.bfloat16)
        if layer_idx + 1 < LAYERS and PROMPT + HALF <= tok_rows:
            early = attention(
                queries, band_kv, band_kv[HALF : HALF + PROMPT], first_pos, total_len, 0, PROMPT
            )
            early_proj = jnp.dot(early, w_out[layer_idx], preferred_element_type=jnp.float32)
            early_rows = (hidden_state[:PROMPT].astype(jnp.float32) + early_proj).astype(
                jnp.bfloat16
            )
        attended = attention(queries, band_kv, prompt_kv, first_pos, total_len, 0, tok_rows)
        projection = jnp.dot(attended, w_out[layer_idx], preferred_element_type=jnp.float32)
        hidden_state = (hidden_state.astype(jnp.float32) + projection).astype(jnp.bfloat16)
        if layer_idx + 1 < LAYERS and PROMPT + HALF <= tok_rows:
            prompt_source = early_rows
        else:
            prompt_source = hidden_state[:PROMPT]
    final = layer_norm(hidden_state, final_gain)
    head_out = jnp.dot(final, w_heads, preferred_element_type=jnp.float32)
    logits = head_out[:, :ACTIONS]
    reward_table = head_out[:, ACTIONS:]
    logit_max = jnp.max(logits, axis=-1, keepdims=True)
    exps = jnp.exp(logits - logit_max)
    policy = exps / jnp.sum(exps, axis=-1, keepdims=True)
    chosen = actions[:, None] == jnp.arange(ACTIONS, dtype=jnp.int32)[None, :]
    rewards = jnp.sum(jnp.where(chosen, reward_table, 0.0), axis=-1)
    chosen_prob = jnp.sum(jnp.where(chosen, policy, 0.0), axis=-1)
    direct = jnp.sum(policy * reward_table, axis=-1)
    logged_prob = propensity.astype(jnp.float32) / 65536.0
    cutoff = 0.5 * switch_index[0].astype(jnp.float32)
    dr_terms = direct + jnp.minimum(chosen_prob / logged_prob, cutoff) * (logged_reward - rewards)
    return (rewards, dr_terms)


def solution(mesh):
    placed = (
        P(("groups", "seq"), None),
        P(),
        P(),
        P(),
        P(),
        P(),
        P(("groups", "seq")),
        P(("groups", "seq")),
        P(("groups", "seq")),
        P("groups"),
    )
    return jax.shard_map(
        per_device,
        mesh=mesh,
        in_specs=placed,
        out_specs=(P(("groups", "seq")), P(("groups", "seq"))),
        check_vma=False,
    )
```

```python
import functools

import jax
import jax.numpy as jnp
from jax import lax
from jax.experimental import pallas as pl
from jax.experimental.pallas import tpu as pltpu
from jax.sharding import PartitionSpec as P

HEADS = 12
HEAD = 64
HALF = 256
PROMPT = 256
ACTIONS = 256
LAYERS = 2


def with_halo(array, sides, width):
    for axis, dim in sides:
        count, length = (lax.axis_size(axis), array.shape[dim])
        up = [(i, (i + 1) % count) for i in range(count - 1)]
        down = [(j, i) for i, j in up]
        last = lax.slice_in_dim(array, length - width, length, axis=dim)
        leading = lax.slice_in_dim(array, 0, width, axis=dim)
        before = lax.ppermute(last, axis, up)
        after = lax.ppermute(leading, axis, down)
        array = jnp.concatenate([before, array, after], axis=dim)
    return array


def tree_rounds(count):
    if count & (count - 1) == 0:
        bits = []
        step = count // 2
        while step:
            bits.append(step)
            step //= 2
        return [[[(i, i + bit) for i in range(0, count, 2 * bit)]] for bit in bits]
    rounds = []
    held = 1
    while held < count:
        rounds.append([[(i, i + held) for i in range(min(held, count - held))]])
        held *= 2
    return rounds


def spread(block, axis):
    place = lax.axis_index(axis)
    for ops in tree_rounds(lax.axis_size(axis)):
        received = block
        for op in ops:
            got = lax.ppermute(block, axis, op)
            targets = jnp.array([t for _, t in op], dtype=jnp.int32)
            received = jnp.where(jnp.any(place == targets), got, received)
        block = received
    return block


def layer_norm(hidden_state, gain_row):
    values_f = hidden_state.astype(jnp.float32)
    row_mean = jnp.mean(values_f, axis=-1, keepdims=True)
    centred = values_f - row_mean
    row_var = jnp.mean(centred * centred, axis=-1, keepdims=True)
    return (centred * lax.rsqrt(row_var + 1e-05) * gain_row).astype(jnp.bfloat16)


QUERY_TILE = 256
GROUP = 4


def attention_kernel(row0, pos_ref, q_ref, *refs):
    band_refs = refs[:-2]
    prompt_ref, out_ref = refs[-2:]
    tile = q_ref.shape[0]
    width = tile * len(band_refs)
    feat = q_ref.shape[1]
    lanes = GROUP * HEAD
    block = pl.program_id(0)
    first = pos_ref[0]
    total = pos_ref[1]
    query_pos = first + row0 + block * tile + lax.broadcasted_iota(jnp.int32, (tile, 1), 0)
    key_pos = first + row0 + block * tile - HALF + lax.broadcasted_iota(jnp.int32, (1, width), 1)
    gap = key_pos - query_pos
    band_ok = (gap >= -HALF) & (gap <= HALF) & (key_pos >= 0) & (key_pos < total)
    prompt_pos = lax.broadcasted_iota(jnp.int32, (1, PROMPT), 1)
    prompt_ok = jnp.abs(prompt_pos - query_pos) > HALF
    contract = (((1,), (1,)), ((), ()))
    lane_head = lax.broadcasted_iota(jnp.int32, (1, lanes), 1) // HEAD
    for group in range(feat // lanes):
        cols = slice(group * lanes, (group + 1) * lanes)
        vcols = slice(feat + group * lanes, feat + (group + 1) * lanes)
        band_keys = jnp.concatenate([ref[:, cols] for ref in band_refs], axis=0)
        band_values = jnp.concatenate([ref[:, vcols] for ref in band_refs], axis=0)
        query = q_ref[:, cols]
        stacked = jnp.concatenate(
            [jnp.where(lane_head == j, query, jnp.zeros_like(query)) for j in range(GROUP)],
            axis=0,
        )
        band_scores = lax.dot_general(
            stacked, band_keys, contract, preferred_element_type=jnp.float32
        ).reshape(GROUP, tile, width)
        prompt_scores = lax.dot_general(
            stacked, prompt_ref[:, cols], contract, preferred_element_type=jnp.float32
        ).reshape(GROUP, tile, PROMPT)
        band_scores = jnp.where(band_ok[None], band_scores, -1e30)
        prompt_scores = jnp.where(prompt_ok[None], prompt_scores, -1e30)
        row_max = jnp.maximum(
            jnp.max(band_scores, axis=2, keepdims=True),
            jnp.max(prompt_scores, axis=2, keepdims=True),
        )
        band_exp = jnp.exp(band_scores - row_max)
        prompt_exp = jnp.exp(prompt_scores - row_max)
        denom = jnp.sum(band_exp, axis=2, keepdims=True) + jnp.sum(
            prompt_exp, axis=2, keepdims=True
        )
        band_probs = band_exp.astype(jnp.bfloat16).reshape(GROUP * tile, width)
        prompt_probs = prompt_exp.astype(jnp.bfloat16).reshape(GROUP * tile, PROMPT)
        mixed = jnp.dot(band_probs, band_values, preferred_element_type=jnp.float32) + jnp.dot(
            prompt_probs, prompt_ref[:, vcols], preferred_element_type=jnp.float32
        )
        mixed = mixed * (1.0 / denom.reshape(GROUP * tile, 1))
        attn = mixed[:tile]
        for j in range(1, GROUP):
            attn = jnp.where(lane_head == j, mixed[j * tile : (j + 1) * tile], attn)
        out_ref[:, cols] = attn.astype(out_ref.dtype)


def attention(queries, band_kv, prompt_kv, first_pos, total_len, row0, count):
    feat = queries.shape[1]
    tile = min(QUERY_TILE, count)
    pos = jnp.stack([first_pos, total_len]).astype(jnp.int32)
    pieces = 1 + 2 * HALF // tile
    width = tile * pieces
    flops = 4 * count * (width + PROMPT) * feat * GROUP
    skip = row0 // tile
    band_specs = [
        pl.BlockSpec((tile, band_kv.shape[1]), lambda b, p, k=k: (b + skip + k, 0))
        for k in range(pieces)
    ]
    return pl.pallas_call(
        functools.partial(attention_kernel, row0),
        out_shape=jax.ShapeDtypeStruct((count, feat), jnp.bfloat16),
        grid_spec=pltpu.PrefetchScalarGridSpec(
            num_scalar_prefetch=1,
            grid=(count // tile,),
            in_specs=[pl.BlockSpec((tile, feat), lambda b, p: (b + skip, 0))]
            + band_specs
            + [pl.BlockSpec(prompt_kv.shape, lambda b, p: (0, 0))],
            out_specs=pl.BlockSpec((tile, feat), lambda b, p: (b, 0)),
        ),
        cost_estimate=pl.CostEstimate(
            flops=flops,
            transcendentals=count * (width + PROMPT) * HEADS,
            bytes_accessed=2 * (2 * count * feat + pieces * count * band_kv.shape[1] + prompt_kv.size),
        ),
    )(pos, queries, *([band_kv] * pieces), prompt_kv)


def per_device(
    hidden_in,
    ln_gain,
    w_qkv,
    w_out,
    final_gain,
    w_heads,
    actions,
    propensity,
    logged_reward,
    switch_index,
):
    tok_rows = hidden_in.shape[0]
    feat_width = hidden_in.shape[1]
    seq_devices = lax.axis_size("seq")
    seq_place = lax.axis_index("seq")
    total_len = tok_rows * seq_devices
    first_pos = seq_place * tok_rows
    hidden_state = hidden_in
    prompt_source = hidden_in[:PROMPT]
    for layer_idx in range(LAYERS):
        gain = ln_gain[layer_idx]
        weights = w_qkv[layer_idx]
        extended = with_halo(hidden_state, (("seq", 0),), HALF)
        prompt_rows = spread(prompt_source, "seq")
        extended_normed = layer_norm(extended, gain)
        band_kv = jnp.dot(
            extended_normed, weights[:, feat_width:], preferred_element_type=jnp.float32
        ).astype(jnp.bfloat16)
        normed = extended_normed[HALF : HALF + tok_rows]
        queries = (
            jnp.dot(normed, weights[:, :feat_width], preferred_element_type=jnp.float32) * 0.125
        ).astype(jnp.bfloat16)
        prompt_kv = jnp.dot(
            layer_norm(prompt_rows, gain),
            weights[:, feat_width:],
            preferred_element_type=jnp.float32,
        ).astype(jnp.bfloat16)
        attended = attention(queries, band_kv, prompt_kv, first_pos, total_len, 0, tok_rows)
        projection = jnp.dot(attended, w_out[layer_idx], preferred_element_type=jnp.float32)
        hidden_state = (hidden_state.astype(jnp.float32) + projection).astype(jnp.bfloat16)
        prompt_source = hidden_state[:PROMPT]
    final = layer_norm(hidden_state, final_gain)
    head_out = jnp.dot(final, w_heads, preferred_element_type=jnp.float32)
    logits = head_out[:, :ACTIONS]
    reward_table = head_out[:, ACTIONS:]
    logit_max = jnp.max(logits, axis=-1, keepdims=True)
    exps = jnp.exp(logits - logit_max)
    policy = exps / jnp.sum(exps, axis=-1, keepdims=True)
    chosen = actions[:, None] == jnp.arange(ACTIONS, dtype=jnp.int32)[None, :]
    rewards = jnp.sum(jnp.where(chosen, reward_table, 0.0), axis=-1)
    chosen_prob = jnp.sum(jnp.where(chosen, policy, 0.0), axis=-1)
    direct = jnp.sum(policy * reward_table, axis=-1)
    logged_prob = propensity.astype(jnp.float32) / 65536.0
    cutoff = 0.5 * switch_index[0].astype(jnp.float32)
    dr_terms = direct + jnp.minimum(chosen_prob / logged_prob, cutoff) * (logged_reward - rewards)
    return (rewards, dr_terms)


def solution(mesh):
    placed = (
        P(("groups", "seq"), None),
        P(),
        P(),
        P(),
        P(),
        P(),
        P(("groups", "seq")),
        P(("groups", "seq")),
        P(("groups", "seq")),
        P("groups"),
    )
    return jax.shard_map(
        per_device,
        mesh=mesh,
        in_specs=placed,
        out_specs=(P(("groups", "seq")), P(("groups", "seq"))),
        check_vma=False,
    )
```

```python
import functools

import jax
import jax.numpy as jnp
from jax import lax
from jax.experimental import pallas as pl
from jax.experimental.pallas import tpu as pltpu
from jax.sharding import PartitionSpec as P

HEADS = 12
HEAD = 64
HALF = 256
PROMPT = 256
ACTIONS = 256
LAYERS = 2


def with_halo(array, sides, width):
    for axis, dim in sides:
        count, length = (lax.axis_size(axis), array.shape[dim])
        up = [(i, (i + 1) % count) for i in range(count - 1)]
        down = [(j, i) for i, j in up]
        last = lax.slice_in_dim(array, length - width, length, axis=dim)
        leading = lax.slice_in_dim(array, 0, width, axis=dim)
        before = lax.ppermute(last, axis, up)
        after = lax.ppermute(leading, axis, down)
        array = jnp.concatenate([before, array, after], axis=dim)
    return array


def tree_rounds(count):
    if count & (count - 1) == 0:
        bits = []
        step = count // 2
        while step:
            bits.append(step)
            step //= 2
        return [[[(i, i + bit) for i in range(0, count, 2 * bit)]] for bit in bits]
    rounds = []
    held = 1
    while held < count:
        rounds.append([[(i, i + held) for i in range(min(held, count - held))]])
        held *= 2
    return rounds


def spread(block, axis):
    place = lax.axis_index(axis)
    for ops in tree_rounds(lax.axis_size(axis)):
        received = block
        for op in ops:
            got = lax.ppermute(block, axis, op)
            targets = jnp.array([t for _, t in op], dtype=jnp.int32)
            received = jnp.where(jnp.any(place == targets), got, received)
        block = received
    return block


def layer_norm(hidden_state, gain_row):
    values_f = hidden_state.astype(jnp.float32)
    row_mean = jnp.mean(values_f, axis=-1, keepdims=True)
    centred = values_f - row_mean
    row_var = jnp.mean(centred * centred, axis=-1, keepdims=True)
    return (centred * lax.rsqrt(row_var + 1e-05) * gain_row).astype(jnp.bfloat16)


QUERY_TILE = 256
GROUP = 4


def attention_kernel(row0, pos_ref, q_ref, *refs):
    band_refs = refs[:-2]
    prompt_ref, out_ref = refs[-2:]
    tile = q_ref.shape[0]
    width = tile * len(band_refs)
    feat = q_ref.shape[1]
    lanes = GROUP * HEAD
    block = pl.program_id(0)
    first = pos_ref[0]
    total = pos_ref[1]
    query_pos = first + row0 + block * tile + lax.broadcasted_iota(jnp.int32, (tile, 1), 0)
    key_pos = first + row0 + block * tile - HALF + lax.broadcasted_iota(jnp.int32, (1, width), 1)
    gap = key_pos - query_pos
    band_ok = (gap >= -HALF) & (gap <= HALF) & (key_pos >= 0) & (key_pos < total)
    prompt_pos = lax.broadcasted_iota(jnp.int32, (1, PROMPT), 1)
    prompt_ok = jnp.abs(prompt_pos - query_pos) > HALF
    contract = (((1,), (1,)), ((), ()))
    lane_head = lax.broadcasted_iota(jnp.int32, (1, lanes), 1) // HEAD
    for group in range(feat // lanes):
        cols = slice(group * lanes, (group + 1) * lanes)
        vcols = slice(feat + group * lanes, feat + (group + 1) * lanes)
        band_keys = jnp.concatenate([ref[:, cols] for ref in band_refs], axis=0)
        band_values = jnp.concatenate([ref[:, vcols] for ref in band_refs], axis=0)
        query = q_ref[:, cols]
        stacked = jnp.concatenate(
            [jnp.where(lane_head == j, query, jnp.zeros_like(query)) for j in range(GROUP)],
            axis=0,
        )
        band_scores = lax.dot_general(
            stacked, band_keys, contract, preferred_element_type=jnp.float32
        ).reshape(GROUP, tile, width)
        prompt_scores = lax.dot_general(
            stacked, prompt_ref[:, cols], contract, preferred_element_type=jnp.float32
        ).reshape(GROUP, tile, PROMPT)
        band_scores = jnp.where(band_ok[None], band_scores, -1e30)
        prompt_scores = jnp.where(prompt_ok[None], prompt_scores, -1e30)
        row_max = jnp.maximum(
            jnp.max(band_scores, axis=2, keepdims=True),
            jnp.max(prompt_scores, axis=2, keepdims=True),
        )
        band_exp = jnp.exp(band_scores - row_max)
        prompt_exp = jnp.exp(prompt_scores - row_max)
        denom = jnp.sum(band_exp, axis=2, keepdims=True) + jnp.sum(
            prompt_exp, axis=2, keepdims=True
        )
        band_probs = band_exp.astype(jnp.bfloat16).reshape(GROUP * tile, width)
        prompt_probs = prompt_exp.astype(jnp.bfloat16).reshape(GROUP * tile, PROMPT)
        mixed = jnp.dot(band_probs, band_values, preferred_element_type=jnp.float32) + jnp.dot(
            prompt_probs, prompt_ref[:, vcols], preferred_element_type=jnp.float32
        )
        mixed = mixed * (1.0 / denom.reshape(GROUP * tile, 1))
        attn = mixed[:tile]
        for j in range(1, GROUP):
            attn = jnp.where(lane_head == j, mixed[j * tile : (j + 1) * tile], attn)
        out_ref[:, cols] = attn.astype(out_ref.dtype)


def attention(queries, band_kv, prompt_kv, first_pos, total_len, row0, count):
    feat = queries.shape[1]
    tile = min(QUERY_TILE, count)
    pos = jnp.stack([first_pos, total_len]).astype(jnp.int32)
    pieces = 1 + 2 * HALF // tile
    width = tile * pieces
    flops = 4 * count * (width + PROMPT) * feat * GROUP
    skip = row0 // tile
    band_specs = [
        pl.BlockSpec((tile, band_kv.shape[1]), lambda b, p, k=k: (b + skip + k, 0))
        for k in range(pieces)
    ]
    return pl.pallas_call(
        functools.partial(attention_kernel, row0),
        out_shape=jax.ShapeDtypeStruct((count, feat), jnp.bfloat16),
        grid_spec=pltpu.PrefetchScalarGridSpec(
            num_scalar_prefetch=1,
            grid=(count // tile,),
            in_specs=[pl.BlockSpec((tile, feat), lambda b, p: (b + skip, 0))]
            + band_specs
            + [pl.BlockSpec(prompt_kv.shape, lambda b, p: (0, 0))],
            out_specs=pl.BlockSpec((tile, feat), lambda b, p: (b, 0)),
        ),
        cost_estimate=pl.CostEstimate(
            flops=flops,
            transcendentals=count * (width + PROMPT) * HEADS,
            bytes_accessed=2 * (2 * count * feat + pieces * count * band_kv.shape[1] + prompt_kv.size),
        ),
    )(pos, queries, *([band_kv] * pieces), prompt_kv)


def per_device(
    hidden_in,
    ln_gain,
    w_qkv,
    w_out,
    final_gain,
    w_heads,
    actions,
    propensity,
    logged_reward,
    switch_index,
):
    tok_rows = hidden_in.shape[0]
    feat_width = hidden_in.shape[1]
    seq_devices = lax.axis_size("seq")
    seq_place = lax.axis_index("seq")
    total_len = tok_rows * seq_devices
    first_pos = seq_place * tok_rows
    hidden_state = hidden_in
    prompt_source = hidden_in[:PROMPT]
    for layer_idx in range(LAYERS):
        gain = ln_gain[layer_idx]
        if layer_idx == 0:
            weights = w_qkv[0]
        else:
            later_weights, hidden_state = lax.optimization_barrier((w_qkv, hidden_state))
            weights = later_weights[layer_idx]
        extended = with_halo(hidden_state, (("seq", 0),), HALF)
        prompt_rows = spread(prompt_source, "seq")
        extended_normed = layer_norm(extended, gain)
        band_kv = jnp.dot(
            extended_normed, weights[:, feat_width:], preferred_element_type=jnp.float32
        ).astype(jnp.bfloat16)
        normed = extended_normed[HALF : HALF + tok_rows]
        queries = (
            jnp.dot(normed, weights[:, :feat_width], preferred_element_type=jnp.float32) * 0.125
        ).astype(jnp.bfloat16)
        prompt_kv = jnp.dot(
            layer_norm(prompt_rows, gain),
            weights[:, feat_width:],
            preferred_element_type=jnp.float32,
        ).astype(jnp.bfloat16)
        attended = attention(queries, band_kv, prompt_kv, first_pos, total_len, 0, tok_rows)
        projection = jnp.dot(attended, w_out[layer_idx], preferred_element_type=jnp.float32)
        hidden_state = (hidden_state.astype(jnp.float32) + projection).astype(jnp.bfloat16)
        prompt_source = hidden_state[:PROMPT]
    final = layer_norm(hidden_state, final_gain)
    head_out = jnp.dot(final, w_heads, preferred_element_type=jnp.float32)
    logits = head_out[:, :ACTIONS]
    reward_table = head_out[:, ACTIONS:]
    logit_max = jnp.max(logits, axis=-1, keepdims=True)
    exps = jnp.exp(logits - logit_max)
    policy = exps / jnp.sum(exps, axis=-1, keepdims=True)
    chosen = actions[:, None] == jnp.arange(ACTIONS, dtype=jnp.int32)[None, :]
    rewards = jnp.sum(jnp.where(chosen, reward_table, 0.0), axis=-1)
    chosen_prob = jnp.sum(jnp.where(chosen, policy, 0.0), axis=-1)
    direct = jnp.sum(policy * reward_table, axis=-1)
    logged_prob = propensity.astype(jnp.float32) / 65536.0
    cutoff = 0.5 * switch_index[0].astype(jnp.float32)
    dr_terms = direct + jnp.minimum(chosen_prob / logged_prob, cutoff) * (logged_reward - rewards)
    return (rewards, dr_terms)


def solution(mesh):
    placed = (
        P(("groups", "seq"), None),
        P(),
        P(),
        P(),
        P(),
        P(),
        P(("groups", "seq")),
        P(("groups", "seq")),
        P(("groups", "seq")),
        P("groups"),
    )
    return jax.shard_map(
        per_device,
        mesh=mesh,
        in_specs=placed,
        out_specs=(P(("groups", "seq")), P(("groups", "seq"))),
        check_vma=False,
    )
```

```python
import functools

import jax
import jax.numpy as jnp
from jax import lax
from jax.experimental import pallas as pl
from jax.experimental.pallas import tpu as pltpu
from jax.sharding import PartitionSpec as P

HEADS = 12
HEAD = 64
HALF = 256
PROMPT = 256
ACTIONS = 256
LAYERS = 2


def with_halo(array, sides, width):
    for axis, dim in sides:
        count, length = (lax.axis_size(axis), array.shape[dim])
        up = [(i, (i + 1) % count) for i in range(count - 1)]
        down = [(j, i) for i, j in up]
        last = lax.slice_in_dim(array, length - width, length, axis=dim)
        leading = lax.slice_in_dim(array, 0, width, axis=dim)
        before = lax.ppermute(last, axis, up)
        after = lax.ppermute(leading, axis, down)
        array = jnp.concatenate([before, array, after], axis=dim)
    return array


def tree_rounds(count):
    if count & (count - 1) == 0:
        bits = []
        step = count // 2
        while step:
            bits.append(step)
            step //= 2
        return [[[(i, i + bit) for i in range(0, count, 2 * bit)]] for bit in bits]
    rounds = []
    held = 1
    while held < count:
        rounds.append([[(i, i + held) for i in range(min(held, count - held))]])
        held *= 2
    return rounds


def spread(block, axis, hold=None):
    place = lax.axis_index(axis)
    for round_idx, ops in enumerate(tree_rounds(lax.axis_size(axis))):
        if round_idx == 1 and hold is not None:
            block, hold = lax.optimization_barrier((block, hold))
        received = block
        for op in ops:
            got = lax.ppermute(block, axis, op)
            targets = jnp.array([t for _, t in op], dtype=jnp.int32)
            received = jnp.where(jnp.any(place == targets), got, received)
        block = received
    return block


def layer_norm(hidden_state, gain_row):
    values_f = hidden_state.astype(jnp.float32)
    row_mean = jnp.mean(values_f, axis=-1, keepdims=True)
    centred = values_f - row_mean
    row_var = jnp.mean(centred * centred, axis=-1, keepdims=True)
    return (centred * lax.rsqrt(row_var + 1e-05) * gain_row).astype(jnp.bfloat16)


QUERY_TILE = 256
GROUP = 4


def attention_kernel(row0, pos_ref, q_ref, *refs):
    band_refs = refs[:-2]
    prompt_ref, out_ref = refs[-2:]
    tile = q_ref.shape[0]
    width = tile * len(band_refs)
    feat = q_ref.shape[1]
    lanes = GROUP * HEAD
    block = pl.program_id(0)
    first = pos_ref[0]
    total = pos_ref[1]
    query_pos = first + row0 + block * tile + lax.broadcasted_iota(jnp.int32, (tile, 1), 0)
    key_pos = first + row0 + block * tile - HALF + lax.broadcasted_iota(jnp.int32, (1, width), 1)
    gap = key_pos - query_pos
    band_ok = (gap >= -HALF) & (gap <= HALF) & (key_pos >= 0) & (key_pos < total)
    prompt_pos = lax.broadcasted_iota(jnp.int32, (1, PROMPT), 1)
    prompt_ok = jnp.abs(prompt_pos - query_pos) > HALF
    contract = (((1,), (1,)), ((), ()))
    lane_head = lax.broadcasted_iota(jnp.int32, (1, lanes), 1) // HEAD
    for group in range(feat // lanes):
        cols = slice(group * lanes, (group + 1) * lanes)
        vcols = slice(feat + group * lanes, feat + (group + 1) * lanes)
        band_keys = jnp.concatenate([ref[:, cols] for ref in band_refs], axis=0)
        band_values = jnp.concatenate([ref[:, vcols] for ref in band_refs], axis=0)
        query = q_ref[:, cols]
        stacked = jnp.concatenate(
            [jnp.where(lane_head == j, query, jnp.zeros_like(query)) for j in range(GROUP)],
            axis=0,
        )
        band_scores = lax.dot_general(
            stacked, band_keys, contract, preferred_element_type=jnp.float32
        ).reshape(GROUP, tile, width)
        prompt_scores = lax.dot_general(
            stacked, prompt_ref[:, cols], contract, preferred_element_type=jnp.float32
        ).reshape(GROUP, tile, PROMPT)
        band_scores = jnp.where(band_ok[None], band_scores, -1e30)
        prompt_scores = jnp.where(prompt_ok[None], prompt_scores, -1e30)
        row_max = jnp.maximum(
            jnp.max(band_scores, axis=2, keepdims=True),
            jnp.max(prompt_scores, axis=2, keepdims=True),
        )
        band_exp = jnp.exp(band_scores - row_max)
        prompt_exp = jnp.exp(prompt_scores - row_max)
        denom = jnp.sum(band_exp, axis=2, keepdims=True) + jnp.sum(
            prompt_exp, axis=2, keepdims=True
        )
        band_probs = band_exp.astype(jnp.bfloat16).reshape(GROUP * tile, width)
        prompt_probs = prompt_exp.astype(jnp.bfloat16).reshape(GROUP * tile, PROMPT)
        mixed = jnp.dot(band_probs, band_values, preferred_element_type=jnp.float32) + jnp.dot(
            prompt_probs, prompt_ref[:, vcols], preferred_element_type=jnp.float32
        )
        mixed = mixed * (1.0 / denom.reshape(GROUP * tile, 1))
        attn = mixed[:tile]
        for j in range(1, GROUP):
            attn = jnp.where(lane_head == j, mixed[j * tile : (j + 1) * tile], attn)
        out_ref[:, cols] = attn.astype(out_ref.dtype)


def attention(queries, band_kv, prompt_kv, first_pos, total_len, row0, count):
    feat = queries.shape[1]
    tile = min(QUERY_TILE, count)
    pos = jnp.stack([first_pos, total_len]).astype(jnp.int32)
    pieces = 1 + 2 * HALF // tile
    width = tile * pieces
    flops = 4 * count * (width + PROMPT) * feat * GROUP
    skip = row0 // tile
    band_specs = [
        pl.BlockSpec((tile, band_kv.shape[1]), lambda b, p, k=k: (b + skip + k, 0))
        for k in range(pieces)
    ]
    return pl.pallas_call(
        functools.partial(attention_kernel, row0),
        out_shape=jax.ShapeDtypeStruct((count, feat), jnp.bfloat16),
        grid_spec=pltpu.PrefetchScalarGridSpec(
            num_scalar_prefetch=1,
            grid=(count // tile,),
            in_specs=[pl.BlockSpec((tile, feat), lambda b, p: (b + skip, 0))]
            + band_specs
            + [pl.BlockSpec(prompt_kv.shape, lambda b, p: (0, 0))],
            out_specs=pl.BlockSpec((tile, feat), lambda b, p: (b, 0)),
        ),
        cost_estimate=pl.CostEstimate(
            flops=flops,
            transcendentals=count * (width + PROMPT) * HEADS,
            bytes_accessed=2 * (2 * count * feat + pieces * count * band_kv.shape[1] + prompt_kv.size),
        ),
    )(pos, queries, *([band_kv] * pieces), prompt_kv)


def per_device(
    hidden_in,
    ln_gain,
    w_qkv,
    w_out,
    final_gain,
    w_heads,
    actions,
    propensity,
    logged_reward,
    switch_index,
):
    tok_rows = hidden_in.shape[0]
    feat_width = hidden_in.shape[1]
    seq_devices = lax.axis_size("seq")
    seq_place = lax.axis_index("seq")
    total_len = tok_rows * seq_devices
    first_pos = seq_place * tok_rows
    hidden_state = hidden_in
    prompt_source = hidden_in[:PROMPT]
    for layer_idx in range(LAYERS):
        gain = ln_gain[layer_idx]
        weights = w_qkv[layer_idx]
        extended = with_halo(hidden_state, (("seq", 0),), HALF)
        extended_normed = layer_norm(extended, gain)
        band_kv = jnp.dot(
            extended_normed, weights[:, feat_width:], preferred_element_type=jnp.float32
        ).astype(jnp.bfloat16)
        normed = extended_normed[HALF : HALF + tok_rows]
        queries = (
            jnp.dot(normed, weights[:, :feat_width], preferred_element_type=jnp.float32) * 0.125
        ).astype(jnp.bfloat16)
        prompt_rows = spread(prompt_source, "seq", hold=(band_kv, queries))
        prompt_kv = jnp.dot(
            layer_norm(prompt_rows, gain),
            weights[:, feat_width:],
            preferred_element_type=jnp.float32,
        ).astype(jnp.bfloat16)
        attended = attention(queries, band_kv, prompt_kv, first_pos, total_len, 0, tok_rows)
        projection = jnp.dot(attended, w_out[layer_idx], preferred_element_type=jnp.float32)
        hidden_state = (hidden_state.astype(jnp.float32) + projection).astype(jnp.bfloat16)
        prompt_source = hidden_state[:PROMPT]
    final = layer_norm(hidden_state, final_gain)
    head_out = jnp.dot(final, w_heads, preferred_element_type=jnp.float32)
    logits = head_out[:, :ACTIONS]
    reward_table = head_out[:, ACTIONS:]
    logit_max = jnp.max(logits, axis=-1, keepdims=True)
    exps = jnp.exp(logits - logit_max)
    policy = exps / jnp.sum(exps, axis=-1, keepdims=True)
    chosen = actions[:, None] == jnp.arange(ACTIONS, dtype=jnp.int32)[None, :]
    rewards = jnp.sum(jnp.where(chosen, reward_table, 0.0), axis=-1)
    chosen_prob = jnp.sum(jnp.where(chosen, policy, 0.0), axis=-1)
    direct = jnp.sum(policy * reward_table, axis=-1)
    logged_prob = propensity.astype(jnp.float32) / 65536.0
    cutoff = 0.5 * switch_index[0].astype(jnp.float32)
    dr_terms = direct + jnp.minimum(chosen_prob / logged_prob, cutoff) * (logged_reward - rewards)
    return (rewards, dr_terms)


def solution(mesh):
    placed = (
        P(("groups", "seq"), None),
        P(),
        P(),
        P(),
        P(),
        P(),
        P(("groups", "seq")),
        P(("groups", "seq")),
        P(("groups", "seq")),
        P("groups"),
    )
    return jax.shard_map(
        per_device,
        mesh=mesh,
        in_specs=placed,
        out_specs=(P(("groups", "seq")), P(("groups", "seq"))),
        check_vma=False,
    )
```

```python
import functools

import jax
import jax.numpy as jnp
from jax import lax
from jax.experimental import pallas as pl
from jax.experimental.pallas import tpu as pltpu
from jax.sharding import PartitionSpec as P

HEADS = 12
HEAD = 64
HALF = 256
PROMPT = 256
ACTIONS = 256
LAYERS = 2


def with_halo(array, sides, width):
    for axis, dim in sides:
        count, length = (lax.axis_size(axis), array.shape[dim])
        up = [(i, (i + 1) % count) for i in range(count - 1)]
        down = [(j, i) for i, j in up]
        last = lax.slice_in_dim(array, length - width, length, axis=dim)
        leading = lax.slice_in_dim(array, 0, width, axis=dim)
        before = lax.ppermute(last, axis, up)
        after = lax.ppermute(leading, axis, down)
        array = jnp.concatenate([before, array, after], axis=dim)
    return array


def tree_rounds(count):
    if count & (count - 1) == 0:
        bits = []
        step = count // 2
        while step:
            bits.append(step)
            step //= 2
        return [[[(i, i + bit) for i in range(0, count, 2 * bit)]] for bit in bits]
    rounds = []
    held = 1
    while held < count:
        rounds.append([[(i, i + held) for i in range(min(held, count - held))]])
        held *= 2
    return rounds


def spread(block, axis):
    place = lax.axis_index(axis)
    for ops in tree_rounds(lax.axis_size(axis)):
        received = block
        for op in ops:
            got = lax.ppermute(block, axis, op)
            targets = jnp.array([t for _, t in op], dtype=jnp.int32)
            received = jnp.where(jnp.any(place == targets), got, received)
        block = received
    return block


def layer_norm(hidden_state, gain_row):
    values_f = hidden_state.astype(jnp.float32)
    row_mean = jnp.mean(values_f, axis=-1, keepdims=True)
    centred = values_f - row_mean
    row_var = jnp.mean(centred * centred, axis=-1, keepdims=True)
    return (centred * lax.rsqrt(row_var + 1e-05) * gain_row).astype(jnp.bfloat16)


QUERY_TILE = 256
GROUP = 4


def attention_kernel(row0, pos_ref, q_ref, *refs):
    key_refs = refs[: (len(refs) - 3) // 2]
    value_refs = refs[(len(refs) - 3) // 2 : -3]
    prompt_key_ref, prompt_value_ref, out_ref = refs[-3:]
    tile = q_ref.shape[0]
    width = tile * len(key_refs)
    lanes = q_ref.shape[1]
    block = pl.program_id(0)
    first = pos_ref[0]
    total = pos_ref[1]
    query_pos = first + row0 + block * tile + lax.broadcasted_iota(jnp.int32, (tile, 1), 0)
    key_pos = first + row0 + block * tile - HALF + lax.broadcasted_iota(jnp.int32, (1, width), 1)
    gap = key_pos - query_pos
    band_ok = (gap >= -HALF) & (gap <= HALF) & (key_pos >= 0) & (key_pos < total)
    prompt_pos = lax.broadcasted_iota(jnp.int32, (1, PROMPT), 1)
    prompt_ok = jnp.abs(prompt_pos - query_pos) > HALF
    contract = (((1,), (1,)), ((), ()))
    lane_head = lax.broadcasted_iota(jnp.int32, (1, lanes), 1) // HEAD
    band_keys = jnp.concatenate([ref[...] for ref in key_refs], axis=0)
    band_values = jnp.concatenate([ref[...] for ref in value_refs], axis=0)
    query = q_ref[...]
    stacked = jnp.concatenate(
        [jnp.where(lane_head == j, query, jnp.zeros_like(query)) for j in range(GROUP)],
        axis=0,
    )
    band_scores = lax.dot_general(
        stacked, band_keys, contract, preferred_element_type=jnp.float32
    ).reshape(GROUP, tile, width)
    prompt_scores = lax.dot_general(
        stacked, prompt_key_ref[...], contract, preferred_element_type=jnp.float32
    ).reshape(GROUP, tile, PROMPT)
    band_scores = jnp.where(band_ok[None], band_scores, -1e30)
    prompt_scores = jnp.where(prompt_ok[None], prompt_scores, -1e30)
    row_max = jnp.maximum(
        jnp.max(band_scores, axis=2, keepdims=True),
        jnp.max(prompt_scores, axis=2, keepdims=True),
    )
    band_exp = jnp.exp(band_scores - row_max)
    prompt_exp = jnp.exp(prompt_scores - row_max)
    denom = jnp.sum(band_exp, axis=2, keepdims=True) + jnp.sum(prompt_exp, axis=2, keepdims=True)
    band_probs = band_exp.astype(jnp.bfloat16).reshape(GROUP * tile, width)
    prompt_probs = prompt_exp.astype(jnp.bfloat16).reshape(GROUP * tile, PROMPT)
    mixed = jnp.dot(band_probs, band_values, preferred_element_type=jnp.float32) + jnp.dot(
        prompt_probs, prompt_value_ref[...], preferred_element_type=jnp.float32
    )
    mixed = mixed * (1.0 / denom.reshape(GROUP * tile, 1))
    attn = mixed[:tile]
    for j in range(1, GROUP):
        attn = jnp.where(lane_head == j, mixed[j * tile : (j + 1) * tile], attn)
    out_ref[...] = attn.astype(out_ref.dtype)


def attention(queries, band_kv, prompt_kv, first_pos, total_len, row0, count):
    feat = queries.shape[1]
    tile = min(QUERY_TILE, count)
    lanes = GROUP * HEAD
    groups = feat // lanes
    pos = jnp.stack([first_pos, total_len]).astype(jnp.int32)
    pieces = 1 + 2 * HALF // tile
    width = tile * pieces
    skip = row0 // tile
    key_specs = [
        pl.BlockSpec((tile, lanes), lambda b, g, p, k=k: (b + skip + k, g)) for k in range(pieces)
    ]
    value_specs = [
        pl.BlockSpec((tile, lanes), lambda b, g, p, k=k: (b + skip + k, g + groups))
        for k in range(pieces)
    ]
    return pl.pallas_call(
        functools.partial(attention_kernel, row0),
        out_shape=jax.ShapeDtypeStruct((count, feat), jnp.bfloat16),
        grid_spec=pltpu.PrefetchScalarGridSpec(
            num_scalar_prefetch=1,
            grid=(count // tile, groups),
            in_specs=[pl.BlockSpec((tile, lanes), lambda b, g, p: (b + skip, g))]
            + key_specs
            + value_specs
            + [
                pl.BlockSpec((PROMPT, lanes), lambda b, g, p: (0, g)),
                pl.BlockSpec((PROMPT, lanes), lambda b, g, p: (0, g + groups)),
            ],
            out_specs=pl.BlockSpec((tile, lanes), lambda b, g, p: (b, g)),
        ),
        cost_estimate=pl.CostEstimate(
            flops=4 * count * (width + PROMPT) * feat * GROUP,
            transcendentals=count * (width + PROMPT) * HEADS,
            bytes_accessed=2 * (2 * count * feat + pieces * count * band_kv.shape[1] + prompt_kv.size),
        ),
    )(pos, queries, *([band_kv] * (2 * pieces)), prompt_kv, prompt_kv)


def per_device(
    hidden_in,
    ln_gain,
    w_qkv,
    w_out,
    final_gain,
    w_heads,
    actions,
    propensity,
    logged_reward,
    switch_index,
):
    tok_rows = hidden_in.shape[0]
    feat_width = hidden_in.shape[1]
    seq_devices = lax.axis_size("seq")
    seq_place = lax.axis_index("seq")
    total_len = tok_rows * seq_devices
    first_pos = seq_place * tok_rows
    hidden_state = hidden_in
    prompt_source = hidden_in[:PROMPT]
    for layer_idx in range(LAYERS):
        gain = ln_gain[layer_idx]
        weights = w_qkv[layer_idx]
        extended = with_halo(hidden_state, (("seq", 0),), HALF)
        prompt_rows = spread(prompt_source, "seq")
        extended_normed = layer_norm(extended, gain)
        band_kv = jnp.dot(
            extended_normed, weights[:, feat_width:], preferred_element_type=jnp.float32
        ).astype(jnp.bfloat16)
        normed = extended_normed[HALF : HALF + tok_rows]
        queries = (
            jnp.dot(normed, weights[:, :feat_width], preferred_element_type=jnp.float32) * 0.125
        ).astype(jnp.bfloat16)
        prompt_kv = jnp.dot(
            layer_norm(prompt_rows, gain),
            weights[:, feat_width:],
            preferred_element_type=jnp.float32,
        ).astype(jnp.bfloat16)
        attended = attention(queries, band_kv, prompt_kv, first_pos, total_len, 0, tok_rows)
        projection = jnp.dot(attended, w_out[layer_idx], preferred_element_type=jnp.float32)
        hidden_state = (hidden_state.astype(jnp.float32) + projection).astype(jnp.bfloat16)
        prompt_source = hidden_state[:PROMPT]
    final = layer_norm(hidden_state, final_gain)
    head_out = jnp.dot(final, w_heads, preferred_element_type=jnp.float32)
    logits = head_out[:, :ACTIONS]
    reward_table = head_out[:, ACTIONS:]
    logit_max = jnp.max(logits, axis=-1, keepdims=True)
    exps = jnp.exp(logits - logit_max)
    policy = exps / jnp.sum(exps, axis=-1, keepdims=True)
    chosen = actions[:, None] == jnp.arange(ACTIONS, dtype=jnp.int32)[None, :]
    rewards = jnp.sum(jnp.where(chosen, reward_table, 0.0), axis=-1)
    chosen_prob = jnp.sum(jnp.where(chosen, policy, 0.0), axis=-1)
    direct = jnp.sum(policy * reward_table, axis=-1)
    logged_prob = propensity.astype(jnp.float32) / 65536.0
    cutoff = 0.5 * switch_index[0].astype(jnp.float32)
    dr_terms = direct + jnp.minimum(chosen_prob / logged_prob, cutoff) * (logged_reward - rewards)
    return (rewards, dr_terms)


def solution(mesh):
    placed = (
        P(("groups", "seq"), None),
        P(),
        P(),
        P(),
        P(),
        P(),
        P(("groups", "seq")),
        P(("groups", "seq")),
        P(("groups", "seq")),
        P("groups"),
    )
    return jax.shard_map(
        per_device,
        mesh=mesh,
        in_specs=placed,
        out_specs=(P(("groups", "seq")), P(("groups", "seq"))),
        check_vma=False,
    )
```

```python
import functools

import jax
import jax.numpy as jnp
from jax import lax
from jax.experimental import pallas as pl
from jax.experimental.pallas import tpu as pltpu
from jax.sharding import PartitionSpec as P

HEADS = 12
HEAD = 64
HALF = 256
PROMPT = 256
ACTIONS = 256
LAYERS = 2


def with_halo(array, sides, width):
    for axis, dim in sides:
        count, length = (lax.axis_size(axis), array.shape[dim])
        up = [(i, (i + 1) % count) for i in range(count - 1)]
        down = [(j, i) for i, j in up]
        last = lax.slice_in_dim(array, length - width, length, axis=dim)
        leading = lax.slice_in_dim(array, 0, width, axis=dim)
        before = lax.ppermute(last, axis, up)
        after = lax.ppermute(leading, axis, down)
        array = jnp.concatenate([before, array, after], axis=dim)
    return array


def tree_rounds(count):
    if count & (count - 1) == 0:
        bits = []
        step = count // 2
        while step:
            bits.append(step)
            step //= 2
        return [[[(i, i + bit) for i in range(0, count, 2 * bit)]] for bit in bits]
    rounds = []
    held = 1
    while held < count:
        rounds.append([[(i, i + held) for i in range(min(held, count - held))]])
        held *= 2
    return rounds


def spread(block, axis):
    place = lax.axis_index(axis)
    for ops in tree_rounds(lax.axis_size(axis)):
        received = block
        for op in ops:
            got = lax.ppermute(block, axis, op)
            targets = jnp.array([t for _, t in op], dtype=jnp.int32)
            received = jnp.where(jnp.any(place == targets), got, received)
        block = received
    return block


def layer_norm(hidden_state, gain_row):
    values_f = hidden_state.astype(jnp.float32)
    row_mean = jnp.mean(values_f, axis=-1, keepdims=True)
    centred = values_f - row_mean
    row_var = jnp.mean(centred * centred, axis=-1, keepdims=True)
    return (centred * lax.rsqrt(row_var + 1e-05) * gain_row).astype(jnp.bfloat16)


QUERY_TILE = 256
GROUP = 4


def attention_kernel(row0, pos_ref, q_ref, *refs):
    band_refs = refs[:-2]
    prompt_ref, out_ref = refs[-2:]
    tile = q_ref.shape[0]
    width = tile * len(band_refs)
    feat = q_ref.shape[1]
    lanes = GROUP * HEAD
    block = pl.program_id(0)
    first = pos_ref[0]
    total = pos_ref[1]
    query_pos = first + row0 + block * tile + lax.broadcasted_iota(jnp.int32, (tile, 1), 0)
    key_pos = first + row0 + block * tile - HALF + lax.broadcasted_iota(jnp.int32, (1, width), 1)
    gap = key_pos - query_pos
    band_ok = (gap >= -HALF) & (gap <= HALF) & (key_pos >= 0) & (key_pos < total)
    prompt_pos = lax.broadcasted_iota(jnp.int32, (1, PROMPT), 1)
    prompt_ok = jnp.abs(prompt_pos - query_pos) > HALF
    contract = (((1,), (1,)), ((), ()))
    lane_head = lax.broadcasted_iota(jnp.int32, (1, lanes), 1) // HEAD
    for group in range(feat // lanes):
        cols = slice(group * lanes, (group + 1) * lanes)
        vcols = slice(feat + group * lanes, feat + (group + 1) * lanes)
        band_keys = jnp.concatenate([ref[:, cols] for ref in band_refs], axis=0)
        band_values = jnp.concatenate([ref[:, vcols] for ref in band_refs], axis=0)
        query = q_ref[:, cols]
        stacked = jnp.concatenate(
            [jnp.where(lane_head == j, query, jnp.zeros_like(query)) for j in range(GROUP)],
            axis=0,
        )
        band_scores = lax.dot_general(
            stacked, band_keys, contract, preferred_element_type=jnp.float32
        ).reshape(GROUP, tile, width)
        prompt_scores = lax.dot_general(
            stacked, prompt_ref[:, cols], contract, preferred_element_type=jnp.float32
        ).reshape(GROUP, tile, PROMPT)
        band_scores = jnp.where(band_ok[None], band_scores, -1e30)
        prompt_scores = jnp.where(prompt_ok[None], prompt_scores, -1e30)
        row_max = jnp.maximum(
            jnp.max(band_scores, axis=2, keepdims=True),
            jnp.max(prompt_scores, axis=2, keepdims=True),
        )
        band_exp = jnp.exp(band_scores - row_max)
        prompt_exp = jnp.exp(prompt_scores - row_max)
        denom = jnp.sum(band_exp, axis=2, keepdims=True) + jnp.sum(
            prompt_exp, axis=2, keepdims=True
        )
        band_probs = band_exp.astype(jnp.bfloat16).reshape(GROUP * tile, width)
        prompt_probs = prompt_exp.astype(jnp.bfloat16).reshape(GROUP * tile, PROMPT)
        mixed = jnp.dot(band_probs, band_values, preferred_element_type=jnp.float32) + jnp.dot(
            prompt_probs, prompt_ref[:, vcols], preferred_element_type=jnp.float32
        )
        mixed = mixed * (1.0 / denom.reshape(GROUP * tile, 1))
        attn = mixed[:tile]
        for j in range(1, GROUP):
            attn = jnp.where(lane_head == j, mixed[j * tile : (j + 1) * tile], attn)
        out_ref[:, cols] = attn.astype(out_ref.dtype)


def attention(queries, band_kv, prompt_kv, first_pos, total_len, row0, count):
    feat = queries.shape[1]
    tile = min(QUERY_TILE, count)
    pos = jnp.stack([first_pos, total_len]).astype(jnp.int32)
    pieces = 1 + 2 * HALF // tile
    width = tile * pieces
    flops = 4 * count * (width + PROMPT) * feat * GROUP
    skip = row0 // tile
    band_specs = [
        pl.BlockSpec((tile, band_kv.shape[1]), lambda b, p, k=k: (b + skip + k, 0))
        for k in range(pieces)
    ]
    return pl.pallas_call(
        functools.partial(attention_kernel, row0),
        out_shape=jax.ShapeDtypeStruct((count, feat), jnp.bfloat16),
        grid_spec=pltpu.PrefetchScalarGridSpec(
            num_scalar_prefetch=1,
            grid=(count // tile,),
            in_specs=[pl.BlockSpec((tile, feat), lambda b, p: (b + skip, 0))]
            + band_specs
            + [pl.BlockSpec(prompt_kv.shape, lambda b, p: (0, 0))],
            out_specs=pl.BlockSpec((tile, feat), lambda b, p: (b, 0)),
        ),
        cost_estimate=pl.CostEstimate(
            flops=flops,
            transcendentals=count * (width + PROMPT) * HEADS,
            bytes_accessed=2 * (2 * count * feat + pieces * count * band_kv.shape[1] + prompt_kv.size),
        ),
    )(pos, queries, *([band_kv] * pieces), prompt_kv)


def per_device(
    hidden_in,
    ln_gain,
    w_qkv,
    w_out,
    final_gain,
    w_heads,
    actions,
    propensity,
    logged_reward,
    switch_index,
):
    tok_rows = hidden_in.shape[0]
    feat_width = hidden_in.shape[1]
    seq_devices = lax.axis_size("seq")
    seq_place = lax.axis_index("seq")
    total_len = tok_rows * seq_devices
    first_pos = seq_place * tok_rows
    hidden_state = hidden_in
    prompt_source = hidden_in[:PROMPT]
    for layer_idx in range(LAYERS):
        gain = ln_gain[layer_idx]
        weights = w_qkv[layer_idx]
        prompt_rows = spread(prompt_source, "seq")
        extended = with_halo(hidden_state, (("seq", 0),), HALF)
        extended_normed = layer_norm(extended, gain)
        band_kv = jnp.dot(
            extended_normed, weights[:, feat_width:], preferred_element_type=jnp.float32
        ).astype(jnp.bfloat16)
        normed = extended_normed[HALF : HALF + tok_rows]
        queries = (
            jnp.dot(normed, weights[:, :feat_width], preferred_element_type=jnp.float32) * 0.125
        ).astype(jnp.bfloat16)
        prompt_kv = jnp.dot(
            layer_norm(prompt_rows, gain),
            weights[:, feat_width:],
            preferred_element_type=jnp.float32,
        ).astype(jnp.bfloat16)
        attended = attention(queries, band_kv, prompt_kv, first_pos, total_len, 0, tok_rows)
        projection = jnp.dot(attended, w_out[layer_idx], preferred_element_type=jnp.float32)
        hidden_state = (hidden_state.astype(jnp.float32) + projection).astype(jnp.bfloat16)
        prompt_source = hidden_state[:PROMPT]
    final = layer_norm(hidden_state, final_gain)
    head_out = jnp.dot(final, w_heads, preferred_element_type=jnp.float32)
    logits = head_out[:, :ACTIONS]
    reward_table = head_out[:, ACTIONS:]
    logit_max = jnp.max(logits, axis=-1, keepdims=True)
    exps = jnp.exp(logits - logit_max)
    policy = exps / jnp.sum(exps, axis=-1, keepdims=True)
    chosen = actions[:, None] == jnp.arange(ACTIONS, dtype=jnp.int32)[None, :]
    rewards = jnp.sum(jnp.where(chosen, reward_table, 0.0), axis=-1)
    chosen_prob = jnp.sum(jnp.where(chosen, policy, 0.0), axis=-1)
    direct = jnp.sum(policy * reward_table, axis=-1)
    logged_prob = propensity.astype(jnp.float32) / 65536.0
    cutoff = 0.5 * switch_index[0].astype(jnp.float32)
    dr_terms = direct + jnp.minimum(chosen_prob / logged_prob, cutoff) * (logged_reward - rewards)
    return (rewards, dr_terms)


def solution(mesh):
    placed = (
        P(("groups", "seq"), None),
        P(),
        P(),
        P(),
        P(),
        P(),
        P(("groups", "seq")),
        P(("groups", "seq")),
        P(("groups", "seq")),
        P("groups"),
    )
    return jax.shard_map(
        per_device,
        mesh=mesh,
        in_specs=placed,
        out_specs=(P(("groups", "seq")), P(("groups", "seq"))),
        check_vma=False,
    )
```

```python
import functools

import jax
import jax.numpy as jnp
from jax import lax
from jax.experimental import pallas as pl
from jax.experimental.pallas import tpu as pltpu
from jax.sharding import PartitionSpec as P

HEADS = 12
HEAD = 64
HALF = 256
PROMPT = 256
ACTIONS = 256
LAYERS = 2


def with_halo(array, sides, width):
    for axis, dim in sides:
        count, length = (lax.axis_size(axis), array.shape[dim])
        up = [(i, (i + 1) % count) for i in range(count - 1)]
        down = [(j, i) for i, j in up]
        last = lax.slice_in_dim(array, length - width, length, axis=dim)
        leading = lax.slice_in_dim(array, 0, width, axis=dim)
        before = lax.ppermute(last, axis, up)
        after = lax.ppermute(leading, axis, down)
        array = jnp.concatenate([before, array, after], axis=dim)
    return array


def tree_rounds(count):
    if count & (count - 1) == 0:
        bits = []
        step = count // 2
        while step:
            bits.append(step)
            step //= 2
        return [[[(i, i + bit) for i in range(0, count, 2 * bit)]] for bit in bits]
    rounds = []
    held = 1
    while held < count:
        rounds.append([[(i, i + held) for i in range(min(held, count - held))]])
        held *= 2
    return rounds


def spread(block, axis):
    place = lax.axis_index(axis)
    for ops in tree_rounds(lax.axis_size(axis)):
        received = block
        for op in ops:
            got = lax.ppermute(block, axis, op)
            targets = jnp.array([t for _, t in op], dtype=jnp.int32)
            received = jnp.where(jnp.any(place == targets), got, received)
        block = received
    return block


def layer_norm(hidden_state, gain_row):
    values_f = hidden_state.astype(jnp.float32)
    row_mean = jnp.mean(values_f, axis=-1, keepdims=True)
    centred = values_f - row_mean
    row_var = jnp.mean(centred * centred, axis=-1, keepdims=True)
    return (centred * lax.rsqrt(row_var + 1e-05) * gain_row).astype(jnp.bfloat16)


QUERY_TILE = 256
GROUP = 4


def attention_kernel(row0, pos_ref, q_ref, *refs):
    band_refs = refs[:-5]
    prompt_ref, hidden_ref, w_out_ref, out_ref, attn_ref = refs[-5:]
    tile = q_ref.shape[0]
    width = tile * len(band_refs)
    feat = q_ref.shape[1]
    lanes = GROUP * HEAD
    block = pl.program_id(0)
    first = pos_ref[0]
    total = pos_ref[1]
    query_pos = first + row0 + block * tile + lax.broadcasted_iota(jnp.int32, (tile, 1), 0)
    key_pos = first + row0 + block * tile - HALF + lax.broadcasted_iota(jnp.int32, (1, width), 1)
    gap = key_pos - query_pos
    band_ok = (gap >= -HALF) & (gap <= HALF) & (key_pos >= 0) & (key_pos < total)
    prompt_pos = lax.broadcasted_iota(jnp.int32, (1, PROMPT), 1)
    prompt_ok = jnp.abs(prompt_pos - query_pos) > HALF
    contract = (((1,), (1,)), ((), ()))
    lane_head = lax.broadcasted_iota(jnp.int32, (1, lanes), 1) // HEAD
    for group in range(feat // lanes):
        cols = slice(group * lanes, (group + 1) * lanes)
        vcols = slice(feat + group * lanes, feat + (group + 1) * lanes)
        band_keys = jnp.concatenate([ref[:, cols] for ref in band_refs], axis=0)
        band_values = jnp.concatenate([ref[:, vcols] for ref in band_refs], axis=0)
        query = q_ref[:, cols]
        stacked = jnp.concatenate(
            [jnp.where(lane_head == j, query, jnp.zeros_like(query)) for j in range(GROUP)],
            axis=0,
        )
        band_scores = lax.dot_general(
            stacked, band_keys, contract, preferred_element_type=jnp.float32
        ).reshape(GROUP, tile, width)
        prompt_scores = lax.dot_general(
            stacked, prompt_ref[:, cols], contract, preferred_element_type=jnp.float32
        ).reshape(GROUP, tile, PROMPT)
        band_scores = jnp.where(band_ok[None], band_scores, -1e30)
        prompt_scores = jnp.where(prompt_ok[None], prompt_scores, -1e30)
        row_max = jnp.maximum(
            jnp.max(band_scores, axis=2, keepdims=True),
            jnp.max(prompt_scores, axis=2, keepdims=True),
        )
        band_exp = jnp.exp(band_scores - row_max)
        prompt_exp = jnp.exp(prompt_scores - row_max)
        denom = jnp.sum(band_exp, axis=2, keepdims=True) + jnp.sum(
            prompt_exp, axis=2, keepdims=True
        )
        band_probs = band_exp.astype(jnp.bfloat16).reshape(GROUP * tile, width)
        prompt_probs = prompt_exp.astype(jnp.bfloat16).reshape(GROUP * tile, PROMPT)
        mixed = jnp.dot(band_probs, band_values, preferred_element_type=jnp.float32) + jnp.dot(
            prompt_probs, prompt_ref[:, vcols], preferred_element_type=jnp.float32
        )
        mixed = mixed * (1.0 / denom.reshape(GROUP * tile, 1))
        attn = mixed[:tile]
        for j in range(1, GROUP):
            attn = jnp.where(lane_head == j, mixed[j * tile : (j + 1) * tile], attn)
        attn_ref[:, cols] = attn.astype(attn_ref.dtype)
    projection = jnp.dot(attn_ref[...], w_out_ref[...], preferred_element_type=jnp.float32)
    out_ref[...] = (hidden_ref[...].astype(jnp.float32) + projection).astype(out_ref.dtype)


def attention(queries, band_kv, prompt_kv, first_pos, total_len, row0, count, hidden, w_out, layer):
    feat = queries.shape[1]
    tile = min(QUERY_TILE, count)
    pos = jnp.stack([first_pos, total_len]).astype(jnp.int32)
    pieces = 1 + 2 * HALF // tile
    width = tile * pieces
    flops = 4 * count * (width + PROMPT) * feat * GROUP + 2 * count * feat * feat
    skip = row0 // tile
    band_specs = [
        pl.BlockSpec((tile, band_kv.shape[1]), lambda b, p, k=k: (b + skip + k, 0))
        for k in range(pieces)
    ]
    return pl.pallas_call(
        functools.partial(attention_kernel, row0),
        out_shape=jax.ShapeDtypeStruct((count, feat), jnp.bfloat16),
        grid_spec=pltpu.PrefetchScalarGridSpec(
            num_scalar_prefetch=1,
            grid=(count // tile,),
            in_specs=[pl.BlockSpec((tile, feat), lambda b, p: (b + skip, 0))]
            + band_specs
            + [
                pl.BlockSpec(prompt_kv.shape, lambda b, p: (0, 0)),
                pl.BlockSpec((tile, feat), lambda b, p: (b + skip, 0)),
                pl.BlockSpec((None, feat, feat), lambda b, p: (layer, 0, 0)),
            ],
            out_specs=pl.BlockSpec((tile, feat), lambda b, p: (b, 0)),
            scratch_shapes=[pltpu.VMEM((tile, feat), jnp.bfloat16)],
        ),
        cost_estimate=pl.CostEstimate(
            flops=flops,
            transcendentals=count * (width + PROMPT) * HEADS,
            bytes_accessed=2 * (3 * count * feat + pieces * count * band_kv.shape[1] + prompt_kv.size + feat * feat),
        ),
    )(pos, queries, *([band_kv] * pieces), prompt_kv, hidden, w_out)


def per_device(
    hidden_in,
    ln_gain,
    w_qkv,
    w_out,
    final_gain,
    w_heads,
    actions,
    propensity,
    logged_reward,
    switch_index,
):
    tok_rows = hidden_in.shape[0]
    feat_width = hidden_in.shape[1]
    seq_devices = lax.axis_size("seq")
    seq_place = lax.axis_index("seq")
    total_len = tok_rows * seq_devices
    first_pos = seq_place * tok_rows
    hidden_state = hidden_in
    prompt_source = hidden_in[:PROMPT]
    for layer_idx in range(LAYERS):
        gain = ln_gain[layer_idx]
        weights = w_qkv[layer_idx]
        extended = with_halo(hidden_state, (("seq", 0),), HALF)
        prompt_rows = spread(prompt_source, "seq")
        extended_normed = layer_norm(extended, gain)
        band_kv = jnp.dot(
            extended_normed, weights[:, feat_width:], preferred_element_type=jnp.float32
        ).astype(jnp.bfloat16)
        normed = extended_normed[HALF : HALF + tok_rows]
        queries = (
            jnp.dot(normed, weights[:, :feat_width], preferred_element_type=jnp.float32) * 0.125
        ).astype(jnp.bfloat16)
        prompt_kv = jnp.dot(
            layer_norm(prompt_rows, gain),
            weights[:, feat_width:],
            preferred_element_type=jnp.float32,
        ).astype(jnp.bfloat16)
        hidden_state = attention(
            queries, band_kv, prompt_kv, first_pos, total_len, 0, tok_rows,
            hidden_state, w_out, layer_idx,
        )
        prompt_source = hidden_state[:PROMPT]
    final = layer_norm(hidden_state, final_gain)
    head_out = jnp.dot(final, w_heads, preferred_element_type=jnp.float32)
    logits = head_out[:, :ACTIONS]
    reward_table = head_out[:, ACTIONS:]
    logit_max = jnp.max(logits, axis=-1, keepdims=True)
    exps = jnp.exp(logits - logit_max)
    policy = exps / jnp.sum(exps, axis=-1, keepdims=True)
    chosen = actions[:, None] == jnp.arange(ACTIONS, dtype=jnp.int32)[None, :]
    rewards = jnp.sum(jnp.where(chosen, reward_table, 0.0), axis=-1)
    chosen_prob = jnp.sum(jnp.where(chosen, policy, 0.0), axis=-1)
    direct = jnp.sum(policy * reward_table, axis=-1)
    logged_prob = propensity.astype(jnp.float32) / 65536.0
    cutoff = 0.5 * switch_index[0].astype(jnp.float32)
    dr_terms = direct + jnp.minimum(chosen_prob / logged_prob, cutoff) * (logged_reward - rewards)
    return (rewards, dr_terms)


def solution(mesh):
    placed = (
        P(("groups", "seq"), None),
        P(),
        P(),
        P(),
        P(),
        P(),
        P(("groups", "seq")),
        P(("groups", "seq")),
        P(("groups", "seq")),
        P("groups"),
    )
    return jax.shard_map(
        per_device,
        mesh=mesh,
        in_specs=placed,
        out_specs=(P(("groups", "seq")), P(("groups", "seq"))),
        check_vma=False,
    )
```

```python
import functools

import jax
import jax.numpy as jnp
from jax import lax
from jax.experimental import pallas as pl
from jax.experimental.pallas import tpu as pltpu
from jax.sharding import PartitionSpec as P

HEADS = 12
HEAD = 64
HALF = 256
PROMPT = 256
ACTIONS = 256
LAYERS = 2


def with_halo(array, sides, width):
    for axis, dim in sides:
        count, length = (lax.axis_size(axis), array.shape[dim])
        up = [(i, (i + 1) % count) for i in range(count - 1)]
        down = [(j, i) for i, j in up]
        last = lax.slice_in_dim(array, length - width, length, axis=dim)
        leading = lax.slice_in_dim(array, 0, width, axis=dim)
        before = lax.ppermute(last, axis, up)
        after = lax.ppermute(leading, axis, down)
        array = jnp.concatenate([before, array, after], axis=dim)
    return array


def tree_rounds(count):
    if count & (count - 1) == 0:
        bits = []
        step = count // 2
        while step:
            bits.append(step)
            step //= 2
        return [[[(i, i + bit) for i in range(0, count, 2 * bit)]] for bit in bits]
    rounds = []
    held = 1
    while held < count:
        rounds.append([[(i, i + held) for i in range(min(held, count - held))]])
        held *= 2
    return rounds


def spread(block, axis):
    place = lax.axis_index(axis)
    for ops in tree_rounds(lax.axis_size(axis)):
        received = block
        for op in ops:
            got = lax.ppermute(block, axis, op)
            targets = jnp.array([t for _, t in op], dtype=jnp.int32)
            received = jnp.where(jnp.any(place == targets), got, received)
        block = received
    return block


def layer_norm(hidden_state, gain_row):
    values_f = hidden_state.astype(jnp.float32)
    row_mean = jnp.mean(values_f, axis=-1, keepdims=True)
    centred = values_f - row_mean
    row_var = jnp.mean(centred * centred, axis=-1, keepdims=True)
    return (centred * lax.rsqrt(row_var + 1e-05) * gain_row).astype(jnp.bfloat16)


QUERY_TILE = 256
GROUP = 4


def attention_kernel(row0, pos_ref, q_ref, *refs):
    band_refs = refs[:-6]
    prompt_ref, hidden_ref, w_out_ref, out_ref, head_ref, attn_ref = refs[-6:]
    tile = q_ref.shape[0]
    width = tile * len(band_refs)
    feat = q_ref.shape[1]
    lanes = GROUP * HEAD
    block = pl.program_id(0)
    first = pos_ref[0]
    total = pos_ref[1]
    query_pos = first + row0 + block * tile + lax.broadcasted_iota(jnp.int32, (tile, 1), 0)
    key_pos = first + row0 + block * tile - HALF + lax.broadcasted_iota(jnp.int32, (1, width), 1)
    gap = key_pos - query_pos
    band_ok = (gap >= -HALF) & (gap <= HALF) & (key_pos >= 0) & (key_pos < total)
    prompt_pos = lax.broadcasted_iota(jnp.int32, (1, PROMPT), 1)
    prompt_ok = jnp.abs(prompt_pos - query_pos) > HALF
    contract = (((1,), (1,)), ((), ()))
    lane_head = lax.broadcasted_iota(jnp.int32, (1, lanes), 1) // HEAD
    for group in range(feat // lanes):
        cols = slice(group * lanes, (group + 1) * lanes)
        vcols = slice(feat + group * lanes, feat + (group + 1) * lanes)
        band_keys = jnp.concatenate([ref[:, cols] for ref in band_refs], axis=0)
        band_values = jnp.concatenate([ref[:, vcols] for ref in band_refs], axis=0)
        query = q_ref[:, cols]
        stacked = jnp.concatenate(
            [jnp.where(lane_head == j, query, jnp.zeros_like(query)) for j in range(GROUP)],
            axis=0,
        )
        band_scores = lax.dot_general(
            stacked, band_keys, contract, preferred_element_type=jnp.float32
        ).reshape(GROUP, tile, width)
        prompt_scores = lax.dot_general(
            stacked, prompt_ref[:, cols], contract, preferred_element_type=jnp.float32
        ).reshape(GROUP, tile, PROMPT)
        band_scores = jnp.where(band_ok[None], band_scores, -1e30)
        prompt_scores = jnp.where(prompt_ok[None], prompt_scores, -1e30)
        row_max = jnp.maximum(
            jnp.max(band_scores, axis=2, keepdims=True),
            jnp.max(prompt_scores, axis=2, keepdims=True),
        )
        band_exp = jnp.exp(band_scores - row_max)
        prompt_exp = jnp.exp(prompt_scores - row_max)
        denom = jnp.sum(band_exp, axis=2, keepdims=True) + jnp.sum(
            prompt_exp, axis=2, keepdims=True
        )
        band_probs = band_exp.astype(jnp.bfloat16).reshape(GROUP * tile, width)
        prompt_probs = prompt_exp.astype(jnp.bfloat16).reshape(GROUP * tile, PROMPT)
        mixed = jnp.dot(band_probs, band_values, preferred_element_type=jnp.float32) + jnp.dot(
            prompt_probs, prompt_ref[:, vcols], preferred_element_type=jnp.float32
        )
        mixed = mixed * (1.0 / denom.reshape(GROUP * tile, 1))
        attn = mixed[:tile]
        for j in range(1, GROUP):
            attn = jnp.where(lane_head == j, mixed[j * tile : (j + 1) * tile], attn)
        attn_ref[:, cols] = attn.astype(attn_ref.dtype)
    projection = jnp.dot(attn_ref[...], w_out_ref[...], preferred_element_type=jnp.float32)
    new_rows = (hidden_ref[...].astype(jnp.float32) + projection).astype(out_ref.dtype)
    out_ref[...] = new_rows

    @pl.when(block == 0)
    def _():
        head_ref[...] = new_rows[: head_ref.shape[0]]


def attention(
    queries, band_kv, prompt_kv, first_pos, total_len, row0, count, hidden, w_out, layer, head_rows
):
    feat = queries.shape[1]
    tile = min(QUERY_TILE, count)
    pos = jnp.stack([first_pos, total_len]).astype(jnp.int32)
    pieces = 1 + 2 * HALF // tile
    width = tile * pieces
    flops = 4 * count * (width + PROMPT) * feat * GROUP + 2 * count * feat * feat
    skip = row0 // tile
    band_specs = [
        pl.BlockSpec((tile, band_kv.shape[1]), lambda b, p, k=k: (b + skip + k, 0))
        for k in range(pieces)
    ]
    return pl.pallas_call(
        functools.partial(attention_kernel, row0),
        out_shape=(
            jax.ShapeDtypeStruct((count, feat), jnp.bfloat16),
            jax.ShapeDtypeStruct((head_rows, feat), jnp.bfloat16),
        ),
        grid_spec=pltpu.PrefetchScalarGridSpec(
            num_scalar_prefetch=1,
            grid=(count // tile,),
            in_specs=[pl.BlockSpec((tile, feat), lambda b, p: (b + skip, 0))]
            + band_specs
            + [
                pl.BlockSpec(prompt_kv.shape, lambda b, p: (0, 0)),
                pl.BlockSpec((tile, feat), lambda b, p: (b + skip, 0)),
                pl.BlockSpec((None, feat, feat), lambda b, p: (layer, 0, 0)),
            ],
            out_specs=(
                pl.BlockSpec((tile, feat), lambda b, p: (b, 0)),
                pl.BlockSpec((head_rows, feat), lambda b, p: (0, 0)),
            ),
            scratch_shapes=[pltpu.VMEM((tile, feat), jnp.bfloat16)],
        ),
        cost_estimate=pl.CostEstimate(
            flops=flops,
            transcendentals=count * (width + PROMPT) * HEADS,
            bytes_accessed=2 * (3 * count * feat + pieces * count * band_kv.shape[1] + prompt_kv.size + feat * feat),
        ),
    )(pos, queries, *([band_kv] * pieces), prompt_kv, hidden, w_out)


def per_device(
    hidden_in,
    ln_gain,
    w_qkv,
    w_out,
    final_gain,
    w_heads,
    actions,
    propensity,
    logged_reward,
    switch_index,
):
    tok_rows = hidden_in.shape[0]
    feat_width = hidden_in.shape[1]
    seq_devices = lax.axis_size("seq")
    seq_place = lax.axis_index("seq")
    total_len = tok_rows * seq_devices
    first_pos = seq_place * tok_rows
    hidden_state = hidden_in
    prompt_source = hidden_in[:PROMPT]
    for layer_idx in range(LAYERS):
        gain = ln_gain[layer_idx]
        weights = w_qkv[layer_idx]
        extended = with_halo(hidden_state, (("seq", 0),), HALF)
        prompt_rows = spread(prompt_source, "seq")
        extended_normed = layer_norm(extended, gain)
        band_kv = jnp.dot(
            extended_normed, weights[:, feat_width:], preferred_element_type=jnp.float32
        ).astype(jnp.bfloat16)
        normed = extended_normed[HALF : HALF + tok_rows]
        queries = (
            jnp.dot(normed, weights[:, :feat_width], preferred_element_type=jnp.float32) * 0.125
        ).astype(jnp.bfloat16)
        prompt_kv = jnp.dot(
            layer_norm(prompt_rows, gain),
            weights[:, feat_width:],
            preferred_element_type=jnp.float32,
        ).astype(jnp.bfloat16)
        tile_rows = min(QUERY_TILE, tok_rows)
        head_rows = PROMPT if PROMPT <= tile_rows else tile_rows
        hidden_state, head_part = attention(
            queries, band_kv, prompt_kv, first_pos, total_len, 0, tok_rows,
            hidden_state, w_out, layer_idx, head_rows,
        )
        prompt_source = head_part if head_rows == PROMPT else hidden_state[:PROMPT]
    final = layer_norm(hidden_state, final_gain)
    head_out = jnp.dot(final, w_heads, preferred_element_type=jnp.float32)
    logits = head_out[:, :ACTIONS]
    reward_table = head_out[:, ACTIONS:]
    logit_max = jnp.max(logits, axis=-1, keepdims=True)
    exps = jnp.exp(logits - logit_max)
    policy = exps / jnp.sum(exps, axis=-1, keepdims=True)
    chosen = actions[:, None] == jnp.arange(ACTIONS, dtype=jnp.int32)[None, :]
    rewards = jnp.sum(jnp.where(chosen, reward_table, 0.0), axis=-1)
    chosen_prob = jnp.sum(jnp.where(chosen, policy, 0.0), axis=-1)
    direct = jnp.sum(policy * reward_table, axis=-1)
    logged_prob = propensity.astype(jnp.float32) / 65536.0
    cutoff = 0.5 * switch_index[0].astype(jnp.float32)
    dr_terms = direct + jnp.minimum(chosen_prob / logged_prob, cutoff) * (logged_reward - rewards)
    return (rewards, dr_terms)


def solution(mesh):
    placed = (
        P(("groups", "seq"), None),
        P(),
        P(),
        P(),
        P(),
        P(),
        P(("groups", "seq")),
        P(("groups", "seq")),
        P(("groups", "seq")),
        P("groups"),
    )
    return jax.shard_map(
        per_device,
        mesh=mesh,
        in_specs=placed,
        out_specs=(P(("groups", "seq")), P(("groups", "seq"))),
        check_vma=False,
    )
```

```python
import functools

import jax
import jax.numpy as jnp
from jax import lax
from jax.experimental import pallas as pl
from jax.experimental.pallas import tpu as pltpu
from jax.sharding import PartitionSpec as P

HEADS = 12
HEAD = 64
HALF = 256
PROMPT = 256
ACTIONS = 256
LAYERS = 2


def with_halo(array, sides, width):
    for axis, dim in sides:
        count, length = (lax.axis_size(axis), array.shape[dim])
        up = [(i, (i + 1) % count) for i in range(count - 1)]
        down = [(j, i) for i, j in up]
        last = lax.slice_in_dim(array, length - width, length, axis=dim)
        leading = lax.slice_in_dim(array, 0, width, axis=dim)
        before = lax.ppermute(last, axis, up)
        after = lax.ppermute(leading, axis, down)
        array = jnp.concatenate([before, array, after], axis=dim)
    return array


def tree_rounds(count):
    if count & (count - 1) == 0:
        bits = []
        step = count // 2
        while step:
            bits.append(step)
            step //= 2
        if len(bits) >= 3:
            bits = [bits[-2]] + bits[:-2] + [bits[-1]]
        rounds = []
        held = [0]
        for bit in bits:
            rounds.append([[(i, i + bit) for i in held]])
            held = sorted(held + [i + bit for i in held])
        return rounds
    rounds = []
    held = 1
    while held < count:
        rounds.append([[(i, i + held) for i in range(min(held, count - held))]])
        held *= 2
    return rounds


def spread(block, axis):
    place = lax.axis_index(axis)
    for ops in tree_rounds(lax.axis_size(axis)):
        received = block
        for op in ops:
            got = lax.ppermute(block, axis, op)
            targets = jnp.array([t for _, t in op], dtype=jnp.int32)
            received = jnp.where(jnp.any(place == targets), got, received)
        block = received
    return block


def layer_norm(hidden_state, gain_row):
    values_f = hidden_state.astype(jnp.float32)
    row_mean = jnp.mean(values_f, axis=-1, keepdims=True)
    centred = values_f - row_mean
    row_var = jnp.mean(centred * centred, axis=-1, keepdims=True)
    return (centred * lax.rsqrt(row_var + 1e-05) * gain_row).astype(jnp.bfloat16)


QUERY_TILE = 256
GROUP = 4


def attention_kernel(row0, pos_ref, q_ref, *refs):
    band_refs = refs[:-2]
    prompt_ref, out_ref = refs[-2:]
    tile = q_ref.shape[0]
    width = tile * len(band_refs)
    feat = q_ref.shape[1]
    lanes = GROUP * HEAD
    block = pl.program_id(0)
    first = pos_ref[0]
    total = pos_ref[1]
    query_pos = first + row0 + block * tile + lax.broadcasted_iota(jnp.int32, (tile, 1), 0)
    key_pos = first + row0 + block * tile - HALF + lax.broadcasted_iota(jnp.int32, (1, width), 1)
    gap = key_pos - query_pos
    band_ok = (gap >= -HALF) & (gap <= HALF) & (key_pos >= 0) & (key_pos < total)
    prompt_pos = lax.broadcasted_iota(jnp.int32, (1, PROMPT), 1)
    prompt_ok = jnp.abs(prompt_pos - query_pos) > HALF
    contract = (((1,), (1,)), ((), ()))
    lane_head = lax.broadcasted_iota(jnp.int32, (1, lanes), 1) // HEAD
    for group in range(feat // lanes):
        cols = slice(group * lanes, (group + 1) * lanes)
        vcols = slice(feat + group * lanes, feat + (group + 1) * lanes)
        band_keys = jnp.concatenate([ref[:, cols] for ref in band_refs], axis=0)
        band_values = jnp.concatenate([ref[:, vcols] for ref in band_refs], axis=0)
        query = q_ref[:, cols]
        stacked = jnp.concatenate(
            [jnp.where(lane_head == j, query, jnp.zeros_like(query)) for j in range(GROUP)],
            axis=0,
        )
        band_scores = lax.dot_general(
            stacked, band_keys, contract, preferred_element_type=jnp.float32
        ).reshape(GROUP, tile, width)
        prompt_scores = lax.dot_general(
            stacked, prompt_ref[:, cols], contract, preferred_element_type=jnp.float32
        ).reshape(GROUP, tile, PROMPT)
        band_scores = jnp.where(band_ok[None], band_scores, -1e30)
        prompt_scores = jnp.where(prompt_ok[None], prompt_scores, -1e30)
        row_max = jnp.maximum(
            jnp.max(band_scores, axis=2, keepdims=True),
            jnp.max(prompt_scores, axis=2, keepdims=True),
        )
        band_exp = jnp.exp(band_scores - row_max)
        prompt_exp = jnp.exp(prompt_scores - row_max)
        denom = jnp.sum(band_exp, axis=2, keepdims=True) + jnp.sum(
            prompt_exp, axis=2, keepdims=True
        )
        band_probs = band_exp.astype(jnp.bfloat16).reshape(GROUP * tile, width)
        prompt_probs = prompt_exp.astype(jnp.bfloat16).reshape(GROUP * tile, PROMPT)
        mixed = jnp.dot(band_probs, band_values, preferred_element_type=jnp.float32) + jnp.dot(
            prompt_probs, prompt_ref[:, vcols], preferred_element_type=jnp.float32
        )
        mixed = mixed * (1.0 / denom.reshape(GROUP * tile, 1))
        attn = mixed[:tile]
        for j in range(1, GROUP):
            attn = jnp.where(lane_head == j, mixed[j * tile : (j + 1) * tile], attn)
        out_ref[:, cols] = attn.astype(out_ref.dtype)


def attention(queries, band_kv, prompt_kv, first_pos, total_len, row0, count):
    feat = queries.shape[1]
    tile = min(QUERY_TILE, count)
    pos = jnp.stack([first_pos, total_len]).astype(jnp.int32)
    pieces = 1 + 2 * HALF // tile
    width = tile * pieces
    flops = 4 * count * (width + PROMPT) * feat * GROUP
    skip = row0 // tile
    band_specs = [
        pl.BlockSpec((tile, band_kv.shape[1]), lambda b, p, k=k: (b + skip + k, 0))
        for k in range(pieces)
    ]
    return pl.pallas_call(
        functools.partial(attention_kernel, row0),
        out_shape=jax.ShapeDtypeStruct((count, feat), jnp.bfloat16),
        grid_spec=pltpu.PrefetchScalarGridSpec(
            num_scalar_prefetch=1,
            grid=(count // tile,),
            in_specs=[pl.BlockSpec((tile, feat), lambda b, p: (b + skip, 0))]
            + band_specs
            + [pl.BlockSpec(prompt_kv.shape, lambda b, p: (0, 0))],
            out_specs=pl.BlockSpec((tile, feat), lambda b, p: (b, 0)),
        ),
        cost_estimate=pl.CostEstimate(
            flops=flops,
            transcendentals=count * (width + PROMPT) * HEADS,
            bytes_accessed=2 * (2 * count * feat + pieces * count * band_kv.shape[1] + prompt_kv.size),
        ),
    )(pos, queries, *([band_kv] * pieces), prompt_kv)


def per_device(
    hidden_in,
    ln_gain,
    w_qkv,
    w_out,
    final_gain,
    w_heads,
    actions,
    propensity,
    logged_reward,
    switch_index,
):
    tok_rows = hidden_in.shape[0]
    feat_width = hidden_in.shape[1]
    seq_devices = lax.axis_size("seq")
    seq_place = lax.axis_index("seq")
    total_len = tok_rows * seq_devices
    first_pos = seq_place * tok_rows
    hidden_state = hidden_in
    prompt_source = hidden_in[:PROMPT]
    for layer_idx in range(LAYERS):
        gain = ln_gain[layer_idx]
        weights = w_qkv[layer_idx]
        extended = with_halo(hidden_state, (("seq", 0),), HALF)
        prompt_rows = spread(prompt_source, "seq")
        extended_normed = layer_norm(extended, gain)
        band_kv = jnp.dot(
            extended_normed, weights[:, feat_width:], preferred_element_type=jnp.float32
        ).astype(jnp.bfloat16)
        normed = extended_normed[HALF : HALF + tok_rows]
        queries = (
            jnp.dot(normed, weights[:, :feat_width], preferred_element_type=jnp.float32) * 0.125
        ).astype(jnp.bfloat16)
        prompt_kv = jnp.dot(
            layer_norm(prompt_rows, gain),
            weights[:, feat_width:],
            preferred_element_type=jnp.float32,
        ).astype(jnp.bfloat16)
        attended = attention(queries, band_kv, prompt_kv, first_pos, total_len, 0, tok_rows)
        projection = jnp.dot(attended, w_out[layer_idx], preferred_element_type=jnp.float32)
        hidden_state = (hidden_state.astype(jnp.float32) + projection).astype(jnp.bfloat16)
        prompt_source = hidden_state[:PROMPT]
    final = layer_norm(hidden_state, final_gain)
    head_out = jnp.dot(final, w_heads, preferred_element_type=jnp.float32)
    logits = head_out[:, :ACTIONS]
    reward_table = head_out[:, ACTIONS:]
    logit_max = jnp.max(logits, axis=-1, keepdims=True)
    exps = jnp.exp(logits - logit_max)
    policy = exps / jnp.sum(exps, axis=-1, keepdims=True)
    chosen = actions[:, None] == jnp.arange(ACTIONS, dtype=jnp.int32)[None, :]
    rewards = jnp.sum(jnp.where(chosen, reward_table, 0.0), axis=-1)
    chosen_prob = jnp.sum(jnp.where(chosen, policy, 0.0), axis=-1)
    direct = jnp.sum(policy * reward_table, axis=-1)
    logged_prob = propensity.astype(jnp.float32) / 65536.0
    cutoff = 0.5 * switch_index[0].astype(jnp.float32)
    dr_terms = direct + jnp.minimum(chosen_prob / logged_prob, cutoff) * (logged_reward - rewards)
    return (rewards, dr_terms)


def solution(mesh):
    placed = (
        P(("groups", "seq"), None),
        P(),
        P(),
        P(),
        P(),
        P(),
        P(("groups", "seq")),
        P(("groups", "seq")),
        P(("groups", "seq")),
        P("groups"),
    )
    return jax.shard_map(
        per_device,
        mesh=mesh,
        in_specs=placed,
        out_specs=(P(("groups", "seq")), P(("groups", "seq"))),
        check_vma=False,
    )
```

```python
import functools

import jax
import jax.numpy as jnp
from jax import lax
from jax.experimental import pallas as pl
from jax.experimental.pallas import tpu as pltpu
from jax.sharding import PartitionSpec as P

HEADS = 12
HEAD = 64
HALF = 256
PROMPT = 256
ACTIONS = 256
LAYERS = 2


def with_halo(array, sides, width):
    for axis, dim in sides:
        count, length = (lax.axis_size(axis), array.shape[dim])
        up = [(i, (i + 1) % count) for i in range(count - 1)]
        down = [(j, i) for i, j in up]
        last = lax.slice_in_dim(array, length - width, length, axis=dim)
        leading = lax.slice_in_dim(array, 0, width, axis=dim)
        before = lax.ppermute(last, axis, up)
        after = lax.ppermute(leading, axis, down)
        array = jnp.concatenate([before, array, after], axis=dim)
    return array


def tree_rounds(count):
    if count & (count - 1) == 0:
        bits = []
        step = count // 2
        while step:
            bits.append(step)
            step //= 2
        return [([[(i, i + bit) for i in range(0, count, 2 * bit)]], bit) for bit in bits]
    rounds = []
    held = 1
    while held < count:
        rounds.append(([[(i, i + held) for i in range(min(held, count - held))]], None))
        held *= 2
    return rounds


def spread(block, axis):
    place = lax.axis_index(axis)
    for ops, bit in tree_rounds(lax.axis_size(axis)):
        received = block
        for op in ops:
            got = lax.ppermute(block, axis, op)
            if bit is not None:
                is_target = place % (2 * bit) == bit
            else:
                targets = jnp.array([t for _, t in op], dtype=jnp.int32)
                is_target = jnp.any(place == targets)
            received = jnp.where(is_target, got, received)
        block = received
    return block


def layer_norm(hidden_state, gain_row):
    values_f = hidden_state.astype(jnp.float32)
    row_mean = jnp.mean(values_f, axis=-1, keepdims=True)
    centred = values_f - row_mean
    row_var = jnp.mean(centred * centred, axis=-1, keepdims=True)
    return (centred * lax.rsqrt(row_var + 1e-05) * gain_row).astype(jnp.bfloat16)


QUERY_TILE = 256
GROUP = 4


def attention_kernel(row0, pos_ref, q_ref, *refs):
    band_refs = refs[:-2]
    prompt_ref, out_ref = refs[-2:]
    tile = q_ref.shape[0]
    width = tile * len(band_refs)
    feat = q_ref.shape[1]
    lanes = GROUP * HEAD
    block = pl.program_id(0)
    first = pos_ref[0]
    total = pos_ref[1]
    query_pos = first + row0 + block * tile + lax.broadcasted_iota(jnp.int32, (tile, 1), 0)
    key_pos = first + row0 + block * tile - HALF + lax.broadcasted_iota(jnp.int32, (1, width), 1)
    gap = key_pos - query_pos
    band_ok = (gap >= -HALF) & (gap <= HALF) & (key_pos >= 0) & (key_pos < total)
    prompt_pos = lax.broadcasted_iota(jnp.int32, (1, PROMPT), 1)
    prompt_ok = jnp.abs(prompt_pos - query_pos) > HALF
    contract = (((1,), (1,)), ((), ()))
    lane_head = lax.broadcasted_iota(jnp.int32, (1, lanes), 1) // HEAD
    for group in range(feat // lanes):
        cols = slice(group * lanes, (group + 1) * lanes)
        vcols = slice(feat + group * lanes, feat + (group + 1) * lanes)
        band_keys = jnp.concatenate([ref[:, cols] for ref in band_refs], axis=0)
        band_values = jnp.concatenate([ref[:, vcols] for ref in band_refs], axis=0)
        query = q_ref[:, cols]
        stacked = jnp.concatenate(
            [jnp.where(lane_head == j, query, jnp.zeros_like(query)) for j in range(GROUP)],
            axis=0,
        )
        band_scores = lax.dot_general(
            stacked, band_keys, contract, preferred_element_type=jnp.float32
        ).reshape(GROUP, tile, width)
        prompt_scores = lax.dot_general(
            stacked, prompt_ref[:, cols], contract, preferred_element_type=jnp.float32
        ).reshape(GROUP, tile, PROMPT)
        band_scores = jnp.where(band_ok[None], band_scores, -1e30)
        prompt_scores = jnp.where(prompt_ok[None], prompt_scores, -1e30)
        row_max = jnp.maximum(
            jnp.max(band_scores, axis=2, keepdims=True),
            jnp.max(prompt_scores, axis=2, keepdims=True),
        )
        band_exp = jnp.exp(band_scores - row_max)
        prompt_exp = jnp.exp(prompt_scores - row_max)
        denom = jnp.sum(band_exp, axis=2, keepdims=True) + jnp.sum(
            prompt_exp, axis=2, keepdims=True
        )
        band_probs = band_exp.astype(jnp.bfloat16).reshape(GROUP * tile, width)
        prompt_probs = prompt_exp.astype(jnp.bfloat16).reshape(GROUP * tile, PROMPT)
        mixed = jnp.dot(band_probs, band_values, preferred_element_type=jnp.float32) + jnp.dot(
            prompt_probs, prompt_ref[:, vcols], preferred_element_type=jnp.float32
        )
        mixed = mixed * (1.0 / denom.reshape(GROUP * tile, 1))
        attn = mixed[:tile]
        for j in range(1, GROUP):
            attn = jnp.where(lane_head == j, mixed[j * tile : (j + 1) * tile], attn)
        out_ref[:, cols] = attn.astype(out_ref.dtype)


def attention(queries, band_kv, prompt_kv, first_pos, total_len, row0, count):
    feat = queries.shape[1]
    tile = min(QUERY_TILE, count)
    pos = jnp.stack([first_pos, total_len]).astype(jnp.int32)
    pieces = 1 + 2 * HALF // tile
    width = tile * pieces
    flops = 4 * count * (width + PROMPT) * feat * GROUP
    skip = row0 // tile
    band_specs = [
        pl.BlockSpec((tile, band_kv.shape[1]), lambda b, p, k=k: (b + skip + k, 0))
        for k in range(pieces)
    ]
    return pl.pallas_call(
        functools.partial(attention_kernel, row0),
        out_shape=jax.ShapeDtypeStruct((count, feat), jnp.bfloat16),
        grid_spec=pltpu.PrefetchScalarGridSpec(
            num_scalar_prefetch=1,
            grid=(count // tile,),
            in_specs=[pl.BlockSpec((tile, feat), lambda b, p: (b + skip, 0))]
            + band_specs
            + [pl.BlockSpec(prompt_kv.shape, lambda b, p: (0, 0))],
            out_specs=pl.BlockSpec((tile, feat), lambda b, p: (b, 0)),
        ),
        cost_estimate=pl.CostEstimate(
            flops=flops,
            transcendentals=count * (width + PROMPT) * HEADS,
            bytes_accessed=2 * (2 * count * feat + pieces * count * band_kv.shape[1] + prompt_kv.size),
        ),
    )(pos, queries, *([band_kv] * pieces), prompt_kv)


def per_device(
    hidden_in,
    ln_gain,
    w_qkv,
    w_out,
    final_gain,
    w_heads,
    actions,
    propensity,
    logged_reward,
    switch_index,
):
    tok_rows = hidden_in.shape[0]
    feat_width = hidden_in.shape[1]
    seq_devices = lax.axis_size("seq")
    seq_place = lax.axis_index("seq")
    total_len = tok_rows * seq_devices
    first_pos = seq_place * tok_rows
    hidden_state = hidden_in
    prompt_source = hidden_in[:PROMPT]
    for layer_idx in range(LAYERS):
        gain = ln_gain[layer_idx]
        weights = w_qkv[layer_idx]
        extended = with_halo(hidden_state, (("seq", 0),), HALF)
        prompt_rows = spread(prompt_source, "seq")
        extended_normed = layer_norm(extended, gain)
        band_kv = jnp.dot(
            extended_normed, weights[:, feat_width:], preferred_element_type=jnp.float32
        ).astype(jnp.bfloat16)
        normed = extended_normed[HALF : HALF + tok_rows]
        queries = (
            jnp.dot(normed, weights[:, :feat_width], preferred_element_type=jnp.float32) * 0.125
        ).astype(jnp.bfloat16)
        prompt_kv = jnp.dot(
            layer_norm(prompt_rows, gain),
            weights[:, feat_width:],
            preferred_element_type=jnp.float32,
        ).astype(jnp.bfloat16)
        attended = attention(queries, band_kv, prompt_kv, first_pos, total_len, 0, tok_rows)
        projection = jnp.dot(attended, w_out[layer_idx], preferred_element_type=jnp.float32)
        hidden_state = (hidden_state.astype(jnp.float32) + projection).astype(jnp.bfloat16)
        prompt_source = hidden_state[:PROMPT]
    final = layer_norm(hidden_state, final_gain)
    head_out = jnp.dot(final, w_heads, preferred_element_type=jnp.float32)
    logits = head_out[:, :ACTIONS]
    reward_table = head_out[:, ACTIONS:]
    logit_max = jnp.max(logits, axis=-1, keepdims=True)
    exps = jnp.exp(logits - logit_max)
    policy = exps / jnp.sum(exps, axis=-1, keepdims=True)
    chosen = actions[:, None] == jnp.arange(ACTIONS, dtype=jnp.int32)[None, :]
    rewards = jnp.sum(jnp.where(chosen, reward_table, 0.0), axis=-1)
    chosen_prob = jnp.sum(jnp.where(chosen, policy, 0.0), axis=-1)
    direct = jnp.sum(policy * reward_table, axis=-1)
    logged_prob = propensity.astype(jnp.float32) / 65536.0
    cutoff = 0.5 * switch_index[0].astype(jnp.float32)
    dr_terms = direct + jnp.minimum(chosen_prob / logged_prob, cutoff) * (logged_reward - rewards)
    return (rewards, dr_terms)


def solution(mesh):
    placed = (
        P(("groups", "seq"), None),
        P(),
        P(),
        P(),
        P(),
        P(),
        P(("groups", "seq")),
        P(("groups", "seq")),
        P(("groups", "seq")),
        P("groups"),
    )
    return jax.shard_map(
        per_device,
        mesh=mesh,
        in_specs=placed,
        out_specs=(P(("groups", "seq")), P(("groups", "seq"))),
        check_vma=False,
    )
```
